32 devices in a mesh: ctx: 8 (over z, x), tp: 4 (over y, core).
Axes of the slice: x: 2, y: 2, z: 4, core: 2. Of those that a mesh axis runs over, the one named last changes fastest.
Arguments:
- projections: bfloat16 [3, 8192, 4096], P(None, 'tp', 'ctx'), may hold values from -6 to 6
- short_filter: bfloat16 [3, 8192, 3], P(None, 'tp'), may hold values from -3.5 to 3.5
- decay_rate: float32 [512, 16], P('tp'), may hold values from 6.1035156e-05 to 0.05
- residue: float32 [512, 16], P('tp'), may hold values from -1.5 to 1.5
- skip: float32 [8192], P('tp'), may hold values from 0.5 to 1.5
- norm_gain: float32 [8192], P('tp'), may hold values from 0.5 to 1.5
- residual: bfloat16 [8192, 4096], P('tp', 'ctx'), may hold values from -64 to 64
Outputs:
- normed: bfloat16 [8192, 4096], P('tp', 'ctx')
The draws below stay inside these ranges and needn't reach their ends.
All inputs are finite; a program needn't handle non-finite values.
Results may differ from the reference program's by a relative error of at most 0.006.
Values may be sent and summed in bfloat16 or wider, within the bound.
No kernel may reach another device: no remote copies, remote signals or barrier semaphores. Data moves between devices by JAX's collectives and lax.ppermute only.
A program may use at most 128 MiB of HBM per device.

```python
import math
import jax
import jax.numpy as jnp
from jax import lax

D = 8192
GROUP = 16
MODES = 16
SHORT = 3
GROUPS = 512
TOKENS = 4096


def draw_residual(key, part):
    subkeys = jax.random.split(key, 3)
    channel_pos = jnp.arange(D, dtype=jnp.float32) / D
    channel_scale = 10.0 ** (0.5 * channel_pos + 0.5 * jax.random.uniform(subkeys[0], (D,)) - 0.5)
    token_scale = 10.0 ** jax.random.uniform(subkeys[1], (TOKENS,), minval=-0.5, maxval=0.5)
    noise_part = jnp.clip(jax.random.normal(subkeys[2], (D, TOKENS)), -5.0, 5.0)
    return (noise_part * channel_scale[:, None] * token_scale[None, :]).astype(jnp.bfloat16)


def shard_levels(rng, dims, shards, least, high):
    factor_of = 1.0
    for axis_at, shards_of in shards:
        draws = jax.random.uniform(jax.random.fold_in(jax.random.fold_in(rng, 6), axis_at), (shards_of,), jnp.float32, least / len(shards), high / len(shards))
        factor_of = factor_of * jnp.repeat(jnp.exp(draws), dims[axis_at] // shards_of).reshape((-1,) + (1,) * (len(dims) - 1 - axis_at))
    return factor_of


def bell_draw(key, dims, deviation, reach, shards=(), kind=jnp.bfloat16):
    gain = shard_levels(key, dims, shards, -0.22, 0.18) if shards else 1.0
    entries = jax.random.normal(key, dims, jnp.float32) * deviation * gain
    return jnp.minimum(jnp.maximum(entries, -reach), reach).astype(kind)


def setup_inputs(seed: int = 0) -> dict:
    keys = jax.random.split(jax.random.key(seed), 8)
    return {
        "projections": bell_draw(keys[0], (3, D, TOKENS), 1.0, 6.0, ((1, 4), (2, 8))),
        "short_filter": bell_draw(keys[1], (3, D, SHORT), SHORT ** -0.5, 3.5, ((1, 4),)),
        "decay_rate": jnp.clip(jnp.exp(math.log(0.05) - 6.7083283 * jax.random.uniform(keys[2], (GROUPS, MODES), jnp.float32) ** shard_levels(keys[2], (GROUPS, MODES), ((0, 4),), -0.2, 0.2)), 6.103515625e-05, 0.05),
        "residue": bell_draw(keys[3], (GROUPS, MODES), MODES ** -0.5, 1.5, ((0, 4),), jnp.float32),
        "skip": jnp.clip(0.5 + 1.0 * jax.random.uniform(keys[4], (D,), jnp.float32) ** shard_levels(keys[4], (D,), ((0, 4),), -0.2, 0.2), 0.5, 1.5),
        "norm_gain": jnp.clip(1.0 + 0.1 * jax.random.normal(keys[5], (D,), jnp.float32), 0.5, 1.5),
        "residual": draw_residual(jax.random.fold_in(keys[7], 71), 0),
    }


epsilon = 1e-06

def short_conv(padded, taps):
    tap_count = taps.shape[-1]
    length = padded.shape[-1] - (tap_count - 1)
    summed = None
    for offset in range(tap_count):
        begin = tap_count - 1 - offset
        term = taps[..., offset:offset + 1].astype(jnp.float32) * padded[..., begin:begin + length].astype(jnp.float32)
        summed = term if summed is None else summed + term
    return summed

def causal_fft(signal, filt):
    length = signal.shape[-1]
    padded_len = 2 * length
    spectrum = jnp.fft.rfft(signal, padded_len) * jnp.fft.rfft(filt, padded_len)
    return jnp.fft.irfft(spectrum, padded_len)[..., :length]

def reference(projections, short_filter, decay_rate, residue, skip, norm_gain, residual):
    length = TOKENS
    slab_len = math.gcd(D, 256)
    slab_count = D // slab_len
    slab_groups = slab_len // GROUP

    def mix_slab(slab_number):
        first_chan = (slab_number * slab_len).astype(jnp.int32)
        first_group = (slab_number * slab_groups).astype(jnp.int32)
        proj_slab = lax.dynamic_slice_in_dim(projections, first_chan, slab_len, 1)
        taps = lax.dynamic_slice_in_dim(short_filter, first_chan, slab_len, 1)
        decays = lax.dynamic_slice_in_dim(decay_rate, first_group, slab_groups, 0)
        weights = lax.dynamic_slice_in_dim(residue, first_group, slab_groups, 0)
        direct = lax.dynamic_slice_in_dim(skip, first_chan, slab_len, 0)
        stream = lax.dynamic_slice_in_dim(residual, first_chan, slab_len, 0)
        padded = jnp.pad(proj_slab, ((0, 0), (0, 0), (SHORT - 1, 0)))
        featurized = short_conv(padded, taps).astype(jnp.bfloat16)
        product = (featurized[1].astype(jnp.float32) * featurized[2].astype(jnp.float32)).astype(jnp.bfloat16)
        lag_axis = jnp.arange(length, dtype=jnp.float32)
        scaled = weights * jnp.sqrt(-jnp.expm1(-2.0 * decays))
        long_taps = lax.optimization_barrier(jnp.sum(scaled[:, :, None] * jnp.exp(-decays[:, :, None] * lag_axis[None, None, :]), axis=1))
        long_full = jnp.repeat(long_taps, GROUP, axis=0)
        signal = product.astype(jnp.float32)
        long_term = causal_fft(signal, long_full)
        mixed = featurized[0].astype(jnp.float32) * (long_term + direct[:, None] * signal)
        return stream.astype(jnp.float32) + mixed
    updated = lax.map(mix_slab, jnp.arange(slab_count, dtype=jnp.int32)).reshape(D, length)
    mean_sq = lax.optimization_barrier(jnp.mean(updated * updated, axis=0))
    return (updated * lax.rsqrt(mean_sq + epsilon)[None, :] * norm_gain[:, None]).astype(jnp.bfloat16)
```

```python
import functools

import jax
import jax.numpy as jnp
from jax import lax
from jax.experimental import pallas as pl
from jax.experimental.pallas import tpu as pltpu
from jax.sharding import PartitionSpec as P

D = 8192
epsilon = 1e-06
BLOCK = 128
LANES = 128
f32 = jnp.float32
bf16 = jnp.bfloat16


def shifted(shard, axis, by):
    size = lax.axis_size(axis)
    pairs = [(i, i + by) for i in range(size) if 0 <= i + by < size]
    return lax.ppermute(shard, axis, pairs)


def split2(a):
    hi = a.astype(bf16)
    lo = (a - hi.astype(f32)).astype(bf16)
    return hi, lo


def dot(a, b):
    return jnp.dot(a, b, preferred_element_type=f32)


def featurize(proj_ref, rim_ref, taps_ref, p, rows):
    x = proj_ref[p, rows, :].astype(f32)
    lane = lax.broadcasted_iota(jnp.int32, x.shape, 1)
    rim = rim_ref[p, rows, :].astype(f32)
    back1 = rim[:, 1:2]
    back2 = rim[:, 0:1]
    x1 = jnp.where(lane == 0, back1, pltpu.roll(x, 1, 1))
    x2 = jnp.where(lane == 0, back2, jnp.where(lane == 1, back1, pltpu.roll(x, 2, 1)))
    taps = taps_ref[p, rows, :].astype(f32)
    summed = taps[:, 0:1] * x + taps[:, 1:2] * x1
    summed = summed + taps[:, 2:3] * x2
    return summed.astype(bf16)


def block_rows(x, width, count):
    return jnp.concatenate([x[:, b * BLOCK : (b + 1) * BLOCK] for b in range(count)], axis=0)


def group_product(proj_ref, rim_ref, taps_ref, rows):
    key = featurize(proj_ref, rim_ref, taps_ref, 1, rows).astype(f32)
    value = featurize(proj_ref, rim_ref, taps_ref, 2, rows).astype(f32)
    return (key * value).astype(bf16)


def block_states(xb, w_hi_ref, w_lo_ref, decay_ref, g, start, width, count):
    ends = dot(xb, w_hi_ref[g]) + dot(xb, w_lo_ref[g])
    decay = decay_ref[g]
    state = start
    entering = []
    for b in range(count):
        entering.append(state)
        state = decay * state + ends[b * width : (b + 1) * width]
    return entering, state


def state_kernel(width, count, proj_ref, rim_ref, taps_ref, w_hi_ref, w_lo_ref, decay_ref, out_ref):
    groups = w_hi_ref.shape[0]

    def body(g, carry):
        rows = pl.ds(pl.multiple_of(g * width, width), width)
        xb = block_rows(group_product(proj_ref, rim_ref, taps_ref, rows), width, count)
        zero = jnp.zeros((width, LANES), f32)
        _, final = block_states(xb, w_hi_ref, w_lo_ref, decay_ref, g, zero, width, count)
        out_ref[rows, :] = final
        return carry

    lax.fori_loop(0, groups, body, 0)


def mix_kernel(
    width,
    count,
    proj_ref,
    rim_ref,
    taps_ref,
    w_hi_ref,
    w_lo_ref,
    decay_ref,
    lead_hi_ref,
    lead_lo_ref,
    taps_long_ref,
    incoming_ref,
    skip_ref,
    res_ref,
    upd_ref,
    sq_ref,
):
    groups = w_hi_ref.shape[0]
    length = res_ref.shape[1]
    s_idx = lax.broadcasted_iota(jnp.int32, (BLOCK, BLOCK), 0)
    t_idx = lax.broadcasted_iota(jnp.int32, (BLOCK, BLOCK), 1)

    def body(g, acc):
        rows = pl.ds(pl.multiple_of(g * width, width), width)
        query = featurize(proj_ref, rim_ref, taps_ref, 0, rows).astype(f32)
        product = group_product(proj_ref, rim_ref, taps_ref, rows)
        xb = block_rows(product, width, count)
        entering, _ = block_states(
            xb, w_hi_ref, w_lo_ref, decay_ref, g, incoming_ref[rows, :], width, count
        )
        zb = jnp.concatenate(entering, axis=0)
        z_hi, z_lo = split2(zb)
        lead_hi = lead_hi_ref[g]
        lead_lo = lead_lo_ref[g]
        far = dot(z_hi, lead_hi) + dot(z_hi, lead_lo) + dot(z_lo, lead_hi)
        row = taps_long_ref[pl.ds(g, 1), :]
        toeplitz = pltpu.roll(jnp.broadcast_to(row, (BLOCK, BLOCK)), 0, 1, stride=1, stride_axis=0)
        toeplitz = jnp.where(t_idx >= s_idx, toeplitz, 0.0)
        t_hi, t_lo = split2(toeplitz)
        near = dot(xb, t_hi) + dot(xb, t_lo)
        long_b = near + far
        long_term = jnp.concatenate(
            [long_b[b * width : (b + 1) * width] for b in range(count)], axis=1
        )
        signal = product.astype(f32)
        mixed = query * (long_term + skip_ref[rows, :] * signal)
        updated = res_ref[rows, :].astype(f32) + mixed
        upd_ref[rows, :] = updated
        sq = updated * updated
        return acc + sq.reshape(width // 8, 8, length).sum(axis=0)

    acc = lax.fori_loop(0, groups, body, jnp.zeros((8, length), f32))
    sq_ref[0] = acc.sum(axis=0, keepdims=True)


def local(projections, short_filter, decay_rate, residue, skip, norm_gain, residual):
    channels, length = residual.shape
    groups, modes = decay_rate.shape
    width = channels // groups
    rim_len = short_filter.shape[2] - 1
    count = length // BLOCK
    chunk = 256 if channels % 256 == 0 else channels
    chunk_groups = chunk // width
    steps = channels // chunk

    rim = shifted(projections[:, :, length - rim_len :], "ctx", 1)

    scaled = residue * jnp.sqrt(-jnp.expm1(-2.0 * decay_rate))
    lag = jnp.arange(BLOCK, dtype=f32)
    pad = ((0, 0), (0, 0), (0, LANES - modes))
    taps_long = jnp.sum(
        scaled[:, :, None] * jnp.exp(-decay_rate[:, :, None] * lag[None, None, :]), axis=1
    )
    tail = jnp.exp(-decay_rate[:, None, :] * (BLOCK - 1 - lag)[None, :, None])
    tail = jnp.pad(tail, pad)
    w_hi, w_lo = split2(tail)
    lead = scaled[:, :, None] * jnp.exp(-decay_rate[:, :, None] * (lag + 1.0)[None, None, :])
    lead = jnp.pad(lead, ((0, 0), (0, LANES - modes), (0, 0)))
    lead_hi, lead_lo = split2(lead)
    decay = jnp.pad(jnp.exp(-decay_rate * BLOCK)[:, None, :], pad)

    proj_spec = pl.BlockSpec((3, chunk, length), lambda i: (0, i, 0))
    rim_spec = pl.BlockSpec((3, chunk, rim_len), lambda i: (0, i, 0))
    taps_spec = pl.BlockSpec((3, chunk, short_filter.shape[2]), lambda i: (0, i, 0))
    w_spec = pl.BlockSpec((chunk_groups, BLOCK, LANES), lambda i: (i, 0, 0))
    decay_spec = pl.BlockSpec((chunk_groups, 1, LANES), lambda i: (i, 0, 0))
    state_spec = pl.BlockSpec((chunk, LANES), lambda i: (i, 0))

    end_state = pl.pallas_call(
        functools.partial(state_kernel, width, count),
        grid=(steps,),
        in_specs=[proj_spec, rim_spec, taps_spec, w_spec, w_spec, decay_spec],
        out_specs=state_spec,
        out_shape=jax.ShapeDtypeStruct((channels, LANES), f32),
    )(projections, rim, short_filter, w_hi, w_lo, decay)

    place = lax.axis_index("ctx")
    size = lax.axis_size("ctx")
    gathered = lax.all_gather(end_state[:, :modes], "ctx")
    earlier = jnp.arange(size, dtype=jnp.int32)
    gap = jnp.maximum(place - 1 - earlier, 0).astype(f32) * length
    rate = jnp.repeat(decay_rate, width, axis=0)
    weight = jnp.where(
        (earlier < place)[:, None, None],
        jnp.exp(-rate[None, :, :] * gap[:, None, None]),
        0.0,
    )
    incoming = jnp.sum(weight * gathered, axis=0)
    incoming = jnp.pad(incoming, ((0, 0), (0, LANES - modes)))

    updated, sq = pl.pallas_call(
        functools.partial(mix_kernel, width, count),
        grid=(steps,),
        in_specs=[
            proj_spec,
            rim_spec,
            taps_spec,
            w_spec,
            w_spec,
            decay_spec,
            w_spec,
            w_spec,
            pl.BlockSpec((chunk_groups, BLOCK), lambda i: (i, 0)),
            state_spec,
            pl.BlockSpec((chunk, 1), lambda i: (i, 0)),
            pl.BlockSpec((chunk, length), lambda i: (i, 0)),
        ],
        out_specs=[
            pl.BlockSpec((chunk, length), lambda i: (i, 0)),
            pl.BlockSpec((1, 1, length), lambda i: (i, 0, 0)),
        ],
        out_shape=[
            jax.ShapeDtypeStruct((channels, length), f32),
            jax.ShapeDtypeStruct((steps, 1, length), f32),
        ],
    )(
        projections,
        rim,
        short_filter,
        w_hi,
        w_lo,
        decay,
        lead_hi,
        lead_lo,
        taps_long,
        incoming,
        skip[:, None],
        residual,
    )
    squares = lax.psum(jnp.sum(sq, axis=(0, 1)), "tp")
    return (updated * lax.rsqrt(squares / D + epsilon)[None, :] * norm_gain[:, None]).astype(bf16)


def solution(mesh):
    placed = (
        P(None, "tp", "ctx"),
        P(None, "tp", None),
        P("tp", None),
        P("tp", None),
        P("tp"),
        P("tp"),
        P("tp", "ctx"),
    )
    return jax.shard_map(
        local, mesh=mesh, in_specs=placed, out_specs=P("tp", "ctx"), check_vma=False
    )
```

```python
import functools

import jax
import jax.numpy as jnp
from jax import lax
from jax.experimental import pallas as pl
from jax.experimental.pallas import tpu as pltpu
from jax.sharding import PartitionSpec as P

D = 8192
epsilon = 1e-06
BLOCK = 128
f32 = jnp.float32
bf16 = jnp.bfloat16


def shifted(shard, axis, by):
    size = lax.axis_size(axis)
    pairs = [(i, i + by) for i in range(size) if 0 <= i + by < size]
    return lax.ppermute(shard, axis, pairs)


def split2(a):
    hi = a.astype(bf16)
    lo = (a - hi.astype(f32)).astype(bf16)
    return hi, lo


def dot(a, b):
    return jnp.dot(a, b, preferred_element_type=f32)


def featurize(proj_ref, rim_ref, taps_ref, p):
    x = proj_ref[p].astype(f32)
    lane = lax.broadcasted_iota(jnp.int32, x.shape, 1)
    rim = rim_ref[p].astype(f32)
    back1 = rim[:, 1:2]
    back2 = rim[:, 0:1]
    x1 = jnp.where(lane == 0, back1, pltpu.roll(x, 1, 1))
    x2 = jnp.where(lane == 0, back2, jnp.where(lane == 1, back1, pltpu.roll(x, 2, 1)))
    taps = taps_ref[p].astype(f32)
    summed = taps[:, 0:1] * x + taps[:, 1:2] * x1
    summed = summed + taps[:, 2:3] * x2
    return summed.astype(bf16)


def product_blocks(proj_ref, rim_ref, taps_ref, count):
    key = featurize(proj_ref, rim_ref, taps_ref, 1).astype(f32)
    value = featurize(proj_ref, rim_ref, taps_ref, 2).astype(f32)
    product = (key * value).astype(bf16)
    stacked = jnp.concatenate(
        [product[:, b * BLOCK : (b + 1) * BLOCK] for b in range(count)], axis=0
    )
    return product, stacked


def own_modes(rows, lanes, width):
    row = lax.broadcasted_iota(jnp.int32, (rows, lanes), 0) // width
    lane = lax.broadcasted_iota(jnp.int32, (rows, lanes), 1) // width
    return row == lane


def block_ends(stacked, w_hi_ref, w_lo_ref, rows, width, count):
    ends = dot(stacked, w_hi_ref[0]) + dot(stacked, w_lo_ref[0])
    lanes = ends.shape[1]
    own = own_modes(rows, lanes, width)
    return [jnp.where(own, ends[b * rows : (b + 1) * rows], 0.0) for b in range(count)]


def state_kernel(width, count, proj_ref, rim_ref, taps_ref, w_hi_ref, w_lo_ref, decay_ref, out_ref):
    rows = proj_ref.shape[1]
    _, stacked = product_blocks(proj_ref, rim_ref, taps_ref, count)
    ends = block_ends(stacked, w_hi_ref, w_lo_ref, rows, width, count)
    decay = decay_ref[0]
    state = ends[0]
    for b in range(1, count):
        state = decay * state + ends[b]
    out_ref[...] = state


def mix_kernel(
    width,
    count,
    proj_ref,
    rim_ref,
    taps_ref,
    w_hi_ref,
    w_lo_ref,
    decay_ref,
    lead_hi_ref,
    lead_lo_ref,
    taps_long_ref,
    incoming_ref,
    skip_ref,
    res_ref,
    upd_ref,
    sq_ref,
):
    rows = proj_ref.shape[1]
    groups = rows // width
    query = featurize(proj_ref, rim_ref, taps_ref, 0).astype(f32)
    product, stacked = product_blocks(proj_ref, rim_ref, taps_ref, count)
    ends = block_ends(stacked, w_hi_ref, w_lo_ref, rows, width, count)
    decay = decay_ref[0]
    state = incoming_ref[...]
    entering = []
    for b in range(count):
        entering.append(state)
        state = decay * state + ends[b]
    z_hi, z_lo = split2(jnp.concatenate(entering, axis=0))
    lead_hi = lead_hi_ref[0]
    lead_lo = lead_lo_ref[0]
    far = dot(z_hi, lead_hi) + dot(z_hi, lead_lo) + dot(z_lo, lead_hi)

    s_idx = lax.broadcasted_iota(jnp.int32, (BLOCK, BLOCK), 0)
    t_idx = lax.broadcasted_iota(jnp.int32, (BLOCK, BLOCK), 1)
    pieces = [[None] * groups for _ in range(count)]
    for g in range(groups):
        lhs = jnp.concatenate(
            [stacked[b * rows + g * width : b * rows + (g + 1) * width] for b in range(count)],
            axis=0,
        )
        row = taps_long_ref[g : g + 1, :]
        toeplitz = pltpu.roll(jnp.broadcast_to(row, (BLOCK, BLOCK)), 0, 1, stride=1, stride_axis=0)
        toeplitz = jnp.where(t_idx >= s_idx, toeplitz, 0.0)
        t_hi, t_lo = split2(toeplitz)
        near = dot(lhs, t_hi) + dot(lhs, t_lo)
        for b in range(count):
            pieces[b][g] = near[b * width : (b + 1) * width]
    long_term = jnp.concatenate(
        [
            jnp.concatenate(pieces[b], axis=0) + far[b * rows : (b + 1) * rows]
            for b in range(count)
        ],
        axis=1,
    )
    signal = product.astype(f32)
    mixed = query * (long_term + skip_ref[...] * signal)
    updated = res_ref[...].astype(f32) + mixed
    upd_ref[...] = updated
    sq_ref[0] = jnp.sum(updated * updated, axis=0, keepdims=True)


def local(projections, short_filter, decay_rate, residue, skip, norm_gain, residual):
    channels, length = residual.shape
    groups, modes = decay_rate.shape
    width = channels // groups
    rim_len = short_filter.shape[2] - 1
    count = length // BLOCK
    chunk = 256 if channels % 256 == 0 else channels
    chunk_groups = chunk // width
    lanes = chunk_groups * modes
    steps = channels // chunk

    rim = shifted(projections[:, :, length - rim_len :], "ctx", 1)

    scaled = residue * jnp.sqrt(-jnp.expm1(-2.0 * decay_rate))
    lag = jnp.arange(BLOCK, dtype=f32)
    taps_long = jnp.sum(
        scaled[:, :, None] * jnp.exp(-decay_rate[:, :, None] * lag[None, None, :]), axis=1
    )
    tail = jnp.exp(-decay_rate[:, None, :] * (BLOCK - 1 - lag)[None, :, None])
    tail = tail.reshape(steps, chunk_groups, BLOCK, modes).transpose(0, 2, 1, 3)
    w_hi, w_lo = split2(tail.reshape(steps, BLOCK, lanes))
    lead = scaled[:, :, None] * jnp.exp(-decay_rate[:, :, None] * (lag + 1.0)[None, None, :])
    lead_hi, lead_lo = split2(lead.reshape(steps, lanes, BLOCK))
    decay = jnp.exp(-decay_rate * BLOCK).reshape(steps, 1, lanes)

    proj_spec = pl.BlockSpec((3, chunk, length), lambda i: (0, i, 0))
    rim_spec = pl.BlockSpec((3, chunk, rim_len), lambda i: (0, i, 0))
    taps_spec = pl.BlockSpec((3, chunk, short_filter.shape[2]), lambda i: (0, i, 0))
    w_spec = pl.BlockSpec((1, BLOCK, lanes), lambda i: (i, 0, 0))
    lead_spec = pl.BlockSpec((1, lanes, BLOCK), lambda i: (i, 0, 0))
    decay_spec = pl.BlockSpec((1, 1, lanes), lambda i: (i, 0, 0))
    state_spec = pl.BlockSpec((chunk, lanes), lambda i: (i, 0))

    end_state = pl.pallas_call(
        functools.partial(state_kernel, width, count),
        grid=(steps,),
        in_specs=[proj_spec, rim_spec, taps_spec, w_spec, w_spec, decay_spec],
        out_specs=state_spec,
        out_shape=jax.ShapeDtypeStruct((channels, lanes), f32),
    )(projections, rim, short_filter, w_hi, w_lo, decay)
    end_state = end_state.reshape(channels, chunk_groups, modes).sum(axis=1)

    place = lax.axis_index("ctx")
    size = lax.axis_size("ctx")
    dense = end_state.reshape(channels * modes // 128, 128)
    gathered = lax.all_gather(dense, "ctx").reshape(size, channels, modes)
    earlier = jnp.arange(size, dtype=jnp.int32)
    gap = jnp.maximum(place - 1 - earlier, 0).astype(f32) * length
    rate = jnp.repeat(decay_rate, width, axis=0)
    weight = jnp.where(
        (earlier < place)[:, None, None],
        jnp.exp(-rate[None, :, :] * gap[:, None, None]),
        0.0,
    )
    incoming = jnp.sum(weight * gathered, axis=0)
    own = (jnp.arange(lanes)[None, :] // modes) == ((jnp.arange(channels) // width) % chunk_groups)[:, None]
    incoming = jnp.where(own, jnp.tile(incoming, (1, chunk_groups)), 0.0)

    updated, sq = pl.pallas_call(
        functools.partial(mix_kernel, width, count),
        grid=(steps,),
        in_specs=[
            proj_spec,
            rim_spec,
            taps_spec,
            w_spec,
            w_spec,
            decay_spec,
            lead_spec,
            lead_spec,
            pl.BlockSpec((chunk_groups, BLOCK), lambda i: (i, 0)),
            state_spec,
            pl.BlockSpec((chunk, 1), lambda i: (i, 0)),
            pl.BlockSpec((chunk, length), lambda i: (i, 0)),
        ],
        out_specs=[
            pl.BlockSpec((chunk, length), lambda i: (i, 0)),
            pl.BlockSpec((1, 1, length), lambda i: (i, 0, 0)),
        ],
        out_shape=[
            jax.ShapeDtypeStruct((channels, length), f32),
            jax.ShapeDtypeStruct((steps, 1, length), f32),
        ],
    )(
        projections,
        rim,
        short_filter,
        w_hi,
        w_lo,
        decay,
        lead_hi,
        lead_lo,
        taps_long,
        incoming,
        skip[:, None],
        residual,
    )
    squares = lax.psum(jnp.sum(sq, axis=(0, 1)), "tp")
    return (updated * lax.rsqrt(squares / D + epsilon)[None, :] * norm_gain[:, None]).astype(bf16)


def solution(mesh):
    placed = (
        P(None, "tp", "ctx"),
        P(None, "tp", None),
        P("tp", None),
        P("tp", None),
        P("tp"),
        P("tp"),
        P("tp", "ctx"),
    )
    return jax.shard_map(
        local, mesh=mesh, in_specs=placed, out_specs=P("tp", "ctx"), check_vma=False
    )
```

```python
import functools

import jax
import jax.numpy as jnp
from jax import lax
from jax.experimental import pallas as pl
from jax.experimental.pallas import tpu as pltpu
from jax.sharding import PartitionSpec as P

D = 8192
epsilon = 1e-06
BLOCK = 128
f32 = jnp.float32
bf16 = jnp.bfloat16


def shifted(shard, axis, by):
    size = lax.axis_size(axis)
    pairs = [(i, i + by) for i in range(size) if 0 <= i + by < size]
    return lax.ppermute(shard, axis, pairs)


def incoming_state(ends, span_rate, size):
    if size <= 8:
        total = jnp.zeros_like(ends)
        for d in range(1, size):
            total = total + jnp.exp(-span_rate * (d - 1)) * shifted(ends, "ctx", d)
        return total
    carry = shifted(ends, "ctx", 1)
    step = 1
    while step < size:
        carry = carry + jnp.exp(-span_rate * step) * shifted(carry, "ctx", step)
        step *= 2
    return carry


def split2(a):
    hi = a.astype(bf16)
    lo = (a - hi.astype(f32)).astype(bf16)
    return hi, lo


def dot(a, b):
    return jnp.dot(a, b, preferred_element_type=f32)


def featurize(proj_ref, rim_ref, taps_ref, p):
    x = proj_ref[p].astype(f32)
    lane = lax.broadcasted_iota(jnp.int32, x.shape, 1)
    rim = rim_ref[p].astype(f32)
    back1 = rim[:, 1:2]
    back2 = rim[:, 0:1]
    x1 = jnp.where(lane == 0, back1, pltpu.roll(x, 1, 1))
    x2 = jnp.where(lane == 0, back2, jnp.where(lane == 1, back1, pltpu.roll(x, 2, 1)))
    taps = taps_ref[p].astype(f32)
    summed = taps[:, 0:1] * x + taps[:, 1:2] * x1
    summed = summed + taps[:, 2:3] * x2
    return summed.astype(bf16)


def product_blocks(proj_ref, rim_ref, taps_ref, count):
    key = featurize(proj_ref, rim_ref, taps_ref, 1).astype(f32)
    value = featurize(proj_ref, rim_ref, taps_ref, 2).astype(f32)
    product = (key * value).astype(bf16)
    stacked = jnp.concatenate(
        [product[:, b * BLOCK : (b + 1) * BLOCK] for b in range(count)], axis=0
    )
    return product, stacked


def own_modes(rows, lanes, width):
    row = lax.broadcasted_iota(jnp.int32, (rows, lanes), 0) // width
    lane = lax.broadcasted_iota(jnp.int32, (rows, lanes), 1) // width
    return row == lane


def block_ends(stacked, w_hi_ref, w_lo_ref, rows, width, count):
    ends = dot(stacked, w_hi_ref[0]) + dot(stacked, w_lo_ref[0])
    lanes = ends.shape[1]
    own = own_modes(rows, lanes, width)
    return [jnp.where(own, ends[b * rows : (b + 1) * rows], 0.0) for b in range(count)]


def state_kernel(width, count, proj_ref, rim_ref, taps_ref, w_hi_ref, w_lo_ref, decay_ref, out_ref):
    rows = proj_ref.shape[1]
    _, stacked = product_blocks(proj_ref, rim_ref, taps_ref, count)
    ends = block_ends(stacked, w_hi_ref, w_lo_ref, rows, width, count)
    decay = decay_ref[0]
    state = ends[0]
    for b in range(1, count):
        state = decay * state + ends[b]
    out_ref[...] = state


def mix_kernel(
    width,
    count,
    proj_ref,
    rim_ref,
    taps_ref,
    w_hi_ref,
    w_lo_ref,
    decay_ref,
    lead_hi_ref,
    lead_lo_ref,
    taps_long_ref,
    incoming_ref,
    skip_ref,
    res_ref,
    upd_ref,
    sq_ref,
):
    rows = proj_ref.shape[1]
    groups = rows // width
    query = featurize(proj_ref, rim_ref, taps_ref, 0).astype(f32)
    product, stacked = product_blocks(proj_ref, rim_ref, taps_ref, count)
    ends = block_ends(stacked, w_hi_ref, w_lo_ref, rows, width, count)
    decay = decay_ref[0]
    state = incoming_ref[...]
    entering = []
    for b in range(count):
        entering.append(state)
        state = decay * state + ends[b]
    z_hi, z_lo = split2(jnp.concatenate(entering, axis=0))
    lead_hi = lead_hi_ref[0]
    lead_lo = lead_lo_ref[0]
    far = dot(z_hi, lead_hi) + dot(z_hi, lead_lo) + dot(z_lo, lead_hi)

    s_idx = lax.broadcasted_iota(jnp.int32, (BLOCK, BLOCK), 0)
    t_idx = lax.broadcasted_iota(jnp.int32, (BLOCK, BLOCK), 1)
    pieces = [[None] * groups for _ in range(count)]
    for g in range(groups):
        lhs = jnp.concatenate(
            [stacked[b * rows + g * width : b * rows + (g + 1) * width] for b in range(count)],
            axis=0,
        )
        row = taps_long_ref[g : g + 1, :]
        toeplitz = pltpu.roll(jnp.broadcast_to(row, (BLOCK, BLOCK)), 0, 1, stride=1, stride_axis=0)
        toeplitz = jnp.where(t_idx >= s_idx, toeplitz, 0.0)
        t_hi, t_lo = split2(toeplitz)
        near = dot(lhs, t_hi) + dot(lhs, t_lo)
        for b in range(count):
            pieces[b][g] = near[b * width : (b + 1) * width]
    long_term = jnp.concatenate(
        [
            jnp.concatenate(pieces[b], axis=0) + far[b * rows : (b + 1) * rows]
            for b in range(count)
        ],
        axis=1,
    )
    signal = product.astype(f32)
    mixed = query * (long_term + skip_ref[...] * signal)
    updated = res_ref[...].astype(f32) + mixed
    upd_ref[...] = updated
    sq_ref[0] = jnp.sum(updated * updated, axis=0, keepdims=True)


def local(projections, short_filter, decay_rate, residue, skip, norm_gain, residual):
    channels, length = residual.shape
    groups, modes = decay_rate.shape
    width = channels // groups
    rim_len = short_filter.shape[2] - 1
    count = length // BLOCK
    chunk = 256 if channels % 256 == 0 else channels
    chunk_groups = chunk // width
    lanes = chunk_groups * modes
    steps = channels // chunk

    rim = shifted(projections[:, :, length - rim_len :], "ctx", 1)

    scaled = residue * jnp.sqrt(-jnp.expm1(-2.0 * decay_rate))
    lag = jnp.arange(BLOCK, dtype=f32)
    taps_long = jnp.sum(
        scaled[:, :, None] * jnp.exp(-decay_rate[:, :, None] * lag[None, None, :]), axis=1
    )
    tail = jnp.exp(-decay_rate[:, None, :] * (BLOCK - 1 - lag)[None, :, None])
    tail = tail.reshape(steps, chunk_groups, BLOCK, modes).transpose(0, 2, 1, 3)
    w_hi, w_lo = split2(tail.reshape(steps, BLOCK, lanes))
    lead = scaled[:, :, None] * jnp.exp(-decay_rate[:, :, None] * (lag + 1.0)[None, None, :])
    lead_hi, lead_lo = split2(lead.reshape(steps, lanes, BLOCK))
    decay = jnp.exp(-decay_rate * BLOCK).reshape(steps, 1, lanes)

    proj_spec = pl.BlockSpec((3, chunk, length), lambda i: (0, i, 0))
    rim_spec = pl.BlockSpec((3, chunk, rim_len), lambda i: (0, i, 0))
    taps_spec = pl.BlockSpec((3, chunk, short_filter.shape[2]), lambda i: (0, i, 0))
    w_spec = pl.BlockSpec((1, BLOCK, lanes), lambda i: (i, 0, 0))
    lead_spec = pl.BlockSpec((1, lanes, BLOCK), lambda i: (i, 0, 0))
    decay_spec = pl.BlockSpec((1, 1, lanes), lambda i: (i, 0, 0))
    state_spec = pl.BlockSpec((chunk, lanes), lambda i: (i, 0))

    end_state = pl.pallas_call(
        functools.partial(state_kernel, width, count),
        grid=(steps,),
        in_specs=[proj_spec, rim_spec, taps_spec, w_spec, w_spec, decay_spec],
        out_specs=state_spec,
        out_shape=jax.ShapeDtypeStruct((channels, lanes), f32),
    )(projections, rim, short_filter, w_hi, w_lo, decay)
    end_state = end_state.reshape(channels, chunk_groups, modes).sum(axis=1)

    size = lax.axis_size("ctx")
    dense = end_state.reshape(channels * modes // 128, 128)
    rate = jnp.repeat(decay_rate, width, axis=0).reshape(dense.shape)
    incoming = incoming_state(dense, rate * length, size).reshape(channels, modes)
    own = (jnp.arange(lanes)[None, :] // modes) == ((jnp.arange(channels) // width) % chunk_groups)[:, None]
    incoming = jnp.where(own, jnp.tile(incoming, (1, chunk_groups)), 0.0)

    updated, sq = pl.pallas_call(
        functools.partial(mix_kernel, width, count),
        grid=(steps,),
        in_specs=[
            proj_spec,
            rim_spec,
            taps_spec,
            w_spec,
            w_spec,
            decay_spec,
            lead_spec,
            lead_spec,
            pl.BlockSpec((chunk_groups, BLOCK), lambda i: (i, 0)),
            state_spec,
            pl.BlockSpec((chunk, 1), lambda i: (i, 0)),
            pl.BlockSpec((chunk, length), lambda i: (i, 0)),
        ],
        out_specs=[
            pl.BlockSpec((chunk, length), lambda i: (i, 0)),
            pl.BlockSpec((1, 1, length), lambda i: (i, 0, 0)),
        ],
        out_shape=[
            jax.ShapeDtypeStruct((channels, length), f32),
            jax.ShapeDtypeStruct((steps, 1, length), f32),
        ],
    )(
        projections,
        rim,
        short_filter,
        w_hi,
        w_lo,
        decay,
        lead_hi,
        lead_lo,
        taps_long,
        incoming,
        skip[:, None],
        residual,
    )
    squares = lax.psum(jnp.sum(sq, axis=(0, 1)), "tp")
    return (updated * lax.rsqrt(squares / D + epsilon)[None, :] * norm_gain[:, None]).astype(bf16)


def solution(mesh):
    placed = (
        P(None, "tp", "ctx"),
        P(None, "tp", None),
        P("tp", None),
        P("tp", None),
        P("tp"),
        P("tp"),
        P("tp", "ctx"),
    )
    return jax.shard_map(
        local, mesh=mesh, in_specs=placed, out_specs=P("tp", "ctx"), check_vma=False
    )
```

```python
import functools

import jax
import jax.numpy as jnp
from jax import lax
from jax.experimental import pallas as pl
from jax.experimental.pallas import tpu as pltpu
from jax.sharding import PartitionSpec as P

D = 8192
epsilon = 1e-06
BLOCK = 128
LANES = 128
f32 = jnp.float32
bf16 = jnp.bfloat16


def shifted(shard, axis, by):
    size = lax.axis_size(axis)
    pairs = [(i, i + by) for i in range(size) if 0 <= i + by < size]
    return lax.ppermute(shard, axis, pairs)


def incoming_state(ends, span_rate, size):
    if size <= 8:
        total = jnp.zeros_like(ends)
        for d in range(1, size):
            total = total + jnp.exp(-span_rate * (d - 1)) * shifted(ends, "ctx", d)
        return total
    carry = shifted(ends, "ctx", 1)
    step = 1
    while step < size:
        carry = carry + jnp.exp(-span_rate * step) * shifted(carry, "ctx", step)
        step *= 2
    return carry


def split2(a):
    hi = a.astype(bf16)
    lo = (a - hi.astype(f32)).astype(bf16)
    return hi, lo


def split3(a):
    hi = a.astype(bf16)
    rest = a - hi.astype(f32)
    mid = rest.astype(bf16)
    lo = (rest - mid.astype(f32)).astype(bf16)
    return hi, mid, lo


def dot(a, b):
    return jnp.dot(a, b, preferred_element_type=f32)


def exact_dot(a, select):
    return sum(dot(part, select) for part in split3(a))


def featurize(proj_ref, prm, p, taps, rims):
    x = proj_ref[p].astype(f32)
    lane = lax.broadcasted_iota(jnp.int32, x.shape, 1)
    back2 = prm[:, rims + 2 * p : rims + 2 * p + 1]
    back1 = prm[:, rims + 2 * p + 1 : rims + 2 * p + 2]
    x1 = jnp.where(lane == 0, back1, pltpu.roll(x, 1, 1))
    x2 = jnp.where(lane == 0, back2, jnp.where(lane == 1, back1, pltpu.roll(x, 2, 1)))
    t = taps * p
    summed = prm[:, t : t + 1] * x + prm[:, t + 1 : t + 2] * x1
    summed = summed + prm[:, t + 2 : t + 3] * x2
    return summed.astype(bf16)


def own_modes(rows, lanes, width, modes):
    row = lax.broadcasted_iota(jnp.int32, (rows, lanes), 0) // width
    lane = lax.broadcasted_iota(jnp.int32, (rows, lanes), 1) // modes
    return row == lane


def local_kernel(
    width,
    modes,
    count,
    proj_ref,
    prm_ref,
    w_hi_ref,
    w_lo_ref,
    decay_ref,
    lead_hi_ref,
    lead_lo_ref,
    taps_long_ref,
    select_ref,
    res_ref,
    u0_ref,
    q_ref,
    end_ref,
):
    rows = proj_ref.shape[1]
    groups = rows // width
    taps = 3
    rims = 3 * taps
    skip_at = rims + 6
    prm = prm_ref[...]
    query = featurize(proj_ref, prm, 0, taps, rims)
    q_ref[...] = query
    key = featurize(proj_ref, prm, 1, taps, rims).astype(f32)
    value = featurize(proj_ref, prm, 2, taps, rims).astype(f32)
    product = (key * value).astype(bf16)
    stacked = jnp.concatenate(
        [product[:, b * BLOCK : (b + 1) * BLOCK] for b in range(count)], axis=0
    )
    ends = dot(stacked, w_hi_ref[0]) + dot(stacked, w_lo_ref[0])
    lanes = ends.shape[1]
    own = own_modes(rows, lanes, width, modes)
    decay = decay_ref[0]
    state = jnp.where(own, ends[0:rows], 0.0)
    entering = [jnp.zeros_like(state)]
    for b in range(1, count):
        entering.append(state)
        state = decay * state + jnp.where(own, ends[b * rows : (b + 1) * rows], 0.0)
    end_ref[...] = exact_dot(state, select_ref[...])
    z_hi, z_lo = split2(jnp.concatenate(entering, axis=0))
    lead_hi = lead_hi_ref[0]
    lead_lo = lead_lo_ref[0]
    far = dot(z_hi, lead_hi) + dot(z_hi, lead_lo) + dot(z_lo, lead_hi)

    s_idx = lax.broadcasted_iota(jnp.int32, (BLOCK, BLOCK), 0)
    t_idx = lax.broadcasted_iota(jnp.int32, (BLOCK, BLOCK), 1)
    pieces = [[None] * groups for _ in range(count)]
    for g in range(groups):
        lhs = jnp.concatenate(
            [stacked[b * rows + g * width : b * rows + (g + 1) * width] for b in range(count)],
            axis=0,
        )
        row = taps_long_ref[g : g + 1, :]
        toeplitz = pltpu.roll(jnp.broadcast_to(row, (BLOCK, BLOCK)), 0, 1, stride=1, stride_axis=0)
        toeplitz = jnp.where(t_idx >= s_idx, toeplitz, 0.0)
        t_hi, t_lo = split2(toeplitz)
        near = dot(lhs, t_hi) + dot(lhs, t_lo)
        for b in range(count):
            pieces[b][g] = near[b * width : (b + 1) * width]
    long_term = jnp.concatenate(
        [
            jnp.concatenate(pieces[b], axis=0) + far[b * rows : (b + 1) * rows]
            for b in range(count)
        ],
        axis=1,
    )
    signal = product.astype(f32)
    mixed = query.astype(f32) * (long_term + prm[:, skip_at : skip_at + 1] * signal)
    u0_ref[...] = res_ref[...].astype(f32) + mixed


def finish_kernel(width, modes, u0_ref, q_ref, z_ref, spread_ref, lead_hi_ref, lead_lo_ref, upd_ref, sq_ref):
    rows = u0_ref.shape[0]
    spread = exact_dot(z_ref[...], spread_ref[...])
    own = own_modes(rows, spread.shape[1], width, modes)
    z_hi, z_lo = split2(jnp.where(own, spread, 0.0))
    lead_hi = lead_hi_ref[0]
    lead_lo = lead_lo_ref[0]
    far = dot(z_hi, lead_hi) + dot(z_hi, lead_lo) + dot(z_lo, lead_hi)
    updated = u0_ref[...] + q_ref[...].astype(f32) * far
    upd_ref[...] = updated
    sq_ref[0] = jnp.sum(updated * updated, axis=0, keepdims=True)


def local(projections, short_filter, decay_rate, residue, skip, norm_gain, residual):
    channels, length = residual.shape
    groups, modes = decay_rate.shape
    width = channels // groups
    rim_len = short_filter.shape[2] - 1
    count = length // BLOCK
    chunk = 256 if channels % 256 == 0 else channels
    chunk_groups = chunk // width
    lanes = chunk_groups * modes
    steps = channels // chunk

    edge = projections[:, :, length - rim_len :].transpose(0, 2, 1)
    rim = shifted(edge, "ctx", 1)
    prm = jnp.concatenate(
        [
            short_filter.astype(f32).transpose(0, 2, 1).reshape(-1, channels),
            rim.astype(f32).reshape(-1, channels),
            skip[None, :],
        ],
        axis=0,
    )
    prm = jnp.pad(prm, ((0, LANES - prm.shape[0]), (0, 0))).T

    scaled = residue * jnp.sqrt(-jnp.expm1(-2.0 * decay_rate))
    lag = jnp.arange(BLOCK, dtype=f32)
    taps_long = jnp.sum(
        scaled[:, :, None] * jnp.exp(-decay_rate[:, :, None] * lag[None, None, :]), axis=1
    )
    tail = jnp.exp(-decay_rate[:, None, :] * (BLOCK - 1 - lag)[None, :, None])
    tail = tail.reshape(steps, chunk_groups, BLOCK, modes).transpose(0, 2, 1, 3)
    w_hi, w_lo = split2(tail.reshape(steps, BLOCK, lanes))
    lead = scaled[:, :, None] * jnp.exp(-decay_rate[:, :, None] * (lag + 1.0)[None, None, :])
    lead_hi, lead_lo = split2(lead.reshape(steps, lanes, BLOCK))
    decay = jnp.exp(-decay_rate * BLOCK).reshape(steps, 1, lanes)
    positions = jnp.arange(length, dtype=f32)
    lead_all = scaled[:, :, None] * jnp.exp(-decay_rate[:, :, None] * (positions + 1.0)[None, None, :])
    lead_all_hi, lead_all_lo = split2(lead_all.reshape(steps, lanes, length))
    mode_of = jnp.arange(lanes) % modes
    select = (mode_of[:, None] == jnp.arange(LANES)[None, :]).astype(bf16)

    proj_spec = pl.BlockSpec((3, chunk, length), lambda i: (0, i, 0))
    prm_spec = pl.BlockSpec((chunk, LANES), lambda i: (i, 0))
    w_spec = pl.BlockSpec((1, BLOCK, lanes), lambda i: (i, 0, 0))
    lead_spec = pl.BlockSpec((1, lanes, BLOCK), lambda i: (i, 0, 0))
    decay_spec = pl.BlockSpec((1, 1, lanes), lambda i: (i, 0, 0))
    row_spec = pl.BlockSpec((chunk, length), lambda i: (i, 0))
    state_spec = pl.BlockSpec((chunk, LANES), lambda i: (i, 0))

    u0, query, end_state = pl.pallas_call(
        functools.partial(local_kernel, width, modes, count),
        grid=(steps,),
        in_specs=[
            proj_spec,
            prm_spec,
            w_spec,
            w_spec,
            decay_spec,
            lead_spec,
            lead_spec,
            pl.BlockSpec((chunk_groups, BLOCK), lambda i: (i, 0)),
            pl.BlockSpec((lanes, LANES), lambda i: (0, 0)),
            row_spec,
        ],
        out_specs=[row_spec, row_spec, state_spec],
        out_shape=[
            jax.ShapeDtypeStruct((channels, length), f32),
            jax.ShapeDtypeStruct((channels, length), bf16),
            jax.ShapeDtypeStruct((channels, LANES), f32),
        ],
    )(projections, prm, w_hi, w_lo, decay, lead_hi, lead_lo, taps_long, select, residual)

    size = lax.axis_size("ctx")
    dense = end_state[:, :modes].reshape(channels * modes // 128, 128)
    rate = jnp.repeat(decay_rate, width, axis=0).reshape(dense.shape)
    incoming = incoming_state(dense, rate * length, size).reshape(channels, modes)
    incoming = jnp.pad(incoming, ((0, 0), (0, LANES - modes)))

    updated, sq = pl.pallas_call(
        functools.partial(finish_kernel, width, modes),
        grid=(steps,),
        in_specs=[
            row_spec,
            row_spec,
            state_spec,
            pl.BlockSpec((LANES, lanes), lambda i: (0, 0)),
            pl.BlockSpec((1, lanes, length), lambda i: (i, 0, 0)),
            pl.BlockSpec((1, lanes, length), lambda i: (i, 0, 0)),
        ],
        out_specs=[row_spec, pl.BlockSpec((1, 1, length), lambda i: (i, 0, 0))],
        out_shape=[
            jax.ShapeDtypeStruct((channels, length), f32),
            jax.ShapeDtypeStruct((steps, 1, length), f32),
        ],
    )(u0, query, incoming, select.T, lead_all_hi, lead_all_lo)
    squares = lax.psum(jnp.sum(sq, axis=(0, 1)), "tp")
    return (updated * lax.rsqrt(squares / D + epsilon)[None, :] * norm_gain[:, None]).astype(bf16)


def solution(mesh):
    placed = (
        P(None, "tp", "ctx"),
        P(None, "tp", None),
        P("tp", None),
        P("tp", None),
        P("tp"),
        P("tp"),
        P("tp", "ctx"),
    )
    return jax.shard_map(
        local, mesh=mesh, in_specs=placed, out_specs=P("tp", "ctx"), check_vma=False
    )
```

```python
import functools

import jax
import jax.numpy as jnp
from jax import lax
from jax.experimental import pallas as pl
from jax.experimental.pallas import tpu as pltpu
from jax.sharding import PartitionSpec as P

D = 8192
epsilon = 1e-06
BLOCK = 128
LANES = 128
f32 = jnp.float32
bf16 = jnp.bfloat16


def shifted(shard, axis, by):
    size = lax.axis_size(axis)
    pairs = [(i, i + by) for i in range(size) if 0 <= i + by < size]
    return lax.ppermute(shard, axis, pairs)


def incoming_state(ends, span_rate, size):
    if size <= 1:
        total = jnp.zeros_like(ends)
        for d in range(1, size):
            total = total + jnp.exp(-span_rate * (d - 1)) * shifted(ends, "ctx", d)
        return total
    carry = shifted(ends, "ctx", 1)
    step = 1
    while step < size:
        carry = carry + jnp.exp(-span_rate * step) * shifted(carry, "ctx", step)
        step *= 2
    return carry


def split2(a):
    hi = a.astype(bf16)
    lo = (a - hi.astype(f32)).astype(bf16)
    return hi, lo


def split3(a):
    hi = a.astype(bf16)
    rest = a - hi.astype(f32)
    mid = rest.astype(bf16)
    lo = (rest - mid.astype(f32)).astype(bf16)
    return hi, mid, lo


def dot(a, b):
    return jnp.dot(a, b, preferred_element_type=f32)


def exact_dot(a, select):
    return sum(dot(part, select) for part in split3(a))


def featurize(proj_ref, prm, p, taps, rims):
    x = proj_ref[p].astype(f32)
    lane = lax.broadcasted_iota(jnp.int32, x.shape, 1)
    back2 = prm[:, rims + 2 * p : rims + 2 * p + 1]
    back1 = prm[:, rims + 2 * p + 1 : rims + 2 * p + 2]
    x1 = jnp.where(lane == 0, back1, pltpu.roll(x, 1, 1))
    x2 = jnp.where(lane == 0, back2, jnp.where(lane == 1, back1, pltpu.roll(x, 2, 1)))
    t = taps * p
    summed = prm[:, t : t + 1] * x + prm[:, t + 1 : t + 2] * x1
    summed = summed + prm[:, t + 2 : t + 3] * x2
    return summed.astype(bf16)


def own_modes(rows, lanes, width, modes):
    row = lax.broadcasted_iota(jnp.int32, (rows, lanes), 0) // width
    lane = lax.broadcasted_iota(jnp.int32, (rows, lanes), 1) // modes
    return row == lane


def product_stack(proj_ref, prm, taps, rims, count):
    key = featurize(proj_ref, prm, 1, taps, rims).astype(f32)
    value = featurize(proj_ref, prm, 2, taps, rims).astype(f32)
    product = (key * value).astype(bf16)
    stacked = jnp.concatenate(
        [product[:, b * BLOCK : (b + 1) * BLOCK] for b in range(count)], axis=0
    )
    return product, stacked


def masked_ends(stacked, w_hi_ref, w_lo_ref, rows, width, modes, count):
    ends = dot(stacked, w_hi_ref[0]) + dot(stacked, w_lo_ref[0])
    own = own_modes(rows, ends.shape[1], width, modes)
    return [jnp.where(own, ends[b * rows : (b + 1) * rows], 0.0) for b in range(count)], own


def state_kernel(width, modes, count, proj_ref, prm_ref, w_hi_ref, w_lo_ref, decay_ref, select_ref, end_ref):
    rows = proj_ref.shape[1]
    prm = prm_ref[...]
    _, stacked = product_stack(proj_ref, prm, 3, 9, count)
    ends, _ = masked_ends(stacked, w_hi_ref, w_lo_ref, rows, width, modes, count)
    decay = decay_ref[0]
    state = ends[0]
    for b in range(1, count):
        state = decay * state + ends[b]
    end_ref[...] = exact_dot(state, select_ref[...])


def mix_kernel(
    width,
    modes,
    count,
    proj_ref,
    prm_ref,
    w_hi_ref,
    w_lo_ref,
    decay_ref,
    lead_hi_ref,
    lead_lo_ref,
    taps_long_ref,
    spread_ref,
    z_ref,
    res_ref,
    upd_ref,
    sq_ref,
):
    rows = proj_ref.shape[1]
    groups = rows // width
    taps = 3
    rims = 3 * taps
    skip_at = rims + 6
    prm = prm_ref[...]
    query = featurize(proj_ref, prm, 0, taps, rims)
    product, stacked = product_stack(proj_ref, prm, taps, rims, count)
    ends, own = masked_ends(stacked, w_hi_ref, w_lo_ref, rows, width, modes, count)
    decay = decay_ref[0]
    state = jnp.where(own, exact_dot(z_ref[...], spread_ref[...]), 0.0)
    entering = []
    for b in range(count):
        entering.append(state)
        state = decay * state + ends[b]
    z_hi, z_lo = split2(jnp.concatenate(entering, axis=0))
    lead_hi = lead_hi_ref[0]
    lead_lo = lead_lo_ref[0]
    far = dot(z_hi, lead_hi) + dot(z_hi, lead_lo) + dot(z_lo, lead_hi)

    s_idx = lax.broadcasted_iota(jnp.int32, (BLOCK, BLOCK), 0)
    t_idx = lax.broadcasted_iota(jnp.int32, (BLOCK, BLOCK), 1)
    pieces = [[None] * groups for _ in range(count)]
    for g in range(groups):
        lhs = jnp.concatenate(
            [stacked[b * rows + g * width : b * rows + (g + 1) * width] for b in range(count)],
            axis=0,
        )
        row = taps_long_ref[g : g + 1, :]
        toeplitz = pltpu.roll(jnp.broadcast_to(row, (BLOCK, BLOCK)), 0, 1, stride=1, stride_axis=0)
        toeplitz = jnp.where(t_idx >= s_idx, toeplitz, 0.0)
        t_hi, t_lo = split2(toeplitz)
        near = dot(lhs, t_hi) + dot(lhs, t_lo)
        for b in range(count):
            pieces[b][g] = near[b * width : (b + 1) * width]
    long_term = jnp.concatenate(
        [
            jnp.concatenate(pieces[b], axis=0) + far[b * rows : (b + 1) * rows]
            for b in range(count)
        ],
        axis=1,
    )
    signal = product.astype(f32)
    mixed = query.astype(f32) * (long_term + prm[:, skip_at : skip_at + 1] * signal)
    updated = res_ref[...].astype(f32) + mixed
    upd_ref[...] = updated
    sq_ref[0] = jnp.sum(updated * updated, axis=0, keepdims=True)


def local(projections, short_filter, decay_rate, residue, skip, norm_gain, residual):
    channels, length = residual.shape
    groups, modes = decay_rate.shape
    width = channels // groups
    rim_len = short_filter.shape[2] - 1
    count = length // BLOCK
    chunk = 256 if channels % 256 == 0 else channels
    chunk_groups = chunk // width
    lanes = chunk_groups * modes
    steps = channels // chunk

    edge = projections[:, :, length - rim_len :].transpose(0, 2, 1)
    rim = shifted(edge, "ctx", 1)
    prm = jnp.concatenate(
        [
            short_filter.astype(f32).transpose(0, 2, 1).reshape(-1, channels),
            rim.astype(f32).reshape(-1, channels),
            skip[None, :],
        ],
        axis=0,
    )
    prm = jnp.pad(prm, ((0, LANES - prm.shape[0]), (0, 0))).T

    scaled = residue * jnp.sqrt(-jnp.expm1(-2.0 * decay_rate))
    lag = jnp.arange(BLOCK, dtype=f32)
    taps_long = jnp.sum(
        scaled[:, :, None] * jnp.exp(-decay_rate[:, :, None] * lag[None, None, :]), axis=1
    )
    tail = jnp.exp(-decay_rate[:, None, :] * (BLOCK - 1 - lag)[None, :, None])
    tail = tail.reshape(steps, chunk_groups, BLOCK, modes).transpose(0, 2, 1, 3)
    w_hi, w_lo = split2(tail.reshape(steps, BLOCK, lanes))
    lead = scaled[:, :, None] * jnp.exp(-decay_rate[:, :, None] * (lag + 1.0)[None, None, :])
    lead_hi, lead_lo = split2(lead.reshape(steps, lanes, BLOCK))
    decay = jnp.exp(-decay_rate * BLOCK).reshape(steps, 1, lanes)
    mode_of = jnp.arange(lanes) % modes
    select = (mode_of[:, None] == jnp.arange(LANES)[None, :]).astype(bf16)

    proj_spec = pl.BlockSpec((3, chunk, length), lambda i: (0, i, 0))
    prm_spec = pl.BlockSpec((chunk, LANES), lambda i: (i, 0))
    w_spec = pl.BlockSpec((1, BLOCK, lanes), lambda i: (i, 0, 0))
    lead_spec = pl.BlockSpec((1, lanes, BLOCK), lambda i: (i, 0, 0))
    decay_spec = pl.BlockSpec((1, 1, lanes), lambda i: (i, 0, 0))
    row_spec = pl.BlockSpec((chunk, length), lambda i: (i, 0))
    state_spec = pl.BlockSpec((chunk, LANES), lambda i: (i, 0))

    end_state = pl.pallas_call(
        functools.partial(state_kernel, width, modes, count),
        grid=(steps,),
        in_specs=[
            proj_spec,
            prm_spec,
            w_spec,
            w_spec,
            decay_spec,
            pl.BlockSpec((lanes, LANES), lambda i: (0, 0)),
        ],
        out_specs=state_spec,
        out_shape=jax.ShapeDtypeStruct((channels, LANES), f32),
    )(projections, prm, w_hi, w_lo, decay, select)

    size = lax.axis_size("ctx")
    dense = end_state[:, :modes].reshape(channels * modes // 128, 128)
    rate = jnp.repeat(decay_rate, width, axis=0).reshape(dense.shape)
    incoming = incoming_state(dense, rate * length, size).reshape(channels, modes)
    incoming = jnp.pad(incoming, ((0, 0), (0, LANES - modes)))

    updated, sq = pl.pallas_call(
        functools.partial(mix_kernel, width, modes, count),
        grid=(steps,),
        in_specs=[
            proj_spec,
            prm_spec,
            w_spec,
            w_spec,
            decay_spec,
            lead_spec,
            lead_spec,
            pl.BlockSpec((chunk_groups, BLOCK), lambda i: (i, 0)),
            pl.BlockSpec((LANES, lanes), lambda i: (0, 0)),
            state_spec,
            row_spec,
        ],
        out_specs=[row_spec, pl.BlockSpec((1, 1, length), lambda i: (i, 0, 0))],
        out_shape=[
            jax.ShapeDtypeStruct((channels, length), f32),
            jax.ShapeDtypeStruct((steps, 1, length), f32),
        ],
    )(projections, prm, w_hi, w_lo, decay, lead_hi, lead_lo, taps_long, select.T, incoming, residual)
    squares = lax.psum(jnp.sum(sq, axis=(0, 1)), "tp")
    return (updated * lax.rsqrt(squares / D + epsilon)[None, :] * norm_gain[:, None]).astype(bf16)


def solution(mesh):
    placed = (
        P(None, "tp", "ctx"),
        P(None, "tp", None),
        P("tp", None),
        P("tp", None),
        P("tp"),
        P("tp"),
        P("tp", "ctx"),
    )
    return jax.shard_map(
        local, mesh=mesh, in_specs=placed, out_specs=P("tp", "ctx"), check_vma=False
    )
```

```python
import functools

import jax
import jax.numpy as jnp
from jax import lax
from jax.experimental import pallas as pl
from jax.experimental.pallas import tpu as pltpu
from jax.sharding import PartitionSpec as P

D = 8192
epsilon = 1e-06
BLOCK = 128
LANES = 128
f32 = jnp.float32
bf16 = jnp.bfloat16


def shifted(shard, axis, by):
    size = lax.axis_size(axis)
    pairs = [(i, i + by) for i in range(size) if 0 <= i + by < size]
    return lax.ppermute(shard, axis, pairs)


def incoming_state(ends, span_rate, size):
    place = lax.axis_index("ctx")
    copies = jnp.broadcast_to(ends[None], (size,) + ends.shape)
    gathered = lax.all_to_all(copies, "ctx", 0, 0)
    earlier = jnp.arange(size, dtype=jnp.int32)
    gap = jnp.maximum(place - 1 - earlier, 0).astype(f32)
    weight = jnp.where(
        (earlier < place)[:, None, None],
        jnp.exp(-span_rate[None] * gap[:, None, None]),
        0.0,
    )
    return jnp.sum(weight * gathered, axis=0)


def split2(a):
    hi = a.astype(bf16)
    lo = (a - hi.astype(f32)).astype(bf16)
    return hi, lo


def split3(a):
    hi = a.astype(bf16)
    rest = a - hi.astype(f32)
    mid = rest.astype(bf16)
    lo = (rest - mid.astype(f32)).astype(bf16)
    return hi, mid, lo


def dot(a, b):
    return jnp.dot(a, b, preferred_element_type=f32)


def exact_dot(a, select):
    return sum(dot(part, select) for part in split3(a))


def featurize(proj_ref, prm, p, taps, rims):
    x = proj_ref[p].astype(f32)
    lane = lax.broadcasted_iota(jnp.int32, x.shape, 1)
    back2 = prm[:, rims + 2 * p : rims + 2 * p + 1]
    back1 = prm[:, rims + 2 * p + 1 : rims + 2 * p + 2]
    x1 = jnp.where(lane == 0, back1, pltpu.roll(x, 1, 1))
    x2 = jnp.where(lane == 0, back2, jnp.where(lane == 1, back1, pltpu.roll(x, 2, 1)))
    t = taps * p
    summed = prm[:, t : t + 1] * x + prm[:, t + 1 : t + 2] * x1
    summed = summed + prm[:, t + 2 : t + 3] * x2
    return summed.astype(bf16)


def own_modes(rows, lanes, width, modes):
    row = lax.broadcasted_iota(jnp.int32, (rows, lanes), 0) // width
    lane = lax.broadcasted_iota(jnp.int32, (rows, lanes), 1) // modes
    return row == lane


def product_stack(proj_ref, prm, taps, rims, count):
    key = featurize(proj_ref, prm, 1, taps, rims).astype(f32)
    value = featurize(proj_ref, prm, 2, taps, rims).astype(f32)
    product = (key * value).astype(bf16)
    stacked = jnp.concatenate(
        [product[:, b * BLOCK : (b + 1) * BLOCK] for b in range(count)], axis=0
    )
    return product, stacked


def masked_ends(stacked, w_hi_ref, w_lo_ref, rows, width, modes, count):
    ends = dot(stacked, w_hi_ref[0]) + dot(stacked, w_lo_ref[0])
    own = own_modes(rows, ends.shape[1], width, modes)
    return [jnp.where(own, ends[b * rows : (b + 1) * rows], 0.0) for b in range(count)], own


def state_kernel(width, modes, count, proj_ref, prm_ref, w_hi_ref, w_lo_ref, decay_ref, select_ref, end_ref):
    rows = proj_ref.shape[1]
    prm = prm_ref[...]
    _, stacked = product_stack(proj_ref, prm, 3, 9, count)
    ends, _ = masked_ends(stacked, w_hi_ref, w_lo_ref, rows, width, modes, count)
    decay = decay_ref[0]
    state = ends[0]
    for b in range(1, count):
        state = decay * state + ends[b]
    end_ref[...] = exact_dot(state, select_ref[...])


def mix_kernel(
    width,
    modes,
    count,
    proj_ref,
    prm_ref,
    w_hi_ref,
    w_lo_ref,
    decay_ref,
    lead_hi_ref,
    lead_lo_ref,
    taps_long_ref,
    spread_ref,
    z_ref,
    res_ref,
    upd_ref,
    sq_ref,
):
    rows = proj_ref.shape[1]
    groups = rows // width
    taps = 3
    rims = 3 * taps
    skip_at = rims + 6
    prm = prm_ref[...]
    query = featurize(proj_ref, prm, 0, taps, rims)
    product, stacked = product_stack(proj_ref, prm, taps, rims, count)
    ends, own = masked_ends(stacked, w_hi_ref, w_lo_ref, rows, width, modes, count)
    decay = decay_ref[0]
    state = jnp.where(own, exact_dot(z_ref[...], spread_ref[...]), 0.0)
    entering = []
    for b in range(count):
        entering.append(state)
        state = decay * state + ends[b]
    z_hi, z_lo = split2(jnp.concatenate(entering, axis=0))
    lead_hi = lead_hi_ref[0]
    lead_lo = lead_lo_ref[0]
    far = dot(z_hi, lead_hi) + dot(z_hi, lead_lo) + dot(z_lo, lead_hi)

    s_idx = lax.broadcasted_iota(jnp.int32, (BLOCK, BLOCK), 0)
    t_idx = lax.broadcasted_iota(jnp.int32, (BLOCK, BLOCK), 1)
    pieces = [[None] * groups for _ in range(count)]
    for g in range(groups):
        lhs = jnp.concatenate(
            [stacked[b * rows + g * width : b * rows + (g + 1) * width] for b in range(count)],
            axis=0,
        )
        row = taps_long_ref[g : g + 1, :]
        toeplitz = pltpu.roll(jnp.broadcast_to(row, (BLOCK, BLOCK)), 0, 1, stride=1, stride_axis=0)
        toeplitz = jnp.where(t_idx >= s_idx, toeplitz, 0.0)
        t_hi, t_lo = split2(toeplitz)
        near = dot(lhs, t_hi) + dot(lhs, t_lo)
        for b in range(count):
            pieces[b][g] = near[b * width : (b + 1) * width]
    long_term = jnp.concatenate(
        [
            jnp.concatenate(pieces[b], axis=0) + far[b * rows : (b + 1) * rows]
            for b in range(count)
        ],
        axis=1,
    )
    signal = product.astype(f32)
    mixed = query.astype(f32) * (long_term + prm[:, skip_at : skip_at + 1] * signal)
    updated = res_ref[...].astype(f32) + mixed
    upd_ref[...] = updated
    sq_ref[0] = jnp.sum(updated * updated, axis=0, keepdims=True)


def local(projections, short_filter, decay_rate, residue, skip, norm_gain, residual):
    channels, length = residual.shape
    groups, modes = decay_rate.shape
    width = channels // groups
    rim_len = short_filter.shape[2] - 1
    count = length // BLOCK
    chunk = 256 if channels % 256 == 0 else channels
    chunk_groups = chunk // width
    lanes = chunk_groups * modes
    steps = channels // chunk

    edge = projections[:, :, length - rim_len :].transpose(0, 2, 1)
    rim = shifted(edge, "ctx", 1)
    prm = jnp.concatenate(
        [
            short_filter.astype(f32).transpose(0, 2, 1).reshape(-1, channels),
            rim.astype(f32).reshape(-1, channels),
            skip[None, :],
        ],
        axis=0,
    )
    prm = jnp.pad(prm, ((0, LANES - prm.shape[0]), (0, 0))).T

    scaled = residue * jnp.sqrt(-jnp.expm1(-2.0 * decay_rate))
    lag = jnp.arange(BLOCK, dtype=f32)
    taps_long = jnp.sum(
        scaled[:, :, None] * jnp.exp(-decay_rate[:, :, None] * lag[None, None, :]), axis=1
    )
    tail = jnp.exp(-decay_rate[:, None, :] * (BLOCK - 1 - lag)[None, :, None])
    tail = tail.reshape(steps, chunk_groups, BLOCK, modes).transpose(0, 2, 1, 3)
    w_hi, w_lo = split2(tail.reshape(steps, BLOCK, lanes))
    lead = scaled[:, :, None] * jnp.exp(-decay_rate[:, :, None] * (lag + 1.0)[None, None, :])
    lead_hi, lead_lo = split2(lead.reshape(steps, lanes, BLOCK))
    decay = jnp.exp(-decay_rate * BLOCK).reshape(steps, 1, lanes)
    mode_of = jnp.arange(lanes) % modes
    select = (mode_of[:, None] == jnp.arange(LANES)[None, :]).astype(bf16)

    proj_spec = pl.BlockSpec((3, chunk, length), lambda i: (0, i, 0))
    prm_spec = pl.BlockSpec((chunk, LANES), lambda i: (i, 0))
    w_spec = pl.BlockSpec((1, BLOCK, lanes), lambda i: (i, 0, 0))
    lead_spec = pl.BlockSpec((1, lanes, BLOCK), lambda i: (i, 0, 0))
    decay_spec = pl.BlockSpec((1, 1, lanes), lambda i: (i, 0, 0))
    row_spec = pl.BlockSpec((chunk, length), lambda i: (i, 0))
    state_spec = pl.BlockSpec((chunk, LANES), lambda i: (i, 0))

    end_state = pl.pallas_call(
        functools.partial(state_kernel, width, modes, count),
        grid=(steps,),
        in_specs=[
            proj_spec,
            prm_spec,
            w_spec,
            w_spec,
            decay_spec,
            pl.BlockSpec((lanes, LANES), lambda i: (0, 0)),
        ],
        out_specs=state_spec,
        out_shape=jax.ShapeDtypeStruct((channels, LANES), f32),
    )(projections, prm, w_hi, w_lo, decay, select)

    size = lax.axis_size("ctx")
    dense = end_state[:, :modes].reshape(channels * modes // 128, 128)
    rate = jnp.repeat(decay_rate, width, axis=0).reshape(dense.shape)
    incoming = incoming_state(dense, rate * length, size).reshape(channels, modes)
    incoming = jnp.pad(incoming, ((0, 0), (0, LANES - modes)))

    updated, sq = pl.pallas_call(
        functools.partial(mix_kernel, width, modes, count),
        grid=(steps,),
        in_specs=[
            proj_spec,
            prm_spec,
            w_spec,
            w_spec,
            decay_spec,
            lead_spec,
            lead_spec,
            pl.BlockSpec((chunk_groups, BLOCK), lambda i: (i, 0)),
            pl.BlockSpec((LANES, lanes), lambda i: (0, 0)),
            state_spec,
            row_spec,
        ],
        out_specs=[row_spec, pl.BlockSpec((1, 1, length), lambda i: (i, 0, 0))],
        out_shape=[
            jax.ShapeDtypeStruct((channels, length), f32),
            jax.ShapeDtypeStruct((steps, 1, length), f32),
        ],
    )(projections, prm, w_hi, w_lo, decay, lead_hi, lead_lo, taps_long, select.T, incoming, residual)
    squares = lax.psum(jnp.sum(sq, axis=(0, 1)), "tp")
    return (updated * lax.rsqrt(squares / D + epsilon)[None, :] * norm_gain[:, None]).astype(bf16)


def solution(mesh):
    placed = (
        P(None, "tp", "ctx"),
        P(None, "tp", None),
        P("tp", None),
        P("tp", None),
        P("tp"),
        P("tp"),
        P("tp", "ctx"),
    )
    return jax.shard_map(
        local, mesh=mesh, in_specs=placed, out_specs=P("tp", "ctx"), check_vma=False
    )
```

```python
import functools

import jax
import jax.numpy as jnp
from jax import lax
from jax.experimental import pallas as pl
from jax.experimental.pallas import tpu as pltpu
from jax.sharding import PartitionSpec as P

D = 8192
epsilon = 1e-06
BLOCK = 128
LANES = 128
f32 = jnp.float32
bf16 = jnp.bfloat16


def shifted(shard, axis, by):
    size = lax.axis_size(axis)
    pairs = [(i, i + by) for i in range(size) if 0 <= i + by < size]
    return lax.ppermute(shard, axis, pairs)


def incoming_state(ends, span_rate, size):
    place = lax.axis_index("ctx")
    copies = jnp.broadcast_to(ends[None], (size,) + ends.shape)
    gathered = lax.all_to_all(copies, "ctx", 0, 0)
    earlier = jnp.arange(size, dtype=jnp.int32)
    gap = jnp.maximum(place - 1 - earlier, 0).astype(f32)
    weight = jnp.where(
        (earlier < place)[:, None, None],
        jnp.exp(-span_rate[None] * gap[:, None, None]),
        0.0,
    )
    return jnp.sum(weight * gathered, axis=0)


def split2(a):
    hi = a.astype(bf16)
    lo = (a - hi.astype(f32)).astype(bf16)
    return hi, lo


def split3(a):
    hi = a.astype(bf16)
    rest = a - hi.astype(f32)
    mid = rest.astype(bf16)
    lo = (rest - mid.astype(f32)).astype(bf16)
    return hi, mid, lo


def dot(a, b):
    return jnp.dot(a, b, preferred_element_type=f32)


def exact_dot(a, select):
    return sum(dot(part, select) for part in split3(a))


def featurize(proj_ref, prm, p, taps, rims):
    x = proj_ref[p].astype(f32)
    lane = lax.broadcasted_iota(jnp.int32, x.shape, 1)
    back2 = prm[:, rims + 2 * p : rims + 2 * p + 1]
    back1 = prm[:, rims + 2 * p + 1 : rims + 2 * p + 2]
    x1 = jnp.where(lane == 0, back1, pltpu.roll(x, 1, 1))
    x2 = jnp.where(lane == 0, back2, jnp.where(lane == 1, back1, pltpu.roll(x, 2, 1)))
    t = taps * p
    summed = prm[:, t : t + 1] * x + prm[:, t + 1 : t + 2] * x1
    summed = summed + prm[:, t + 2 : t + 3] * x2
    return summed.astype(bf16)


def own_modes(rows, lanes, width, modes):
    row = lax.broadcasted_iota(jnp.int32, (rows, lanes), 0) // width
    lane = lax.broadcasted_iota(jnp.int32, (rows, lanes), 1) // modes
    return row == lane


def product_stack(proj_ref, prm, taps, rims, count):
    key = featurize(proj_ref, prm, 1, taps, rims).astype(f32)
    value = featurize(proj_ref, prm, 2, taps, rims).astype(f32)
    product = (key * value).astype(bf16)
    stacked = jnp.concatenate(
        [product[:, b * BLOCK : (b + 1) * BLOCK] for b in range(count)], axis=0
    )
    return product, stacked


def masked_ends(stacked, w_hi_ref, w_lo_ref, rows, width, modes, count):
    ends = dot(stacked, w_hi_ref[0]) + dot(stacked, w_lo_ref[0])
    own = own_modes(rows, ends.shape[1], width, modes)
    return [jnp.where(own, ends[b * rows : (b + 1) * rows], 0.0) for b in range(count)], own


def state_kernel(width, modes, count, proj_ref, prm_ref, w_hi_ref, w_lo_ref, decay_ref, select_ref, end_ref):
    rows = proj_ref.shape[1]
    prm = prm_ref[...]
    _, stacked = product_stack(proj_ref, prm, 3, 9, count)
    ends, _ = masked_ends(stacked, w_hi_ref, w_lo_ref, rows, width, modes, count)
    decay = decay_ref[0]
    state = ends[0]
    for b in range(1, count):
        state = decay * state + ends[b]
    end_ref[...] = exact_dot(state, select_ref[...])


def local_kernel(
    width,
    modes,
    count,
    proj_ref,
    prm_ref,
    w_hi_ref,
    w_lo_ref,
    decay_ref,
    lead_hi_ref,
    lead_lo_ref,
    taps_long_ref,
    res_ref,
    u0_ref,
    q_ref,
):
    rows = proj_ref.shape[1]
    groups = rows // width
    taps = 3
    rims = 3 * taps
    skip_at = rims + 6
    prm = prm_ref[...]
    query = featurize(proj_ref, prm, 0, taps, rims)
    q_ref[...] = query
    key = featurize(proj_ref, prm, 1, taps, rims).astype(f32)
    value = featurize(proj_ref, prm, 2, taps, rims).astype(f32)
    product = (key * value).astype(bf16)
    stacked = jnp.concatenate(
        [product[:, b * BLOCK : (b + 1) * BLOCK] for b in range(count)], axis=0
    )
    ends = dot(stacked, w_hi_ref[0]) + dot(stacked, w_lo_ref[0])
    lanes = ends.shape[1]
    own = own_modes(rows, lanes, width, modes)
    decay = decay_ref[0]
    state = jnp.where(own, ends[0:rows], 0.0)
    entering = [jnp.zeros_like(state)]
    for b in range(1, count):
        entering.append(state)
        state = decay * state + jnp.where(own, ends[b * rows : (b + 1) * rows], 0.0)
    z_hi, z_lo = split2(jnp.concatenate(entering, axis=0))
    lead_hi = lead_hi_ref[0]
    lead_lo = lead_lo_ref[0]
    far = dot(z_hi, lead_hi) + dot(z_hi, lead_lo) + dot(z_lo, lead_hi)

    s_idx = lax.broadcasted_iota(jnp.int32, (BLOCK, BLOCK), 0)
    t_idx = lax.broadcasted_iota(jnp.int32, (BLOCK, BLOCK), 1)
    pieces = [[None] * groups for _ in range(count)]
    for g in range(groups):
        lhs = jnp.concatenate(
            [stacked[b * rows + g * width : b * rows + (g + 1) * width] for b in range(count)],
            axis=0,
        )
        row = taps_long_ref[g : g + 1, :]
        toeplitz = pltpu.roll(jnp.broadcast_to(row, (BLOCK, BLOCK)), 0, 1, stride=1, stride_axis=0)
        toeplitz = jnp.where(t_idx >= s_idx, toeplitz, 0.0)
        t_hi, t_lo = split2(toeplitz)
        near = dot(lhs, t_hi) + dot(lhs, t_lo)
        for b in range(count):
            pieces[b][g] = near[b * width : (b + 1) * width]
    long_term = jnp.concatenate(
        [
            jnp.concatenate(pieces[b], axis=0) + far[b * rows : (b + 1) * rows]
            for b in range(count)
        ],
        axis=1,
    )
    signal = product.astype(f32)
    mixed = query.astype(f32) * (long_term + prm[:, skip_at : skip_at + 1] * signal)
    u0_ref[...] = res_ref[...].astype(f32) + mixed


def finish_kernel(width, modes, u0_ref, q_ref, z_ref, spread_ref, lead_hi_ref, lead_lo_ref, upd_ref, sq_ref):
    rows = u0_ref.shape[0]
    spread = exact_dot(z_ref[...], spread_ref[...])
    own = own_modes(rows, spread.shape[1], width, modes)
    z_hi, z_lo = split2(jnp.where(own, spread, 0.0))
    lead_hi = lead_hi_ref[0]
    lead_lo = lead_lo_ref[0]
    far = dot(z_hi, lead_hi) + dot(z_hi, lead_lo) + dot(z_lo, lead_hi)
    updated = u0_ref[...] + q_ref[...].astype(f32) * far
    upd_ref[...] = updated
    sq_ref[0] = jnp.sum(updated * updated, axis=0, keepdims=True)


def local(projections, short_filter, decay_rate, residue, skip, norm_gain, residual):
    channels, length = residual.shape
    groups, modes = decay_rate.shape
    width = channels // groups
    rim_len = short_filter.shape[2] - 1
    count = length // BLOCK
    chunk = 256 if channels % 256 == 0 else channels
    chunk_groups = chunk // width
    lanes = chunk_groups * modes
    steps = channels // chunk

    edge = projections[:, :, length - rim_len :].transpose(0, 2, 1)
    rim = shifted(edge, "ctx", 1)
    prm = jnp.concatenate(
        [
            short_filter.astype(f32).transpose(0, 2, 1).reshape(-1, channels),
            rim.astype(f32).reshape(-1, channels),
            skip[None, :],
        ],
        axis=0,
    )
    prm = jnp.pad(prm, ((0, LANES - prm.shape[0]), (0, 0))).T

    scaled = residue * jnp.sqrt(-jnp.expm1(-2.0 * decay_rate))
    lag = jnp.arange(BLOCK, dtype=f32)
    taps_long = jnp.sum(
        scaled[:, :, None] * jnp.exp(-decay_rate[:, :, None] * lag[None, None, :]), axis=1
    )
    tail = jnp.exp(-decay_rate[:, None, :] * (BLOCK - 1 - lag)[None, :, None])
    tail = tail.reshape(steps, chunk_groups, BLOCK, modes).transpose(0, 2, 1, 3)
    w_hi, w_lo = split2(tail.reshape(steps, BLOCK, lanes))
    lead = scaled[:, :, None] * jnp.exp(-decay_rate[:, :, None] * (lag + 1.0)[None, None, :])
    lead_hi, lead_lo = split2(lead.reshape(steps, lanes, BLOCK))
    decay = jnp.exp(-decay_rate * BLOCK).reshape(steps, 1, lanes)
    mode_of = jnp.arange(lanes) % modes
    select = (mode_of[:, None] == jnp.arange(LANES)[None, :]).astype(bf16)

    proj_spec = pl.BlockSpec((3, chunk, length), lambda i: (0, i, 0))
    prm_spec = pl.BlockSpec((chunk, LANES), lambda i: (i, 0))
    w_spec = pl.BlockSpec((1, BLOCK, lanes), lambda i: (i, 0, 0))
    lead_spec = pl.BlockSpec((1, lanes, BLOCK), lambda i: (i, 0, 0))
    decay_spec = pl.BlockSpec((1, 1, lanes), lambda i: (i, 0, 0))
    row_spec = pl.BlockSpec((chunk, length), lambda i: (i, 0))
    state_spec = pl.BlockSpec((chunk, LANES), lambda i: (i, 0))

    end_state = pl.pallas_call(
        functools.partial(state_kernel, width, modes, count),
        grid=(steps,),
        in_specs=[
            proj_spec,
            prm_spec,
            w_spec,
            w_spec,
            decay_spec,
            pl.BlockSpec((lanes, LANES), lambda i: (0, 0)),
        ],
        out_specs=state_spec,
        out_shape=jax.ShapeDtypeStruct((channels, LANES), f32),
    )(projections, prm, w_hi, w_lo, decay, select)

    size = lax.axis_size("ctx")
    dense = end_state[:, :modes].reshape(channels * modes // 128, 128)
    rate = jnp.repeat(decay_rate, width, axis=0).reshape(dense.shape)
    incoming = incoming_state(dense, rate * length, size).reshape(channels, modes)
    incoming = jnp.pad(incoming, ((0, 0), (0, LANES - modes)))

    u0, query = pl.pallas_call(
        functools.partial(local_kernel, width, modes, count),
        grid=(steps,),
        in_specs=[
            proj_spec,
            prm_spec,
            w_spec,
            w_spec,
            decay_spec,
            lead_spec,
            lead_spec,
            pl.BlockSpec((chunk_groups, BLOCK), lambda i: (i, 0)),
            row_spec,
        ],
        out_specs=[row_spec, row_spec],
        out_shape=[
            jax.ShapeDtypeStruct((channels, length), f32),
            jax.ShapeDtypeStruct((channels, length), bf16),
        ],
    )(projections, prm, w_hi, w_lo, decay, lead_hi, lead_lo, taps_long, residual)

    positions = jnp.arange(length, dtype=f32)
    lead_all = scaled[:, :, None] * jnp.exp(-decay_rate[:, :, None] * (positions + 1.0)[None, None, :])
    lead_all_hi, lead_all_lo = split2(lead_all.reshape(steps, lanes, length))
    updated, sq = pl.pallas_call(
        functools.partial(finish_kernel, width, modes),
        grid=(steps,),
        in_specs=[
            row_spec,
            row_spec,
            state_spec,
            pl.BlockSpec((LANES, lanes), lambda i: (0, 0)),
            pl.BlockSpec((1, lanes, length), lambda i: (i, 0, 0)),
            pl.BlockSpec((1, lanes, length), lambda i: (i, 0, 0)),
        ],
        out_specs=[row_spec, pl.BlockSpec((1, 1, length), lambda i: (i, 0, 0))],
        out_shape=[
            jax.ShapeDtypeStruct((channels, length), f32),
            jax.ShapeDtypeStruct((steps, 1, length), f32),
        ],
    )(u0, query, incoming, select.T, lead_all_hi, lead_all_lo)
    squares = lax.psum(jnp.sum(sq, axis=(0, 1)), "tp")
    return (updated * lax.rsqrt(squares / D + epsilon)[None, :] * norm_gain[:, None]).astype(bf16)


def solution(mesh):
    placed = (
        P(None, "tp", "ctx"),
        P(None, "tp", None),
        P("tp", None),
        P("tp", None),
        P("tp"),
        P("tp"),
        P("tp", "ctx"),
    )
    return jax.shard_map(
        local, mesh=mesh, in_specs=placed, out_specs=P("tp", "ctx"), check_vma=False
    )
```

```python
import functools

import jax
import jax.numpy as jnp
from jax import lax
from jax.experimental import pallas as pl
from jax.experimental.pallas import tpu as pltpu
from jax.sharding import PartitionSpec as P

D = 8192
epsilon = 1e-06
BLOCK = 128
LANES = 128
f32 = jnp.float32
bf16 = jnp.bfloat16


def shifted(shard, axis, by):
    size = lax.axis_size(axis)
    pairs = [(i, i + by) for i in range(size) if 0 <= i + by < size]
    return lax.ppermute(shard, axis, pairs)


def incoming_state(ends, span_rate, size):
    place = lax.axis_index("ctx")
    copies = jnp.broadcast_to(ends[None], (size,) + ends.shape)
    gathered = lax.all_to_all(copies, "ctx", 0, 0)
    earlier = jnp.arange(size, dtype=jnp.int32)
    gap = jnp.maximum(place - 1 - earlier, 0).astype(f32)
    weight = jnp.where(
        (earlier < place)[:, None, None],
        jnp.exp(-span_rate[None] * gap[:, None, None]),
        0.0,
    )
    return jnp.sum(weight * gathered, axis=0)


def split2(a):
    hi = a.astype(bf16)
    lo = (a - hi.astype(f32)).astype(bf16)
    return hi, lo


def split3(a):
    hi = a.astype(bf16)
    rest = a - hi.astype(f32)
    mid = rest.astype(bf16)
    lo = (rest - mid.astype(f32)).astype(bf16)
    return hi, mid, lo


def dot(a, b):
    return jnp.dot(a, b, preferred_element_type=f32)


def exact_dot(a, select):
    return sum(dot(part, select) for part in split3(a))


def featurize(proj_ref, prm, p, taps, rims):
    x = proj_ref[p].astype(f32)
    lane = lax.broadcasted_iota(jnp.int32, x.shape, 1)
    back2 = prm[:, rims + 2 * p : rims + 2 * p + 1]
    back1 = prm[:, rims + 2 * p + 1 : rims + 2 * p + 2]
    x1 = jnp.where(lane == 0, back1, pltpu.roll(x, 1, 1))
    x2 = jnp.where(lane == 0, back2, jnp.where(lane == 1, back1, pltpu.roll(x, 2, 1)))
    t = taps * p
    summed = prm[:, t : t + 1] * x + prm[:, t + 1 : t + 2] * x1
    summed = summed + prm[:, t + 2 : t + 3] * x2
    return summed.astype(bf16)


def own_modes(rows, lanes, width, modes):
    row = lax.broadcasted_iota(jnp.int32, (rows, lanes), 0) // width
    lane = lax.broadcasted_iota(jnp.int32, (rows, lanes), 1) // modes
    return row == lane


def product_stack(proj_ref, prm, taps, rims, count):
    key = featurize(proj_ref, prm, 1, taps, rims).astype(f32)
    value = featurize(proj_ref, prm, 2, taps, rims).astype(f32)
    product = (key * value).astype(bf16)
    stacked = jnp.concatenate(
        [product[:, b * BLOCK : (b + 1) * BLOCK] for b in range(count)], axis=0
    )
    return product, stacked


def masked_ends(stacked, w_hi_ref, w_lo_ref, rows, width, modes, count):
    ends = dot(stacked, w_hi_ref[0]) + dot(stacked, w_lo_ref[0])
    own = own_modes(rows, ends.shape[1], width, modes)
    return [jnp.where(own, ends[b * rows : (b + 1) * rows], 0.0) for b in range(count)], own


def state_kernel(width, modes, proj_ref, prm_ref, lam_ref, out_ref):
    rows, length = proj_ref.shape[1], proj_ref.shape[2]
    prm = prm_ref[...]
    key = featurize(proj_ref, prm, 1, 3, 9).astype(f32)
    value = featurize(proj_ref, prm, 2, 3, 9).astype(f32)
    product = (key * value).astype(bf16)
    lam = lam_ref[0]
    lanes = lam.shape[1]
    span = (length - 1 - lax.broadcasted_iota(jnp.int32, (length, lanes), 0)).astype(f32)
    w_hi, w_lo = split2(jnp.exp(-lam * span))
    ends = dot(product, w_hi) + dot(product, w_lo)
    own = own_modes(rows, lanes, width, modes)
    out_ref[...] = exact_dot(jnp.where(own, ends, 0.0), select_matrix(lanes, modes))


def select_matrix(lanes, modes):
    mode = lax.broadcasted_iota(jnp.int32, (lanes, LANES), 0) % modes
    lane = lax.broadcasted_iota(jnp.int32, (lanes, LANES), 1)
    return (mode == lane).astype(bf16)


def spread_matrix(lanes, modes):
    lane = lax.broadcasted_iota(jnp.int32, (LANES, lanes), 0)
    mode = lax.broadcasted_iota(jnp.int32, (LANES, lanes), 1) % modes
    return (mode == lane).astype(bf16)


def lead_table(col, first, count):
    lag = (first + lax.broadcasted_iota(jnp.int32, (col.shape[0], count), 1)).astype(f32)
    return col[:, 1:2] * jnp.exp(-col[:, 0:1] * lag)


def local_kernel(
    width,
    modes,
    count,
    proj_ref,
    prm_ref,
    lam_ref,
    col_ref,
    res_ref,
    u0_ref,
    q_ref,
):
    rows = proj_ref.shape[1]
    groups = rows // width
    taps = 3
    rims = 3 * taps
    skip_at = rims + 6
    prm = prm_ref[...]
    query = featurize(proj_ref, prm, 0, taps, rims)
    q_ref[...] = query
    key = featurize(proj_ref, prm, 1, taps, rims).astype(f32)
    value = featurize(proj_ref, prm, 2, taps, rims).astype(f32)
    product = (key * value).astype(bf16)
    stacked = jnp.concatenate(
        [product[:, b * BLOCK : (b + 1) * BLOCK] for b in range(count)], axis=0
    )
    lam = lam_ref[0]
    col = col_ref[0]
    lanes = lam.shape[1]
    span = (BLOCK - 1 - lax.broadcasted_iota(jnp.int32, (BLOCK, lanes), 0)).astype(f32)
    w_hi, w_lo = split2(jnp.exp(-lam * span))
    ends = dot(stacked, w_hi) + dot(stacked, w_lo)
    own = own_modes(rows, lanes, width, modes)
    decay = jnp.exp(-lam * float(BLOCK))
    state = jnp.where(own, ends[0:rows], 0.0)
    entering = [jnp.zeros_like(state)]
    for b in range(1, count):
        entering.append(state)
        state = decay * state + jnp.where(own, ends[b * rows : (b + 1) * rows], 0.0)
    z_hi, z_lo = split2(jnp.concatenate(entering, axis=0))
    lead_hi, lead_lo = split2(lead_table(col, 1, BLOCK))
    far = dot(z_hi, lead_hi) + dot(z_hi, lead_lo) + dot(z_lo, lead_hi)
    member = lax.broadcasted_iota(jnp.int32, (groups, lanes), 0) == (
        lax.broadcasted_iota(jnp.int32, (groups, lanes), 1) // modes
    )
    taps_long = sum(dot(member.astype(bf16), part) for part in split3(lead_table(col, 0, BLOCK)))

    s_idx = lax.broadcasted_iota(jnp.int32, (BLOCK, BLOCK), 0)
    t_idx = lax.broadcasted_iota(jnp.int32, (BLOCK, BLOCK), 1)
    pieces = [[None] * groups for _ in range(count)]
    for g in range(groups):
        lhs = jnp.concatenate(
            [stacked[b * rows + g * width : b * rows + (g + 1) * width] for b in range(count)],
            axis=0,
        )
        row = taps_long[g : g + 1, :]
        toeplitz = pltpu.roll(jnp.broadcast_to(row, (BLOCK, BLOCK)), 0, 1, stride=1, stride_axis=0)
        toeplitz = jnp.where(t_idx >= s_idx, toeplitz, 0.0)
        t_hi, t_lo = split2(toeplitz)
        near = dot(lhs, t_hi) + dot(lhs, t_lo)
        for b in range(count):
            pieces[b][g] = near[b * width : (b + 1) * width]
    long_term = jnp.concatenate(
        [
            jnp.concatenate(pieces[b], axis=0) + far[b * rows : (b + 1) * rows]
            for b in range(count)
        ],
        axis=1,
    )
    signal = product.astype(f32)
    mixed = query.astype(f32) * (long_term + prm[:, skip_at : skip_at + 1] * signal)
    u0_ref[...] = res_ref[...].astype(f32) + mixed


def finish_kernel(width, modes, u0_ref, q_ref, z_ref, col_ref, upd_ref, sq_ref):
    rows, length = u0_ref.shape
    col = col_ref[0]
    lanes = col.shape[0]
    spread = exact_dot(z_ref[...], spread_matrix(lanes, modes))
    own = own_modes(rows, lanes, width, modes)
    z_hi, z_lo = split2(jnp.where(own, spread, 0.0))
    lead_hi, lead_lo = split2(lead_table(col, 1, length))
    far = dot(z_hi, lead_hi) + dot(z_hi, lead_lo) + dot(z_lo, lead_hi)
    updated = u0_ref[...] + q_ref[...].astype(f32) * far
    upd_ref[...] = updated
    sq_ref[0] = jnp.sum(updated * updated, axis=0, keepdims=True)


def local(projections, short_filter, decay_rate, residue, skip, norm_gain, residual):
    channels, length = residual.shape
    groups, modes = decay_rate.shape
    width = channels // groups
    rim_len = short_filter.shape[2] - 1
    count = length // BLOCK
    chunk = 256 if channels % 256 == 0 else channels
    chunk_groups = chunk // width
    lanes = chunk_groups * modes
    steps = channels // chunk

    edge = projections[:, :, length - rim_len :].transpose(0, 2, 1)
    rim = shifted(edge, "ctx", 1)
    prm = jnp.concatenate(
        [
            short_filter.astype(f32).transpose(0, 2, 1).reshape(-1, channels),
            rim.astype(f32).reshape(-1, channels),
            skip[None, :],
        ],
        axis=0,
    )
    prm = jnp.pad(prm, ((0, LANES - prm.shape[0]), (0, 0))).T

    scaled = residue * jnp.sqrt(-jnp.expm1(-2.0 * decay_rate))
    lam = decay_rate.reshape(steps, 1, lanes)
    col = jnp.stack([decay_rate.reshape(steps, lanes), scaled.reshape(steps, lanes)], axis=2)
    col = jnp.pad(col, ((0, 0), (0, 0), (0, LANES - 2)))

    proj_spec = pl.BlockSpec((3, chunk, length), lambda i: (0, i, 0))
    prm_spec = pl.BlockSpec((chunk, LANES), lambda i: (i, 0))
    lam_spec = pl.BlockSpec((1, 1, lanes), lambda i: (i, 0, 0))
    col_spec = pl.BlockSpec((1, lanes, LANES), lambda i: (i, 0, 0))
    row_spec = pl.BlockSpec((chunk, length), lambda i: (i, 0))
    state_spec = pl.BlockSpec((chunk, LANES), lambda i: (i, 0))

    end_state = pl.pallas_call(
        functools.partial(state_kernel, width, modes),
        grid=(steps,),
        in_specs=[proj_spec, prm_spec, lam_spec],
        out_specs=state_spec,
        out_shape=jax.ShapeDtypeStruct((channels, LANES), f32),
    )(projections, prm, lam)

    size = lax.axis_size("ctx")
    dense = end_state[:, :modes].reshape(channels * modes // 128, 128)
    rate = jnp.repeat(decay_rate, width, axis=0).reshape(dense.shape)
    incoming = incoming_state(dense, rate * length, size).reshape(channels, modes)
    incoming = jnp.pad(incoming, ((0, 0), (0, LANES - modes)))

    u0, query = pl.pallas_call(
        functools.partial(local_kernel, width, modes, count),
        grid=(steps,),
        in_specs=[proj_spec, prm_spec, lam_spec, col_spec, row_spec],
        out_specs=[row_spec, row_spec],
        out_shape=[
            jax.ShapeDtypeStruct((channels, length), f32),
            jax.ShapeDtypeStruct((channels, length), bf16),
        ],
    )(projections, prm, lam, col, residual)

    updated, sq = pl.pallas_call(
        functools.partial(finish_kernel, width, modes),
        grid=(steps,),
        in_specs=[row_spec, row_spec, state_spec, col_spec],
        out_specs=[row_spec, pl.BlockSpec((1, 1, length), lambda i: (i, 0, 0))],
        out_shape=[
            jax.ShapeDtypeStruct((channels, length), f32),
            jax.ShapeDtypeStruct((steps, 1, length), f32),
        ],
    )(u0, query, incoming, col)
    squares = lax.psum(jnp.sum(sq, axis=(0, 1)), "tp")
    return (updated * lax.rsqrt(squares / D + epsilon)[None, :] * norm_gain[:, None]).astype(bf16)


def solution(mesh):
    placed = (
        P(None, "tp", "ctx"),
        P(None, "tp", None),
        P("tp", None),
        P("tp", None),
        P("tp"),
        P("tp"),
        P("tp", "ctx"),
    )
    return jax.shard_map(
        local, mesh=mesh, in_specs=placed, out_specs=P("tp", "ctx"), check_vma=False
    )
```

```python
import functools

import jax
import jax.numpy as jnp
from jax import lax
from jax.experimental import pallas as pl
from jax.experimental.pallas import tpu as pltpu
from jax.sharding import PartitionSpec as P

D = 8192
epsilon = 1e-06
BLOCK = 128
LANES = 128
f32 = jnp.float32
bf16 = jnp.bfloat16


def shifted(shard, axis, by):
    size = lax.axis_size(axis)
    pairs = [(i, i + by) for i in range(size) if 0 <= i + by < size]
    return lax.ppermute(shard, axis, pairs)


def incoming_state(ends, span_rate, size):
    place = lax.axis_index("ctx")
    copies = jnp.broadcast_to(ends[None], (size,) + ends.shape)
    gathered = lax.all_to_all(copies, "ctx", 0, 0)
    earlier = jnp.arange(size, dtype=jnp.int32)
    gap = jnp.maximum(place - 1 - earlier, 0).astype(f32)
    weight = jnp.where(
        (earlier < place)[:, None, None],
        jnp.exp(-span_rate[None] * gap[:, None, None]),
        0.0,
    )
    return jnp.sum(weight * gathered, axis=0)


def split2(a):
    hi = a.astype(bf16)
    lo = (a - hi.astype(f32)).astype(bf16)
    return hi, lo


def split3(a):
    hi = a.astype(bf16)
    rest = a - hi.astype(f32)
    mid = rest.astype(bf16)
    lo = (rest - mid.astype(f32)).astype(bf16)
    return hi, mid, lo


def dot(a, b):
    return jnp.dot(a, b, preferred_element_type=f32)


def exact_dot(a, select):
    return sum(dot(part, select) for part in split3(a))


def column(prm, k, rows):
    return jnp.broadcast_to(prm[:, k : k + 1], (rows, LANES))


def featurize(proj_ref, prm, p, taps, rims):
    rows, length = proj_ref.shape[1], proj_ref.shape[2]
    t = taps * p
    weights = [column(prm, t + k, rows) for k in range(3)]
    back2 = column(prm, rims + 2 * p, rows)
    back1 = column(prm, rims + 2 * p + 1, rows)
    lane = lax.broadcasted_iota(jnp.int32, (rows, LANES), 1)
    tiles = [proj_ref[p, :, j * LANES : (j + 1) * LANES].astype(f32) for j in range(length // LANES)]
    once = [pltpu.roll(x, 1, 1) for x in tiles]
    twice = [pltpu.roll(x, 2, 1) for x in tiles]
    out = []
    for j, x in enumerate(tiles):
        if j == 0:
            x1 = jnp.where(lane == 0, back1, once[0])
            x2 = jnp.where(lane == 0, back2, jnp.where(lane == 1, back1, twice[0]))
        else:
            x1 = jnp.where(lane == 0, once[j - 1], once[j])
            x2 = jnp.where(lane < 2, twice[j - 1], twice[j])
        summed = weights[0] * x + weights[1] * x1
        summed = summed + weights[2] * x2
        out.append(summed.astype(bf16))
    return jnp.concatenate(out, axis=1)


def own_modes(rows, lanes, width, modes):
    row = lax.broadcasted_iota(jnp.int32, (rows, lanes), 0) // width
    lane = lax.broadcasted_iota(jnp.int32, (rows, lanes), 1) // modes
    return row == lane


def product_stack(proj_ref, prm, taps, rims, count):
    key = featurize(proj_ref, prm, 1, taps, rims).astype(f32)
    value = featurize(proj_ref, prm, 2, taps, rims).astype(f32)
    product = (key * value).astype(bf16)
    stacked = jnp.concatenate(
        [product[:, b * BLOCK : (b + 1) * BLOCK] for b in range(count)], axis=0
    )
    return product, stacked


def masked_ends(stacked, w_hi_ref, w_lo_ref, rows, width, modes, count):
    ends = dot(stacked, w_hi_ref[0]) + dot(stacked, w_lo_ref[0])
    own = own_modes(rows, ends.shape[1], width, modes)
    return [jnp.where(own, ends[b * rows : (b + 1) * rows], 0.0) for b in range(count)], own


def state_kernel(width, modes, proj_ref, prm_ref, lam_ref, out_ref):
    rows, length = proj_ref.shape[1], proj_ref.shape[2]
    prm = prm_ref[...]
    key = featurize(proj_ref, prm, 1, 3, 9).astype(f32)
    value = featurize(proj_ref, prm, 2, 3, 9).astype(f32)
    product = (key * value).astype(bf16)
    lam = lam_ref[0]
    lanes = lam.shape[1]
    span = (length - 1 - lax.broadcasted_iota(jnp.int32, (length, lanes), 0)).astype(f32)
    w_hi, w_lo = split2(jnp.exp(-lam * span))
    ends = dot(product, w_hi) + dot(product, w_lo)
    own = own_modes(rows, lanes, width, modes)
    out_ref[...] = exact_dot(jnp.where(own, ends, 0.0), select_matrix(lanes, modes))


def select_matrix(lanes, modes):
    mode = lax.broadcasted_iota(jnp.int32, (lanes, LANES), 0) % modes
    lane = lax.broadcasted_iota(jnp.int32, (lanes, LANES), 1)
    return (mode == lane).astype(bf16)


def spread_matrix(lanes, modes):
    lane = lax.broadcasted_iota(jnp.int32, (LANES, lanes), 0)
    mode = lax.broadcasted_iota(jnp.int32, (LANES, lanes), 1) % modes
    return (mode == lane).astype(bf16)


def lead_table(col, first, count):
    lag = (first + lax.broadcasted_iota(jnp.int32, (col.shape[0], count), 1)).astype(f32)
    return col[:, 1:2] * jnp.exp(-col[:, 0:1] * lag)


def local_kernel(
    width,
    modes,
    count,
    proj_ref,
    prm_ref,
    lam_ref,
    col_ref,
    res_ref,
    u0_ref,
    q_ref,
):
    rows = proj_ref.shape[1]
    groups = rows // width
    taps = 3
    rims = 3 * taps
    skip_at = rims + 6
    prm = prm_ref[...]
    query = featurize(proj_ref, prm, 0, taps, rims)
    q_ref[...] = query
    key = featurize(proj_ref, prm, 1, taps, rims).astype(f32)
    value = featurize(proj_ref, prm, 2, taps, rims).astype(f32)
    product = (key * value).astype(bf16)
    stacked = jnp.concatenate(
        [product[:, b * BLOCK : (b + 1) * BLOCK] for b in range(count)], axis=0
    )
    lam = lam_ref[0]
    col = col_ref[0]
    lanes = lam.shape[1]
    span = (BLOCK - 1 - lax.broadcasted_iota(jnp.int32, (BLOCK, lanes), 0)).astype(f32)
    w_hi, w_lo = split2(jnp.exp(-lam * span))
    ends = dot(stacked, w_hi) + dot(stacked, w_lo)
    own = own_modes(rows, lanes, width, modes)
    decay = jnp.exp(-lam * float(BLOCK))
    state = jnp.where(own, ends[0:rows], 0.0)
    entering = [jnp.zeros_like(state)]
    for b in range(1, count):
        entering.append(state)
        state = decay * state + jnp.where(own, ends[b * rows : (b + 1) * rows], 0.0)
    z_hi, z_lo = split2(jnp.concatenate(entering, axis=0))
    lead_hi, lead_lo = split2(lead_table(col, 1, BLOCK))
    far = dot(z_hi, lead_hi) + dot(z_hi, lead_lo) + dot(z_lo, lead_hi)
    member = lax.broadcasted_iota(jnp.int32, (groups, lanes), 0) == (
        lax.broadcasted_iota(jnp.int32, (groups, lanes), 1) // modes
    )
    taps_long = sum(dot(member.astype(bf16), part) for part in split3(lead_table(col, 0, BLOCK)))

    s_idx = lax.broadcasted_iota(jnp.int32, (BLOCK, BLOCK), 0)
    t_idx = lax.broadcasted_iota(jnp.int32, (BLOCK, BLOCK), 1)
    pieces = [[None] * groups for _ in range(count)]
    for g in range(groups):
        lhs = jnp.concatenate(
            [stacked[b * rows + g * width : b * rows + (g + 1) * width] for b in range(count)],
            axis=0,
        )
        row = taps_long[g : g + 1, :]
        toeplitz = pltpu.roll(jnp.broadcast_to(row, (BLOCK, BLOCK)), 0, 1, stride=1, stride_axis=0)
        toeplitz = jnp.where(t_idx >= s_idx, toeplitz, 0.0)
        t_hi, t_lo = split2(toeplitz)
        near = dot(lhs, t_hi) + dot(lhs, t_lo)
        for b in range(count):
            pieces[b][g] = near[b * width : (b + 1) * width]
    long_term = jnp.concatenate(
        [
            jnp.concatenate(pieces[b], axis=0) + far[b * rows : (b + 1) * rows]
            for b in range(count)
        ],
        axis=1,
    )
    signal = product.astype(f32)
    skip_b = jnp.concatenate([column(prm, skip_at, rows)] * (signal.shape[1] // LANES), axis=1)
    mixed = query.astype(f32) * (long_term + skip_b * signal)
    u0_ref[...] = res_ref[...].astype(f32) + mixed


def finish_kernel(width, modes, u0_ref, q_ref, z_ref, col_ref, upd_ref, sq_ref):
    rows, length = u0_ref.shape
    col = col_ref[0]
    lanes = col.shape[0]
    spread = exact_dot(z_ref[...], spread_matrix(lanes, modes))
    own = own_modes(rows, lanes, width, modes)
    z_hi, z_lo = split2(jnp.where(own, spread, 0.0))
    lead_hi, lead_lo = split2(lead_table(col, 1, length))
    far = dot(z_hi, lead_hi) + dot(z_hi, lead_lo) + dot(z_lo, lead_hi)
    updated = u0_ref[...] + q_ref[...].astype(f32) * far
    upd_ref[...] = updated
    sq_ref[0] = jnp.sum(updated * updated, axis=0, keepdims=True)


def local(projections, short_filter, decay_rate, residue, skip, norm_gain, residual):
    channels, length = residual.shape
    groups, modes = decay_rate.shape
    width = channels // groups
    rim_len = short_filter.shape[2] - 1
    count = length // BLOCK
    chunk = 256 if channels % 256 == 0 else channels
    chunk_groups = chunk // width
    lanes = chunk_groups * modes
    steps = channels // chunk

    edge = projections[:, :, length - rim_len :].transpose(0, 2, 1)
    rim = shifted(edge, "ctx", 1)
    prm = jnp.concatenate(
        [
            short_filter.astype(f32).transpose(0, 2, 1).reshape(-1, channels),
            rim.astype(f32).reshape(-1, channels),
            skip[None, :],
        ],
        axis=0,
    )
    prm = jnp.pad(prm, ((0, LANES - prm.shape[0]), (0, 0))).T

    scaled = residue * jnp.sqrt(-jnp.expm1(-2.0 * decay_rate))
    lam = decay_rate.reshape(steps, 1, lanes)
    col = jnp.stack([decay_rate.reshape(steps, lanes), scaled.reshape(steps, lanes)], axis=2)
    col = jnp.pad(col, ((0, 0), (0, 0), (0, LANES - 2)))

    proj_spec = pl.BlockSpec((3, chunk, length), lambda i: (0, i, 0))
    prm_spec = pl.BlockSpec((chunk, LANES), lambda i: (i, 0))
    lam_spec = pl.BlockSpec((1, 1, lanes), lambda i: (i, 0, 0))
    col_spec = pl.BlockSpec((1, lanes, LANES), lambda i: (i, 0, 0))
    row_spec = pl.BlockSpec((chunk, length), lambda i: (i, 0))
    state_spec = pl.BlockSpec((chunk, LANES), lambda i: (i, 0))

    end_state = pl.pallas_call(
        functools.partial(state_kernel, width, modes),
        grid=(steps,),
        in_specs=[proj_spec, prm_spec, lam_spec],
        out_specs=state_spec,
        out_shape=jax.ShapeDtypeStruct((channels, LANES), f32),
    )(projections, prm, lam)

    size = lax.axis_size("ctx")
    dense = end_state[:, :modes].reshape(channels * modes // 128, 128)
    rate = jnp.repeat(decay_rate, width, axis=0).reshape(dense.shape)
    incoming = incoming_state(dense, rate * length, size).reshape(channels, modes)
    incoming = jnp.pad(incoming, ((0, 0), (0, LANES - modes)))

    u0, query = pl.pallas_call(
        functools.partial(local_kernel, width, modes, count),
        grid=(steps,),
        in_specs=[proj_spec, prm_spec, lam_spec, col_spec, row_spec],
        out_specs=[row_spec, row_spec],
        out_shape=[
            jax.ShapeDtypeStruct((channels, length), f32),
            jax.ShapeDtypeStruct((channels, length), bf16),
        ],
    )(projections, prm, lam, col, residual)

    updated, sq = pl.pallas_call(
        functools.partial(finish_kernel, width, modes),
        grid=(steps,),
        in_specs=[row_spec, row_spec, state_spec, col_spec],
        out_specs=[row_spec, pl.BlockSpec((1, 1, length), lambda i: (i, 0, 0))],
        out_shape=[
            jax.ShapeDtypeStruct((channels, length), f32),
            jax.ShapeDtypeStruct((steps, 1, length), f32),
        ],
    )(u0, query, incoming, col)
    squares = lax.psum(jnp.sum(sq, axis=(0, 1)), "tp")
    return (updated * lax.rsqrt(squares / D + epsilon)[None, :] * norm_gain[:, None]).astype(bf16)


def solution(mesh):
    placed = (
        P(None, "tp", "ctx"),
        P(None, "tp", None),
        P("tp", None),
        P("tp", None),
        P("tp"),
        P("tp"),
        P("tp", "ctx"),
    )
    return jax.shard_map(
        local, mesh=mesh, in_specs=placed, out_specs=P("tp", "ctx"), check_vma=False
    )
```

```python
import functools

import jax
import jax.numpy as jnp
from jax import lax
from jax.experimental import pallas as pl
from jax.experimental.pallas import tpu as pltpu
from jax.sharding import PartitionSpec as P

D = 8192
epsilon = 1e-06
BLOCK = 128
LANES = 128
f32 = jnp.float32
bf16 = jnp.bfloat16


def shifted(shard, axis, by):
    size = lax.axis_size(axis)
    pairs = [(i, i + by) for i in range(size) if 0 <= i + by < size]
    return lax.ppermute(shard, axis, pairs)


def incoming_state(ends, span_rate, size):
    place = lax.axis_index("ctx")
    copies = jnp.broadcast_to(ends[None], (size,) + ends.shape)
    gathered = lax.all_to_all(copies, "ctx", 0, 0)
    earlier = jnp.arange(size, dtype=jnp.int32)
    gap = jnp.maximum(place - 1 - earlier, 0).astype(f32)
    weight = jnp.where(
        (earlier < place)[:, None, None],
        jnp.exp(-span_rate[None] * gap[:, None, None]),
        0.0,
    )
    return jnp.sum(weight * gathered, axis=0)


def split2(a):
    hi = a.astype(bf16)
    lo = (a - hi.astype(f32)).astype(bf16)
    return hi, lo


def split3(a):
    hi = a.astype(bf16)
    rest = a - hi.astype(f32)
    mid = rest.astype(bf16)
    lo = (rest - mid.astype(f32)).astype(bf16)
    return hi, mid, lo


def dot(a, b):
    return jnp.dot(a, b, preferred_element_type=f32)


def exact_dot(a, select):
    return sum(dot(part, select) for part in split3(a))


def column(prm, k, rows):
    return jnp.broadcast_to(prm[:, k : k + 1], (rows, LANES))


def featurize(proj_ref, prm, p, taps, rims):
    rows, length = proj_ref.shape[1], proj_ref.shape[2]
    t = taps * p
    weights = [column(prm, t + k, rows) for k in range(3)]
    back2 = column(prm, rims + 2 * p, rows)
    back1 = column(prm, rims + 2 * p + 1, rows)
    lane = lax.broadcasted_iota(jnp.int32, (rows, LANES), 1)
    tiles = [proj_ref[p, :, j * LANES : (j + 1) * LANES].astype(f32) for j in range(length // LANES)]
    once = [pltpu.roll(x, 1, 1) for x in tiles]
    twice = [pltpu.roll(x, 2, 1) for x in tiles]
    out = []
    for j, x in enumerate(tiles):
        if j == 0:
            x1 = jnp.where(lane == 0, back1, once[0])
            x2 = jnp.where(lane == 0, back2, jnp.where(lane == 1, back1, twice[0]))
        else:
            x1 = jnp.where(lane == 0, once[j - 1], once[j])
            x2 = jnp.where(lane < 2, twice[j - 1], twice[j])
        summed = weights[0] * x + weights[1] * x1
        summed = summed + weights[2] * x2
        out.append(summed.astype(bf16))
    return jnp.concatenate(out, axis=1)


def own_modes(rows, lanes, width, modes):
    row = lax.broadcasted_iota(jnp.int32, (rows, lanes), 0) // width
    lane = lax.broadcasted_iota(jnp.int32, (rows, lanes), 1) // modes
    return row == lane


def product_stack(proj_ref, prm, taps, rims, count):
    key = featurize(proj_ref, prm, 1, taps, rims).astype(f32)
    value = featurize(proj_ref, prm, 2, taps, rims).astype(f32)
    product = (key * value).astype(bf16)
    stacked = jnp.concatenate(
        [product[:, b * BLOCK : (b + 1) * BLOCK] for b in range(count)], axis=0
    )
    return product, stacked


def masked_ends(stacked, w_hi_ref, w_lo_ref, rows, width, modes, count):
    ends = dot(stacked, w_hi_ref[0]) + dot(stacked, w_lo_ref[0])
    own = own_modes(rows, ends.shape[1], width, modes)
    return [jnp.where(own, ends[b * rows : (b + 1) * rows], 0.0) for b in range(count)], own


def featurize_rows(proj_ref, prm, p, taps, rims, rows):
    return featurize(proj_ref.at[:, rows, :], prm, p, taps, rims)


def state_kernel(width, modes, part, proj_ref, prm_ref, lam_ref, out_ref, w_hi_ref, w_lo_ref):
    rows, length = proj_ref.shape[1], proj_ref.shape[2]
    lam = lam_ref[0]
    lanes = lam.shape[1]
    span = (length - 1 - lax.broadcasted_iota(jnp.int32, (length, lanes), 0)).astype(f32)
    w_hi, w_lo = split2(jnp.exp(-lam * span))
    w_hi_ref[...] = w_hi
    w_lo_ref[...] = w_lo
    select = select_matrix(lanes, modes)

    def body(r, carry):
        at = pl.ds(pl.multiple_of(r * part, part), part)
        prm = prm_ref[at, :]
        key = featurize_rows(proj_ref, prm, 1, 3, 9, at).astype(f32)
        value = featurize_rows(proj_ref, prm, 2, 3, 9, at).astype(f32)
        product = (key * value).astype(bf16)
        ends = dot(product, w_hi_ref[...]) + dot(product, w_lo_ref[...])
        row = r * part + lax.broadcasted_iota(jnp.int32, (part, lanes), 0)
        own = (row // width) == (lax.broadcasted_iota(jnp.int32, (part, lanes), 1) // modes)
        out_ref[at, :] = exact_dot(jnp.where(own, ends, 0.0), select)
        return carry

    lax.fori_loop(0, rows // part, body, 0)


def select_matrix(lanes, modes):
    mode = lax.broadcasted_iota(jnp.int32, (lanes, LANES), 0) % modes
    lane = lax.broadcasted_iota(jnp.int32, (lanes, LANES), 1)
    return (mode == lane).astype(bf16)


def spread_matrix(lanes, modes):
    lane = lax.broadcasted_iota(jnp.int32, (LANES, lanes), 0)
    mode = lax.broadcasted_iota(jnp.int32, (LANES, lanes), 1) % modes
    return (mode == lane).astype(bf16)


def lead_table(col, first, count):
    lag = (first + lax.broadcasted_iota(jnp.int32, (col.shape[0], count), 1)).astype(f32)
    return col[:, 1:2] * jnp.exp(-col[:, 0:1] * lag)


def local_kernel(
    width,
    modes,
    count,
    proj_ref,
    prm_ref,
    lam_ref,
    col_ref,
    res_ref,
    u0_ref,
    q_ref,
):
    rows = proj_ref.shape[1]
    groups = rows // width
    taps = 3
    rims = 3 * taps
    skip_at = rims + 6
    prm = prm_ref[...]
    query = featurize(proj_ref, prm, 0, taps, rims)
    q_ref[...] = query
    key = featurize(proj_ref, prm, 1, taps, rims).astype(f32)
    value = featurize(proj_ref, prm, 2, taps, rims).astype(f32)
    product = (key * value).astype(bf16)
    stacked = jnp.concatenate(
        [product[:, b * BLOCK : (b + 1) * BLOCK] for b in range(count)], axis=0
    )
    lam = lam_ref[0]
    col = col_ref[0]
    lanes = lam.shape[1]
    span = (BLOCK - 1 - lax.broadcasted_iota(jnp.int32, (BLOCK, lanes), 0)).astype(f32)
    w_hi, w_lo = split2(jnp.exp(-lam * span))
    ends = dot(stacked, w_hi) + dot(stacked, w_lo)
    own = own_modes(rows, lanes, width, modes)
    decay = jnp.exp(-lam * float(BLOCK))
    state = jnp.where(own, ends[0:rows], 0.0)
    entering = [jnp.zeros_like(state)]
    for b in range(1, count):
        entering.append(state)
        state = decay * state + jnp.where(own, ends[b * rows : (b + 1) * rows], 0.0)
    z_hi, z_lo = split2(jnp.concatenate(entering, axis=0))
    lead_hi, lead_lo = split2(lead_table(col, 1, BLOCK))
    far = dot(z_hi, lead_hi) + dot(z_hi, lead_lo) + dot(z_lo, lead_hi)
    member = lax.broadcasted_iota(jnp.int32, (groups, lanes), 0) == (
        lax.broadcasted_iota(jnp.int32, (groups, lanes), 1) // modes
    )
    taps_long = sum(dot(member.astype(bf16), part) for part in split3(lead_table(col, 0, BLOCK)))

    s_idx = lax.broadcasted_iota(jnp.int32, (BLOCK, BLOCK), 0)
    t_idx = lax.broadcasted_iota(jnp.int32, (BLOCK, BLOCK), 1)
    pieces = [[None] * groups for _ in range(count)]
    for g in range(groups):
        lhs = jnp.concatenate(
            [stacked[b * rows + g * width : b * rows + (g + 1) * width] for b in range(count)],
            axis=0,
        )
        row = taps_long[g : g + 1, :]
        toeplitz = pltpu.roll(jnp.broadcast_to(row, (BLOCK, BLOCK)), 0, 1, stride=1, stride_axis=0)
        toeplitz = jnp.where(t_idx >= s_idx, toeplitz, 0.0)
        t_hi, t_lo = split2(toeplitz)
        near = dot(lhs, t_hi) + dot(lhs, t_lo)
        for b in range(count):
            pieces[b][g] = near[b * width : (b + 1) * width]
    long_term = jnp.concatenate(
        [
            jnp.concatenate(pieces[b], axis=0) + far[b * rows : (b + 1) * rows]
            for b in range(count)
        ],
        axis=1,
    )
    signal = product.astype(f32)
    skip_b = jnp.concatenate([column(prm, skip_at, rows)] * (signal.shape[1] // LANES), axis=1)
    mixed = query.astype(f32) * (long_term + skip_b * signal)
    u0_ref[...] = res_ref[...].astype(f32) + mixed


def finish_kernel(width, modes, u0_ref, q_ref, z_ref, col_ref, upd_ref, sq_ref):
    rows, length = u0_ref.shape
    col = col_ref[0]
    lanes = col.shape[0]
    spread = exact_dot(z_ref[...], spread_matrix(lanes, modes))
    own = own_modes(rows, lanes, width, modes)
    z_hi, z_lo = split2(jnp.where(own, spread, 0.0))
    lead_hi, lead_lo = split2(lead_table(col, 1, length))
    far = dot(z_hi, lead_hi) + dot(z_hi, lead_lo) + dot(z_lo, lead_hi)
    updated = u0_ref[...] + q_ref[...].astype(f32) * far
    upd_ref[...] = updated
    sq_ref[0] = jnp.sum(updated * updated, axis=0, keepdims=True)


def local(projections, short_filter, decay_rate, residue, skip, norm_gain, residual):
    channels, length = residual.shape
    groups, modes = decay_rate.shape
    width = channels // groups
    rim_len = short_filter.shape[2] - 1
    count = length // BLOCK
    chunk = 256 if channels % 256 == 0 else channels
    chunk_groups = chunk // width
    lanes = chunk_groups * modes
    steps = channels // chunk

    edge = projections[:, :, length - rim_len :].transpose(0, 2, 1)
    rim = shifted(edge, "ctx", 1)
    prm = jnp.concatenate(
        [
            short_filter.astype(f32).transpose(0, 2, 1).reshape(-1, channels),
            rim.astype(f32).reshape(-1, channels),
            skip[None, :],
        ],
        axis=0,
    )
    prm = jnp.pad(prm, ((0, LANES - prm.shape[0]), (0, 0))).T

    scaled = residue * jnp.sqrt(-jnp.expm1(-2.0 * decay_rate))
    lam = decay_rate.reshape(steps, 1, lanes)
    col = jnp.stack([decay_rate.reshape(steps, lanes), scaled.reshape(steps, lanes)], axis=2)
    col = jnp.pad(col, ((0, 0), (0, 0), (0, LANES - 2)))

    proj_spec = pl.BlockSpec((3, chunk, length), lambda i: (0, i, 0))
    prm_spec = pl.BlockSpec((chunk, LANES), lambda i: (i, 0))
    lam_spec = pl.BlockSpec((1, 1, lanes), lambda i: (i, 0, 0))
    col_spec = pl.BlockSpec((1, lanes, LANES), lambda i: (i, 0, 0))
    row_spec = pl.BlockSpec((chunk, length), lambda i: (i, 0))
    state_spec = pl.BlockSpec((chunk, LANES), lambda i: (i, 0))

    end_state = pl.pallas_call(
        functools.partial(state_kernel, width, modes, 64),
        grid=(steps,),
        in_specs=[proj_spec, prm_spec, lam_spec],
        out_specs=state_spec,
        out_shape=jax.ShapeDtypeStruct((channels, LANES), f32),
        scratch_shapes=[pltpu.VMEM((length, lanes), bf16), pltpu.VMEM((length, lanes), bf16)],
    )(projections, prm, lam)

    size = lax.axis_size("ctx")
    dense = end_state[:, :modes].reshape(channels * modes // 128, 128)
    rate = jnp.repeat(decay_rate, width, axis=0).reshape(dense.shape)
    incoming = incoming_state(dense, rate * length, size).reshape(channels, modes)
    incoming = jnp.pad(incoming, ((0, 0), (0, LANES - modes)))

    u0, query = pl.pallas_call(
        functools.partial(local_kernel, width, modes, count),
        grid=(steps,),
        in_specs=[proj_spec, prm_spec, lam_spec, col_spec, row_spec],
        out_specs=[row_spec, row_spec],
        out_shape=[
            jax.ShapeDtypeStruct((channels, length), f32),
            jax.ShapeDtypeStruct((channels, length), bf16),
        ],
    )(projections, prm, lam, col, residual)

    updated, sq = pl.pallas_call(
        functools.partial(finish_kernel, width, modes),
        grid=(steps,),
        in_specs=[row_spec, row_spec, state_spec, col_spec],
        out_specs=[row_spec, pl.BlockSpec((1, 1, length), lambda i: (i, 0, 0))],
        out_shape=[
            jax.ShapeDtypeStruct((channels, length), f32),
            jax.ShapeDtypeStruct((steps, 1, length), f32),
        ],
    )(u0, query, incoming, col)
    squares = lax.psum(jnp.sum(sq, axis=(0, 1)), "tp")
    return (updated * lax.rsqrt(squares / D + epsilon)[None, :] * norm_gain[:, None]).astype(bf16)


def solution(mesh):
    placed = (
        P(None, "tp", "ctx"),
        P(None, "tp", None),
        P("tp", None),
        P("tp", None),
        P("tp"),
        P("tp"),
        P("tp", "ctx"),
    )
    return jax.shard_map(
        local, mesh=mesh, in_specs=placed, out_specs=P("tp", "ctx"), check_vma=False
    )
```

```python
import functools

import jax
import jax.numpy as jnp
from jax import lax
from jax.experimental import pallas as pl
from jax.experimental.pallas import tpu as pltpu
from jax.sharding import PartitionSpec as P

D = 8192
epsilon = 1e-06
BLOCK = 128
LANES = 128
f32 = jnp.float32
bf16 = jnp.bfloat16


def shifted(shard, axis, by):
    size = lax.axis_size(axis)
    pairs = [(i, i + by) for i in range(size) if 0 <= i + by < size]
    return lax.ppermute(shard, axis, pairs)


def incoming_state(ends, span_rate, size):
    place = lax.axis_index("ctx")
    copies = jnp.broadcast_to(ends[None], (size,) + ends.shape)
    gathered = lax.all_to_all(copies, "ctx", 0, 0)
    earlier = jnp.arange(size, dtype=jnp.int32)
    gap = jnp.maximum(place - 1 - earlier, 0).astype(f32)
    weight = jnp.where(
        (earlier < place)[:, None, None],
        jnp.exp(-span_rate[None] * gap[:, None, None]),
        0.0,
    )
    return jnp.sum(weight * gathered, axis=0)


def split2(a):
    hi = a.astype(bf16)
    lo = (a - hi.astype(f32)).astype(bf16)
    return hi, lo


def split3(a):
    hi = a.astype(bf16)
    rest = a - hi.astype(f32)
    mid = rest.astype(bf16)
    lo = (rest - mid.astype(f32)).astype(bf16)
    return hi, mid, lo


def dot(a, b):
    return jnp.dot(a, b, preferred_element_type=f32)


def exact_dot(a, select):
    return sum(dot(part, select) for part in split3(a))


def column(prm, k, rows):
    return jnp.broadcast_to(prm[:, k : k + 1], (rows, LANES))


def featurize(proj_ref, prm, p, taps, rims):
    rows, length = proj_ref.shape[1], proj_ref.shape[2]
    t = taps * p
    weights = [column(prm, t + k, rows) for k in range(3)]
    back2 = column(prm, rims + 2 * p, rows)
    back1 = column(prm, rims + 2 * p + 1, rows)
    lane = lax.broadcasted_iota(jnp.int32, (rows, LANES), 1)
    tiles = [proj_ref[p, :, j * LANES : (j + 1) * LANES].astype(f32) for j in range(length // LANES)]
    once = [pltpu.roll(x, 1, 1) for x in tiles]
    twice = [pltpu.roll(x, 2, 1) for x in tiles]
    out = []
    for j, x in enumerate(tiles):
        if j == 0:
            x1 = jnp.where(lane == 0, back1, once[0])
            x2 = jnp.where(lane == 0, back2, jnp.where(lane == 1, back1, twice[0]))
        else:
            x1 = jnp.where(lane == 0, once[j - 1], once[j])
            x2 = jnp.where(lane < 2, twice[j - 1], twice[j])
        summed = weights[0] * x + weights[1] * x1
        summed = summed + weights[2] * x2
        out.append(summed.astype(bf16))
    return jnp.concatenate(out, axis=1)


def own_modes(rows, lanes, width, modes):
    row = lax.broadcasted_iota(jnp.int32, (rows, lanes), 0) // width
    lane = lax.broadcasted_iota(jnp.int32, (rows, lanes), 1) // modes
    return row == lane


def product_stack(proj_ref, prm, taps, rims, count):
    key = featurize(proj_ref, prm, 1, taps, rims).astype(f32)
    value = featurize(proj_ref, prm, 2, taps, rims).astype(f32)
    product = (key * value).astype(bf16)
    stacked = jnp.concatenate(
        [product[:, b * BLOCK : (b + 1) * BLOCK] for b in range(count)], axis=0
    )
    return product, stacked


def masked_ends(stacked, w_hi_ref, w_lo_ref, rows, width, modes, count):
    ends = dot(stacked, w_hi_ref[0]) + dot(stacked, w_lo_ref[0])
    own = own_modes(rows, ends.shape[1], width, modes)
    return [jnp.where(own, ends[b * rows : (b + 1) * rows], 0.0) for b in range(count)], own


def state_kernel(width, modes, proj_ref, prm_ref, lam_ref, out_ref):
    rows, length = proj_ref.shape[1], proj_ref.shape[2]
    prm = prm_ref[...]
    key = featurize(proj_ref, prm, 1, 3, 9).astype(f32)
    value = featurize(proj_ref, prm, 2, 3, 9).astype(f32)
    product = (key * value).astype(bf16)
    lam = lam_ref[0]
    lanes = lam.shape[1]
    span = (length - 1 - lax.broadcasted_iota(jnp.int32, (length, lanes), 0)).astype(f32)
    w_hi, w_lo = split2(jnp.exp(-lam * span))
    ends = dot(product, w_hi) + dot(product, w_lo)
    own = own_modes(rows, lanes, width, modes)
    out_ref[...] = exact_dot(jnp.where(own, ends, 0.0), select_matrix(lanes, modes))


def select_matrix(lanes, modes):
    mode = lax.broadcasted_iota(jnp.int32, (lanes, LANES), 0) % modes
    lane = lax.broadcasted_iota(jnp.int32, (lanes, LANES), 1)
    return (mode == lane).astype(bf16)


def spread_matrix(lanes, modes):
    lane = lax.broadcasted_iota(jnp.int32, (LANES, lanes), 0)
    mode = lax.broadcasted_iota(jnp.int32, (LANES, lanes), 1) % modes
    return (mode == lane).astype(bf16)


def lead_table(col, first, count):
    lag = (first + lax.broadcasted_iota(jnp.int32, (col.shape[0], count), 1)).astype(f32)
    return col[:, 1:2] * jnp.exp(-col[:, 0:1] * lag)


def local_kernel(
    width,
    modes,
    count,
    proj_ref,
    prm_ref,
    lam_ref,
    col_ref,
    res_ref,
    u0_ref,
    q_ref,
):
    rows = proj_ref.shape[1]
    groups = rows // width
    taps = 3
    rims = 3 * taps
    skip_at = rims + 6
    prm = prm_ref[...]
    query = featurize(proj_ref, prm, 0, taps, rims)
    q_ref[...] = query
    key = featurize(proj_ref, prm, 1, taps, rims).astype(f32)
    value = featurize(proj_ref, prm, 2, taps, rims).astype(f32)
    product = (key * value).astype(bf16)
    stacked = jnp.concatenate(
        [product[:, b * BLOCK : (b + 1) * BLOCK] for b in range(count)], axis=0
    )
    lam = lam_ref[0]
    col = col_ref[0]
    lanes = lam.shape[1]
    span = (BLOCK - 1 - lax.broadcasted_iota(jnp.int32, (BLOCK, lanes), 0)).astype(f32)
    w_hi, w_lo = split2(jnp.exp(-lam * span))
    used = stacked[: (count - 1) * rows]
    ends = dot(used, w_hi) + dot(used, w_lo)
    own = own_modes(rows, lanes, width, modes)
    decay = jnp.exp(-lam * float(BLOCK))
    state = jnp.where(own, ends[0:rows], 0.0)
    entering = [state]
    for b in range(1, count - 1):
        state = decay * state + jnp.where(own, ends[b * rows : (b + 1) * rows], 0.0)
        entering.append(state)
    z_hi, z_lo = split2(jnp.concatenate(entering, axis=0))
    lead_hi, lead_lo = split2(lead_table(col, 1, BLOCK))
    far = dot(z_hi, lead_hi) + dot(z_hi, lead_lo) + dot(z_lo, lead_hi)
    member = lax.broadcasted_iota(jnp.int32, (groups, lanes), 0) == (
        lax.broadcasted_iota(jnp.int32, (groups, lanes), 1) // modes
    )
    taps_long = sum(dot(member.astype(bf16), part) for part in split3(lead_table(col, 0, BLOCK)))

    s_idx = lax.broadcasted_iota(jnp.int32, (BLOCK, BLOCK), 0)
    t_idx = lax.broadcasted_iota(jnp.int32, (BLOCK, BLOCK), 1)
    pieces = [[None] * groups for _ in range(count)]
    for g in range(groups):
        lhs = jnp.concatenate(
            [stacked[b * rows + g * width : b * rows + (g + 1) * width] for b in range(count)],
            axis=0,
        )
        row = taps_long[g : g + 1, :]
        toeplitz = pltpu.roll(jnp.broadcast_to(row, (BLOCK, BLOCK)), 0, 1, stride=1, stride_axis=0)
        toeplitz = jnp.where(t_idx >= s_idx, toeplitz, 0.0)
        t_hi, t_lo = split2(toeplitz)
        near = dot(lhs, t_hi) + dot(lhs, t_lo)
        for b in range(count):
            pieces[b][g] = near[b * width : (b + 1) * width]
    long_term = jnp.concatenate(
        [
            jnp.concatenate(pieces[b], axis=0) + (far[(b - 1) * rows : b * rows] if b else 0.0)
            for b in range(count)
        ],
        axis=1,
    )
    signal = product.astype(f32)
    skip_b = jnp.concatenate([column(prm, skip_at, rows)] * (signal.shape[1] // LANES), axis=1)
    mixed = query.astype(f32) * (long_term + skip_b * signal)
    u0_ref[...] = res_ref[...].astype(f32) + mixed


def finish_kernel(width, modes, u0_ref, q_ref, z_ref, col_ref, upd_ref, sq_ref):
    rows, length = u0_ref.shape
    col = col_ref[0]
    lanes = col.shape[0]
    spread = exact_dot(z_ref[...], spread_matrix(lanes, modes))
    own = own_modes(rows, lanes, width, modes)
    z_hi, z_lo = split2(jnp.where(own, spread, 0.0))
    lead_hi, lead_lo = split2(lead_table(col, 1, length))
    far = dot(z_hi, lead_hi) + dot(z_hi, lead_lo) + dot(z_lo, lead_hi)
    updated = u0_ref[...] + q_ref[...].astype(f32) * far
    upd_ref[...] = updated
    sq_ref[0] = jnp.sum(updated * updated, axis=0, keepdims=True)


def norm_kernel(upd_ref, scale_ref, gain_ref, out_ref):
    out_ref[...] = (upd_ref[...] * scale_ref[...] * gain_ref[...]).astype(bf16)


def local(projections, short_filter, decay_rate, residue, skip, norm_gain, residual):
    channels, length = residual.shape
    groups, modes = decay_rate.shape
    width = channels // groups
    rim_len = short_filter.shape[2] - 1
    count = length // BLOCK
    chunk = 256 if channels % 256 == 0 else channels
    chunk_groups = chunk // width
    lanes = chunk_groups * modes
    steps = channels // chunk

    edge = projections[:, :, length - rim_len :].transpose(0, 2, 1)
    rim = shifted(edge, "ctx", 1)
    prm = jnp.concatenate(
        [
            short_filter.astype(f32).transpose(0, 2, 1).reshape(-1, channels),
            rim.astype(f32).reshape(-1, channels),
            skip[None, :],
        ],
        axis=0,
    )
    prm = jnp.pad(prm, ((0, LANES - prm.shape[0]), (0, 0))).T

    scaled = residue * jnp.sqrt(-jnp.expm1(-2.0 * decay_rate))
    lam = decay_rate.reshape(steps, 1, lanes)
    col = jnp.stack([decay_rate.reshape(steps, lanes), scaled.reshape(steps, lanes)], axis=2)
    col = jnp.pad(col, ((0, 0), (0, 0), (0, LANES - 2)))

    proj_spec = pl.BlockSpec((3, chunk, length), lambda i: (0, i, 0))
    prm_spec = pl.BlockSpec((chunk, LANES), lambda i: (i, 0))
    lam_spec = pl.BlockSpec((1, 1, lanes), lambda i: (i, 0, 0))
    col_spec = pl.BlockSpec((1, lanes, LANES), lambda i: (i, 0, 0))
    row_spec = pl.BlockSpec((chunk, length), lambda i: (i, 0))
    state_spec = pl.BlockSpec((chunk, LANES), lambda i: (i, 0))

    end_state = pl.pallas_call(
        functools.partial(state_kernel, width, modes),
        grid=(steps,),
        in_specs=[proj_spec, prm_spec, lam_spec],
        out_specs=state_spec,
        out_shape=jax.ShapeDtypeStruct((channels, LANES), f32),
    )(projections, prm, lam)

    size = lax.axis_size("ctx")
    dense = end_state[:, :modes].reshape(channels * modes // 128, 128)
    rate = jnp.repeat(decay_rate, width, axis=0).reshape(dense.shape)
    incoming = incoming_state(dense, rate * length, size).reshape(channels, modes)
    incoming = jnp.pad(incoming, ((0, 0), (0, LANES - modes)))

    u0, query = pl.pallas_call(
        functools.partial(local_kernel, width, modes, count),
        grid=(steps,),
        in_specs=[proj_spec, prm_spec, lam_spec, col_spec, row_spec],
        out_specs=[row_spec, row_spec],
        out_shape=[
            jax.ShapeDtypeStruct((channels, length), f32),
            jax.ShapeDtypeStruct((channels, length), bf16),
        ],
    )(projections, prm, lam, col, residual)

    updated, sq = pl.pallas_call(
        functools.partial(finish_kernel, width, modes),
        grid=(steps,),
        in_specs=[row_spec, row_spec, state_spec, col_spec],
        out_specs=[row_spec, pl.BlockSpec((1, 1, length), lambda i: (i, 0, 0))],
        out_shape=[
            jax.ShapeDtypeStruct((channels, length), f32),
            jax.ShapeDtypeStruct((steps, 1, length), f32),
        ],
    )(u0, query, incoming, col)
    squares = lax.psum(jnp.sum(sq, axis=(0, 1)), "tp")
    scale = lax.rsqrt(squares / D + epsilon)[None, :]
    return pl.pallas_call(
        norm_kernel,
        grid=(steps,),
        in_specs=[
            row_spec,
            pl.BlockSpec((1, length), lambda i: (0, 0)),
            pl.BlockSpec((chunk, 1), lambda i: (i, 0)),
        ],
        out_specs=row_spec,
        out_shape=jax.ShapeDtypeStruct((channels, length), bf16),
    )(updated, scale, norm_gain[:, None])


def solution(mesh):
    placed = (
        P(None, "tp", "ctx"),
        P(None, "tp", None),
        P("tp", None),
        P("tp", None),
        P("tp"),
        P("tp"),
        P("tp", "ctx"),
    )
    return jax.shard_map(
        local, mesh=mesh, in_specs=placed, out_specs=P("tp", "ctx"), check_vma=False
    )
```

```python
import functools

import jax
import jax.numpy as jnp
from jax import lax
from jax.experimental import pallas as pl
from jax.experimental.pallas import tpu as pltpu
from jax.sharding import PartitionSpec as P

D = 8192
epsilon = 1e-06
BLOCK = 128
LANES = 128
f32 = jnp.float32
bf16 = jnp.bfloat16


def shifted(shard, axis, by):
    size = lax.axis_size(axis)
    pairs = [(i, i + by) for i in range(size) if 0 <= i + by < size]
    return lax.ppermute(shard, axis, pairs)


def incoming_state(ends, span_rate, size):
    place = lax.axis_index("ctx")
    copies = jnp.broadcast_to(ends[None], (size,) + ends.shape)
    gathered = lax.all_to_all(copies, "ctx", 0, 0)
    earlier = jnp.arange(size, dtype=jnp.int32)
    gap = jnp.maximum(place - 1 - earlier, 0).astype(f32)
    weight = jnp.where(
        (earlier < place)[:, None, None],
        jnp.exp(-span_rate[None] * gap[:, None, None]),
        0.0,
    )
    return jnp.sum(weight * gathered, axis=0)


def split2(a):
    hi = a.astype(bf16)
    lo = (a - hi.astype(f32)).astype(bf16)
    return hi, lo


def split3(a):
    hi = a.astype(bf16)
    rest = a - hi.astype(f32)
    mid = rest.astype(bf16)
    lo = (rest - mid.astype(f32)).astype(bf16)
    return hi, mid, lo


def dot(a, b):
    return jnp.dot(a, b, preferred_element_type=f32)


def exact_dot(a, select):
    return sum(dot(part, select) for part in split3(a))


def column(prm, k, rows):
    return jnp.broadcast_to(prm[:, k : k + 1], (rows, LANES))


def featurize(proj_ref, prm, p, taps, rims):
    rows, length = proj_ref.shape[1], proj_ref.shape[2]
    t = taps * p
    weights = [column(prm, t + k, rows) for k in range(3)]
    back2 = column(prm, rims + 2 * p, rows)
    back1 = column(prm, rims + 2 * p + 1, rows)
    lane = lax.broadcasted_iota(jnp.int32, (rows, LANES), 1)
    tiles = [proj_ref[p, :, j * LANES : (j + 1) * LANES].astype(f32) for j in range(length // LANES)]
    once = [pltpu.roll(x, 1, 1) for x in tiles]
    twice = [pltpu.roll(x, 2, 1) for x in tiles]
    out = []
    for j, x in enumerate(tiles):
        if j == 0:
            x1 = jnp.where(lane == 0, back1, once[0])
            x2 = jnp.where(lane == 0, back2, jnp.where(lane == 1, back1, twice[0]))
        else:
            x1 = jnp.where(lane == 0, once[j - 1], once[j])
            x2 = jnp.where(lane < 2, twice[j - 1], twice[j])
        summed = weights[0] * x + weights[1] * x1
        summed = summed + weights[2] * x2
        out.append(summed.astype(bf16))
    return jnp.concatenate(out, axis=1)


def own_modes(rows, lanes, width, modes):
    row = lax.broadcasted_iota(jnp.int32, (rows, lanes), 0) // width
    lane = lax.broadcasted_iota(jnp.int32, (rows, lanes), 1) // modes
    return row == lane


def product_stack(proj_ref, prm, taps, rims, count):
    key = featurize(proj_ref, prm, 1, taps, rims).astype(f32)
    value = featurize(proj_ref, prm, 2, taps, rims).astype(f32)
    product = (key * value).astype(bf16)
    stacked = jnp.concatenate(
        [product[:, b * BLOCK : (b + 1) * BLOCK] for b in range(count)], axis=0
    )
    return product, stacked


def masked_ends(stacked, w_hi_ref, w_lo_ref, rows, width, modes, count):
    ends = dot(stacked, w_hi_ref[0]) + dot(stacked, w_lo_ref[0])
    own = own_modes(rows, ends.shape[1], width, modes)
    return [jnp.where(own, ends[b * rows : (b + 1) * rows], 0.0) for b in range(count)], own


def state_kernel(width, modes, proj_ref, prm_ref, lam_ref, out_ref):
    rows, length = proj_ref.shape[1], proj_ref.shape[2]
    prm = prm_ref[...]
    key = featurize(proj_ref, prm, 1, 3, 9).astype(f32)
    value = featurize(proj_ref, prm, 2, 3, 9).astype(f32)
    product = (key * value).astype(bf16)
    lam = lam_ref[0]
    lanes = lam.shape[1]
    span = (length - 1 - lax.broadcasted_iota(jnp.int32, (length, lanes), 0)).astype(f32)
    w_hi, w_lo = split2(jnp.exp(-lam * span))
    ends = dot(product, w_hi) + dot(product, w_lo)
    own = own_modes(rows, lanes, width, modes)
    out_ref[...] = exact_dot(jnp.where(own, ends, 0.0), select_matrix(lanes, modes))


def select_matrix(lanes, modes):
    mode = lax.broadcasted_iota(jnp.int32, (lanes, LANES), 0) % modes
    lane = lax.broadcasted_iota(jnp.int32, (lanes, LANES), 1)
    return (mode == lane).astype(bf16)


def spread_matrix(lanes, modes):
    lane = lax.broadcasted_iota(jnp.int32, (LANES, lanes), 0)
    mode = lax.broadcasted_iota(jnp.int32, (LANES, lanes), 1) % modes
    return (mode == lane).astype(bf16)


def lead_table(col, first, count):
    lag = (first + lax.broadcasted_iota(jnp.int32, (col.shape[0], count), 1)).astype(f32)
    return col[:, 1:2] * jnp.exp(-col[:, 0:1] * lag)


def local_kernel(
    width,
    modes,
    count,
    proj_ref,
    prm_ref,
    lam_ref,
    col_ref,
    res_ref,
    u0_ref,
    q_ref,
):
    rows = proj_ref.shape[1]
    groups = rows // width
    taps = 3
    rims = 3 * taps
    skip_at = rims + 6
    prm = prm_ref[...]
    query = featurize(proj_ref, prm, 0, taps, rims)
    q_ref[...] = query
    key = featurize(proj_ref, prm, 1, taps, rims).astype(f32)
    value = featurize(proj_ref, prm, 2, taps, rims).astype(f32)
    product = (key * value).astype(bf16)
    stacked = jnp.concatenate(
        [product[:, b * BLOCK : (b + 1) * BLOCK] for b in range(count)], axis=0
    )
    lam = lam_ref[0]
    col = col_ref[0]
    lanes = lam.shape[1]
    span = (BLOCK - 1 - lax.broadcasted_iota(jnp.int32, (BLOCK, lanes), 0)).astype(f32)
    w_hi, w_lo = split2(jnp.exp(-lam * span))
    used = stacked[: (count - 1) * rows]
    ends = dot(used, w_hi) + dot(used, w_lo)
    own = own_modes(rows, lanes, width, modes)
    decay = jnp.exp(-lam * float(BLOCK))
    state = jnp.where(own, ends[0:rows], 0.0)
    entering = [state]
    for b in range(1, count - 1):
        state = decay * state + jnp.where(own, ends[b * rows : (b + 1) * rows], 0.0)
        entering.append(state)
    z_hi, z_lo = split2(jnp.concatenate(entering, axis=0))
    lead_hi, lead_lo = split2(lead_table(col, 1, BLOCK))
    far = dot(z_hi, lead_hi) + dot(z_hi, lead_lo) + dot(z_lo, lead_hi)
    member = lax.broadcasted_iota(jnp.int32, (groups, lanes), 0) == (
        lax.broadcasted_iota(jnp.int32, (groups, lanes), 1) // modes
    )
    taps_long = sum(dot(member.astype(bf16), part) for part in split3(lead_table(col, 0, BLOCK)))

    s_idx = lax.broadcasted_iota(jnp.int32, (BLOCK, BLOCK), 0)
    t_idx = lax.broadcasted_iota(jnp.int32, (BLOCK, BLOCK), 1)
    pieces = [[None] * groups for _ in range(count)]
    for g in range(groups):
        lhs = jnp.concatenate(
            [stacked[b * rows + g * width : b * rows + (g + 1) * width] for b in range(count)],
            axis=0,
        )
        row = taps_long[g : g + 1, :]
        toeplitz = pltpu.roll(jnp.broadcast_to(row, (BLOCK, BLOCK)), 0, 1, stride=1, stride_axis=0)
        toeplitz = jnp.where(t_idx >= s_idx, toeplitz, 0.0)
        t_hi, t_lo = split2(toeplitz)
        near = dot(lhs, t_hi) + dot(lhs, t_lo)
        for b in range(count):
            pieces[b][g] = near[b * width : (b + 1) * width]
    long_term = jnp.concatenate(
        [
            jnp.concatenate(pieces[b], axis=0) + (far[(b - 1) * rows : b * rows] if b else 0.0)
            for b in range(count)
        ],
        axis=1,
    )
    signal = product.astype(f32)
    skip_b = jnp.concatenate([column(prm, skip_at, rows)] * (signal.shape[1] // LANES), axis=1)
    mixed = query.astype(f32) * (long_term + skip_b * signal)
    u0_ref[...] = res_ref[...].astype(f32) + mixed


def finish_kernel(width, modes, u0_ref, q_ref, z_ref, col_ref, upd_ref, sq_ref):
    rows, length = u0_ref.shape
    col = col_ref[0]
    lanes = col.shape[0]
    spread = exact_dot(z_ref[...], spread_matrix(lanes, modes))
    own = own_modes(rows, lanes, width, modes)
    z_hi, z_lo = split2(jnp.where(own, spread, 0.0))
    lead_hi, lead_lo = split2(lead_table(col, 1, length))
    far = dot(z_hi, lead_hi) + dot(z_hi, lead_lo) + dot(z_lo, lead_hi)
    updated = u0_ref[...] + q_ref[...].astype(f32) * far
    upd_ref[...] = updated
    sq_ref[0] = jnp.sum(updated * updated, axis=0, keepdims=True)


def local(projections, short_filter, decay_rate, residue, skip, norm_gain, residual):
    channels, length = residual.shape
    groups, modes = decay_rate.shape
    width = channels // groups
    rim_len = short_filter.shape[2] - 1
    count = length // BLOCK
    chunk = 256 if channels % 256 == 0 else channels
    chunk_groups = chunk // width
    lanes = chunk_groups * modes
    steps = channels // chunk

    edge = projections[:, :, length - rim_len :].transpose(0, 2, 1)
    rim = shifted(edge, "ctx", 1)
    prm = jnp.concatenate(
        [
            short_filter.astype(f32).transpose(0, 2, 1).reshape(-1, channels),
            rim.astype(f32).reshape(-1, channels),
            skip[None, :],
        ],
        axis=0,
    )
    prm = jnp.pad(prm, ((0, LANES - prm.shape[0]), (0, 0))).T

    scaled = residue * jnp.sqrt(-jnp.expm1(-2.0 * decay_rate))
    lam = decay_rate.reshape(steps, 1, lanes)
    col = jnp.stack([decay_rate.reshape(steps, lanes), scaled.reshape(steps, lanes)], axis=2)
    col = jnp.pad(col, ((0, 0), (0, 0), (0, LANES - 2)))

    proj_spec = pl.BlockSpec((3, chunk, length), lambda i: (0, i, 0))
    prm_spec = pl.BlockSpec((chunk, LANES), lambda i: (i, 0))
    lam_spec = pl.BlockSpec((1, 1, lanes), lambda i: (i, 0, 0))
    col_spec = pl.BlockSpec((1, lanes, LANES), lambda i: (i, 0, 0))
    row_spec = pl.BlockSpec((chunk, length), lambda i: (i, 0))
    state_spec = pl.BlockSpec((chunk, LANES), lambda i: (i, 0))

    end_state = pl.pallas_call(
        functools.partial(state_kernel, width, modes),
        grid=(steps,),
        in_specs=[proj_spec, prm_spec, lam_spec],
        out_specs=state_spec,
        out_shape=jax.ShapeDtypeStruct((channels, LANES), f32),
    )(projections, prm, lam)

    size = lax.axis_size("ctx")
    dense = end_state[:, :modes].reshape(channels * modes // 128, 128)
    rate = jnp.repeat(decay_rate, width, axis=0).reshape(dense.shape)
    incoming = incoming_state(dense, rate * length, size).reshape(channels, modes)
    incoming = jnp.pad(incoming, ((0, 0), (0, LANES - modes)))

    u0, query = pl.pallas_call(
        functools.partial(local_kernel, width, modes, count),
        grid=(steps,),
        in_specs=[proj_spec, prm_spec, lam_spec, col_spec, row_spec],
        out_specs=[row_spec, row_spec],
        out_shape=[
            jax.ShapeDtypeStruct((channels, length), f32),
            jax.ShapeDtypeStruct((channels, length), bf16),
        ],
    )(projections, prm, lam, col, residual)

    updated, sq = pl.pallas_call(
        functools.partial(finish_kernel, width, modes),
        grid=(steps,),
        in_specs=[row_spec, row_spec, state_spec, col_spec],
        out_specs=[row_spec, pl.BlockSpec((1, 1, length), lambda i: (i, 0, 0))],
        out_shape=[
            jax.ShapeDtypeStruct((channels, length), f32),
            jax.ShapeDtypeStruct((steps, 1, length), f32),
        ],
    )(u0, query, incoming, col)
    squares = lax.psum(jnp.sum(sq, axis=(0, 1)), "tp")
    return (updated * lax.rsqrt(squares / D + epsilon)[None, :] * norm_gain[:, None]).astype(bf16)


def solution(mesh):
    placed = (
        P(None, "tp", "ctx"),
        P(None, "tp", None),
        P("tp", None),
        P("tp", None),
        P("tp"),
        P("tp"),
        P("tp", "ctx"),
    )
    return jax.shard_map(
        local, mesh=mesh, in_specs=placed, out_specs=P("tp", "ctx"), check_vma=False
    )
```

```python
import functools

import jax
import jax.numpy as jnp
from jax import lax
from jax.experimental import pallas as pl
from jax.experimental.pallas import tpu as pltpu
from jax.sharding import PartitionSpec as P

D = 8192
epsilon = 1e-06
BLOCK = 128
LANES = 128
f32 = jnp.float32
bf16 = jnp.bfloat16


def shifted(shard, axis, by):
    size = lax.axis_size(axis)
    pairs = [(i, i + by) for i in range(size) if 0 <= i + by < size]
    return lax.ppermute(shard, axis, pairs)


def incoming_state(ends, span_rate, size):
    place = lax.axis_index("ctx")
    copies = jnp.broadcast_to(ends[None], (size,) + ends.shape)
    gathered = lax.all_to_all(copies, "ctx", 0, 0)
    earlier = jnp.arange(size, dtype=jnp.int32)
    gap = jnp.maximum(place - 1 - earlier, 0).astype(f32)
    weight = jnp.where(
        (earlier < place)[:, None, None],
        jnp.exp(-span_rate[None] * gap[:, None, None]),
        0.0,
    )
    return jnp.sum(weight * gathered, axis=0)


def split2(a):
    hi = a.astype(bf16)
    lo = (a - hi.astype(f32)).astype(bf16)
    return hi, lo


def split3(a):
    hi = a.astype(bf16)
    rest = a - hi.astype(f32)
    mid = rest.astype(bf16)
    lo = (rest - mid.astype(f32)).astype(bf16)
    return hi, mid, lo


def dot(a, b):
    return jnp.dot(a, b, preferred_element_type=f32)


def exact_dot(a, select):
    return sum(dot(part, select) for part in split3(a))


def column(prm, k, rows):
    return jnp.broadcast_to(prm[:, k : k + 1], (rows, LANES))


def featurize(proj_ref, prm, p, taps, rims):
    rows, length = proj_ref.shape[1], proj_ref.shape[2]
    t = taps * p
    weights = [column(prm, t + k, rows) for k in range(3)]
    back2 = column(prm, rims + 2 * p, rows)
    back1 = column(prm, rims + 2 * p + 1, rows)
    lane = lax.broadcasted_iota(jnp.int32, (rows, LANES), 1)
    tiles = [proj_ref[p, :, j * LANES : (j + 1) * LANES].astype(f32) for j in range(length // LANES)]
    once = [pltpu.roll(x, 1, 1) for x in tiles]
    twice = [pltpu.roll(x, 2, 1) for x in tiles]
    out = []
    for j, x in enumerate(tiles):
        if j == 0:
            x1 = jnp.where(lane == 0, back1, once[0])
            x2 = jnp.where(lane == 0, back2, jnp.where(lane == 1, back1, twice[0]))
        else:
            x1 = jnp.where(lane == 0, once[j - 1], once[j])
            x2 = jnp.where(lane < 2, twice[j - 1], twice[j])
        summed = weights[0] * x + weights[1] * x1
        summed = summed + weights[2] * x2
        out.append(summed.astype(bf16))
    return jnp.concatenate(out, axis=1)


def own_modes(rows, lanes, width, modes):
    row = lax.broadcasted_iota(jnp.int32, (rows, lanes), 0) // width
    lane = lax.broadcasted_iota(jnp.int32, (rows, lanes), 1) // modes
    return row == lane


def product_stack(proj_ref, prm, taps, rims, count):
    key = featurize(proj_ref, prm, 1, taps, rims).astype(f32)
    value = featurize(proj_ref, prm, 2, taps, rims).astype(f32)
    product = (key * value).astype(bf16)
    stacked = jnp.concatenate(
        [product[:, b * BLOCK : (b + 1) * BLOCK] for b in range(count)], axis=0
    )
    return product, stacked


def masked_ends(stacked, w_hi_ref, w_lo_ref, rows, width, modes, count):
    ends = dot(stacked, w_hi_ref[0]) + dot(stacked, w_lo_ref[0])
    own = own_modes(rows, ends.shape[1], width, modes)
    return [jnp.where(own, ends[b * rows : (b + 1) * rows], 0.0) for b in range(count)], own


def state_kernel(width, modes, proj_ref, prm_ref, lam_ref, out_ref):
    rows, length = proj_ref.shape[1], proj_ref.shape[2]
    prm = prm_ref[...]
    key = featurize(proj_ref, prm, 1, 3, 9).astype(f32)
    value = featurize(proj_ref, prm, 2, 3, 9).astype(f32)
    product = (key * value).astype(bf16)
    lam = lam_ref[0]
    lanes = lam.shape[1]
    span = (length - 1 - lax.broadcasted_iota(jnp.int32, (length, lanes), 0)).astype(f32)
    w_hi, w_lo = split2(jnp.exp(-lam * span))
    ends = dot(product, w_hi) + dot(product, w_lo)
    own = own_modes(rows, lanes, width, modes)
    out_ref[...] = exact_dot(jnp.where(own, ends, 0.0), select_matrix(lanes, modes))


def select_matrix(lanes, modes):
    mode = lax.broadcasted_iota(jnp.int32, (lanes, LANES), 0) % modes
    lane = lax.broadcasted_iota(jnp.int32, (lanes, LANES), 1)
    return (mode == lane).astype(bf16)


def spread_matrix(lanes, modes):
    lane = lax.broadcasted_iota(jnp.int32, (LANES, lanes), 0)
    mode = lax.broadcasted_iota(jnp.int32, (LANES, lanes), 1) % modes
    return (mode == lane).astype(bf16)


def lead_table(col, first, count):
    lag = (first + lax.broadcasted_iota(jnp.int32, (col.shape[0], count), 1)).astype(f32)
    return col[:, 1:2] * jnp.exp(-col[:, 0:1] * lag)


def local_kernel(
    width,
    modes,
    count,
    proj_ref,
    prm_ref,
    lam_ref,
    col_ref,
    res_ref,
    u0_ref,
    q_ref,
    lead_hi_ref,
    lead_lo_ref,
):
    rows = proj_ref.shape[1]
    groups = rows // width
    taps = 3
    rims = 3 * taps
    skip_at = rims + 6
    prm = prm_ref[...]
    query = featurize(proj_ref, prm, 0, taps, rims)
    q_ref[...] = query
    key = featurize(proj_ref, prm, 1, taps, rims).astype(f32)
    value = featurize(proj_ref, prm, 2, taps, rims).astype(f32)
    product = (key * value).astype(bf16)
    stacked = jnp.concatenate(
        [product[:, b * BLOCK : (b + 1) * BLOCK] for b in range(count)], axis=0
    )
    lam = lam_ref[0]
    col = col_ref[0]
    lanes = lam.shape[1]
    span = (BLOCK - 1 - lax.broadcasted_iota(jnp.int32, (BLOCK, lanes), 0)).astype(f32)
    w_hi, w_lo = split2(jnp.exp(-lam * span))
    used = stacked[: (count - 1) * rows]
    ends = dot(used, w_hi) + dot(used, w_lo)
    own = own_modes(rows, lanes, width, modes)
    decay = jnp.exp(-lam * float(BLOCK))
    state = jnp.where(own, ends[0:rows], 0.0)
    entering = [state]
    for b in range(1, count - 1):
        state = decay * state + jnp.where(own, ends[b * rows : (b + 1) * rows], 0.0)
        entering.append(state)
    z_hi, z_lo = split2(jnp.concatenate(entering, axis=0))
    lead_hi, lead_lo = split2(lead_table(col, 1, BLOCK))
    far = dot(z_hi, lead_hi) + dot(z_hi, lead_lo) + dot(z_lo, lead_hi)
    member = lax.broadcasted_iota(jnp.int32, (groups, lanes), 0) == (
        lax.broadcasted_iota(jnp.int32, (groups, lanes), 1) // modes
    )
    taps_long = sum(dot(member.astype(bf16), part) for part in split3(lead_table(col, 0, BLOCK)))

    s_idx = lax.broadcasted_iota(jnp.int32, (BLOCK, BLOCK), 0)
    t_idx = lax.broadcasted_iota(jnp.int32, (BLOCK, BLOCK), 1)
    pieces = [[None] * groups for _ in range(count)]
    for g in range(groups):
        lhs = jnp.concatenate(
            [stacked[b * rows + g * width : b * rows + (g + 1) * width] for b in range(count)],
            axis=0,
        )
        row = taps_long[g : g + 1, :]
        toeplitz = pltpu.roll(jnp.broadcast_to(row, (BLOCK, BLOCK)), 0, 1, stride=1, stride_axis=0)
        toeplitz = jnp.where(t_idx >= s_idx, toeplitz, 0.0)
        t_hi, t_lo = split2(toeplitz)
        near = dot(lhs, t_hi) + dot(lhs, t_lo)
        for b in range(count):
            pieces[b][g] = near[b * width : (b + 1) * width]
    long_term = jnp.concatenate(
        [
            jnp.concatenate(pieces[b], axis=0) + (far[(b - 1) * rows : b * rows] if b else 0.0)
            for b in range(count)
        ],
        axis=1,
    )
    signal = product.astype(f32)
    skip_b = jnp.concatenate([column(prm, skip_at, rows)] * (signal.shape[1] // LANES), axis=1)
    mixed = query.astype(f32) * (long_term + skip_b * signal)
    u0_ref[...] = res_ref[...].astype(f32) + mixed
    whole_hi, whole_lo = split2(lead_table(col, 1, res_ref.shape[1]))
    lead_hi_ref[0] = whole_hi
    lead_lo_ref[0] = whole_lo


def finish_kernel(width, modes, u0_ref, q_ref, z_ref, lead_hi_ref, lead_lo_ref, upd_ref, sq_ref):
    rows, length = u0_ref.shape
    lanes = lead_hi_ref.shape[1]
    spread = exact_dot(z_ref[...], spread_matrix(lanes, modes))
    own = own_modes(rows, lanes, width, modes)
    z_hi, z_lo = split2(jnp.where(own, spread, 0.0))
    lead_hi = lead_hi_ref[0]
    lead_lo = lead_lo_ref[0]
    far = dot(z_hi, lead_hi) + dot(z_hi, lead_lo) + dot(z_lo, lead_hi)
    updated = u0_ref[...] + q_ref[...].astype(f32) * far
    upd_ref[...] = updated
    sq_ref[0] = jnp.sum(updated * updated, axis=0, keepdims=True)


def local(projections, short_filter, decay_rate, residue, skip, norm_gain, residual):
    channels, length = residual.shape
    groups, modes = decay_rate.shape
    width = channels // groups
    rim_len = short_filter.shape[2] - 1
    count = length // BLOCK
    chunk = 256 if channels % 256 == 0 else channels
    chunk_groups = chunk // width
    lanes = chunk_groups * modes
    steps = channels // chunk

    edge = projections[:, :, length - rim_len :].transpose(0, 2, 1)
    rim = shifted(edge, "ctx", 1)
    prm = jnp.concatenate(
        [
            short_filter.astype(f32).transpose(0, 2, 1).reshape(-1, channels),
            rim.astype(f32).reshape(-1, channels),
            skip[None, :],
        ],
        axis=0,
    )
    prm = jnp.pad(prm, ((0, LANES - prm.shape[0]), (0, 0))).T

    scaled = residue * jnp.sqrt(-jnp.expm1(-2.0 * decay_rate))
    lam = decay_rate.reshape(steps, 1, lanes)
    col = jnp.stack([decay_rate.reshape(steps, lanes), scaled.reshape(steps, lanes)], axis=2)
    col = jnp.pad(col, ((0, 0), (0, 0), (0, LANES - 2)))

    proj_spec = pl.BlockSpec((3, chunk, length), lambda i: (0, i, 0))
    prm_spec = pl.BlockSpec((chunk, LANES), lambda i: (i, 0))
    lam_spec = pl.BlockSpec((1, 1, lanes), lambda i: (i, 0, 0))
    col_spec = pl.BlockSpec((1, lanes, LANES), lambda i: (i, 0, 0))
    row_spec = pl.BlockSpec((chunk, length), lambda i: (i, 0))
    state_spec = pl.BlockSpec((chunk, LANES), lambda i: (i, 0))

    end_state = pl.pallas_call(
        functools.partial(state_kernel, width, modes),
        grid=(steps,),
        in_specs=[proj_spec, prm_spec, lam_spec],
        out_specs=state_spec,
        out_shape=jax.ShapeDtypeStruct((channels, LANES), f32),
    )(projections, prm, lam)

    size = lax.axis_size("ctx")
    dense = end_state[:, :modes].reshape(channels * modes // 128, 128)
    rate = jnp.repeat(decay_rate, width, axis=0).reshape(dense.shape)
    incoming = incoming_state(dense, rate * length, size).reshape(channels, modes)
    incoming = jnp.pad(incoming, ((0, 0), (0, LANES - modes)))

    whole_spec = pl.BlockSpec((1, lanes, length), lambda i: (i, 0, 0))
    u0, query, whole_hi, whole_lo = pl.pallas_call(
        functools.partial(local_kernel, width, modes, count),
        grid=(steps,),
        in_specs=[proj_spec, prm_spec, lam_spec, col_spec, row_spec],
        out_specs=[row_spec, row_spec, whole_spec, whole_spec],
        out_shape=[
            jax.ShapeDtypeStruct((channels, length), f32),
            jax.ShapeDtypeStruct((channels, length), bf16),
            jax.ShapeDtypeStruct((steps, lanes, length), bf16),
            jax.ShapeDtypeStruct((steps, lanes, length), bf16),
        ],
    )(projections, prm, lam, col, residual)

    updated, sq = pl.pallas_call(
        functools.partial(finish_kernel, width, modes),
        grid=(steps,),
        in_specs=[row_spec, row_spec, state_spec, whole_spec, whole_spec],
        out_specs=[row_spec, pl.BlockSpec((1, 1, length), lambda i: (i, 0, 0))],
        out_shape=[
            jax.ShapeDtypeStruct((channels, length), f32),
            jax.ShapeDtypeStruct((steps, 1, length), f32),
        ],
    )(u0, query, incoming, whole_hi, whole_lo)
    squares = lax.psum(jnp.sum(sq, axis=(0, 1)), "tp")
    return (updated * lax.rsqrt(squares / D + epsilon)[None, :] * norm_gain[:, None]).astype(bf16)


def solution(mesh):
    placed = (
        P(None, "tp", "ctx"),
        P(None, "tp", None),
        P("tp", None),
        P("tp", None),
        P("tp"),
        P("tp"),
        P("tp", "ctx"),
    )
    return jax.shard_map(
        local, mesh=mesh, in_specs=placed, out_specs=P("tp", "ctx"), check_vma=False
    )
```

```python
import functools

import jax
import jax.numpy as jnp
from jax import lax
from jax.experimental import pallas as pl
from jax.experimental.pallas import tpu as pltpu
from jax.sharding import PartitionSpec as P

D = 8192
epsilon = 1e-06
BLOCK = 128
LANES = 128
f32 = jnp.float32
bf16 = jnp.bfloat16


def shifted(shard, axis, by):
    size = lax.axis_size(axis)
    pairs = [(i, i + by) for i in range(size) if 0 <= i + by < size]
    return lax.ppermute(shard, axis, pairs)


def incoming_state(ends, span_rate, size):
    place = lax.axis_index("ctx")
    copies = jnp.broadcast_to(ends[None], (size,) + ends.shape)
    gathered = lax.all_to_all(copies, "ctx", 0, 0)
    earlier = jnp.arange(size, dtype=jnp.int32)
    gap = jnp.maximum(place - 1 - earlier, 0).astype(f32)
    weight = jnp.where(
        (earlier < place)[:, None, None],
        jnp.exp(-span_rate[None] * gap[:, None, None]),
        0.0,
    )
    return jnp.sum(weight * gathered, axis=0)


def split2(a):
    hi = a.astype(bf16)
    lo = (a - hi.astype(f32)).astype(bf16)
    return hi, lo


def split3(a):
    hi = a.astype(bf16)
    rest = a - hi.astype(f32)
    mid = rest.astype(bf16)
    lo = (rest - mid.astype(f32)).astype(bf16)
    return hi, mid, lo


def dot(a, b):
    return jnp.dot(a, b, preferred_element_type=f32)


def exact_dot(a, select):
    return sum(dot(part, select) for part in split3(a))


def column(prm, k, rows):
    return jnp.broadcast_to(prm[:, k : k + 1], (rows, LANES))


def featurize(proj_ref, prm, p, taps, rims):
    rows, length = proj_ref.shape[1], proj_ref.shape[2]
    t = taps * p
    weights = [column(prm, t + k, rows) for k in range(3)]
    back2 = column(prm, rims + 2 * p, rows)
    back1 = column(prm, rims + 2 * p + 1, rows)
    lane = lax.broadcasted_iota(jnp.int32, (rows, LANES), 1)
    tiles = [proj_ref[p, :, j * LANES : (j + 1) * LANES].astype(f32) for j in range(length // LANES)]
    once = [pltpu.roll(x, 1, 1) for x in tiles]
    twice = [pltpu.roll(x, 2, 1) for x in tiles]
    out = []
    for j, x in enumerate(tiles):
        if j == 0:
            x1 = jnp.where(lane == 0, back1, once[0])
            x2 = jnp.where(lane == 0, back2, jnp.where(lane == 1, back1, twice[0]))
        else:
            x1 = jnp.where(lane == 0, once[j - 1], once[j])
            x2 = jnp.where(lane < 2, twice[j - 1], twice[j])
        summed = weights[0] * x + weights[1] * x1
        summed = summed + weights[2] * x2
        out.append(summed.astype(bf16))
    return jnp.concatenate(out, axis=1)


def own_modes(rows, lanes, width, modes):
    row = lax.broadcasted_iota(jnp.int32, (rows, lanes), 0) // width
    lane = lax.broadcasted_iota(jnp.int32, (rows, lanes), 1) // modes
    return row == lane


def product_stack(proj_ref, prm, taps, rims, count):
    key = featurize(proj_ref, prm, 1, taps, rims).astype(f32)
    value = featurize(proj_ref, prm, 2, taps, rims).astype(f32)
    product = (key * value).astype(bf16)
    stacked = jnp.concatenate(
        [product[:, b * BLOCK : (b + 1) * BLOCK] for b in range(count)], axis=0
    )
    return product, stacked


def masked_ends(stacked, w_hi_ref, w_lo_ref, rows, width, modes, count):
    ends = dot(stacked, w_hi_ref[0]) + dot(stacked, w_lo_ref[0])
    own = own_modes(rows, ends.shape[1], width, modes)
    return [jnp.where(own, ends[b * rows : (b + 1) * rows], 0.0) for b in range(count)], own


def state_kernel(width, modes, proj_ref, prm_ref, lam_ref, out_ref):
    rows, length = proj_ref.shape[1], proj_ref.shape[2]
    prm = prm_ref[...]
    key = featurize(proj_ref, prm, 1, 3, 9).astype(f32)
    value = featurize(proj_ref, prm, 2, 3, 9).astype(f32)
    product = (key * value).astype(bf16)
    lam = lam_ref[0][0:1, :]
    lanes = lam.shape[1]
    span = (length - 1 - lax.broadcasted_iota(jnp.int32, (length, lanes), 0)).astype(f32)
    w_hi, w_lo = split2(jnp.exp(-lam * span))
    ends = dot(product, w_hi) + dot(product, w_lo)
    own = own_modes(rows, lanes, width, modes)
    out_ref[...] = exact_dot(jnp.where(own, ends, 0.0), select_matrix(lanes, modes))[:, :modes]


def select_matrix(lanes, modes):
    mode = lax.broadcasted_iota(jnp.int32, (lanes, LANES), 0) % modes
    lane = lax.broadcasted_iota(jnp.int32, (lanes, LANES), 1)
    return (mode == lane).astype(bf16)


def spread_matrix(lanes, modes):
    lane = lax.broadcasted_iota(jnp.int32, (modes, lanes), 0)
    mode = lax.broadcasted_iota(jnp.int32, (modes, lanes), 1) % modes
    return (mode == lane).astype(bf16)


def columns(row):
    lanes = row.shape[1]
    diagonal = lax.broadcasted_iota(jnp.int32, (lanes, lanes), 0) == lax.broadcasted_iota(
        jnp.int32, (lanes, lanes), 1
    )
    spread = jnp.where(diagonal, jnp.broadcast_to(row, (lanes, lanes)), 0.0)
    return exact_dot(spread, jnp.ones((lanes, LANES), bf16))


def lead_table(rates, weights, first, count):
    wide = count // LANES
    rates = jnp.concatenate([rates] * wide, axis=1) if wide > 1 else rates
    weights = jnp.concatenate([weights] * wide, axis=1) if wide > 1 else weights
    lag = (first + lax.broadcasted_iota(jnp.int32, (rates.shape[0], count), 1)).astype(f32)
    return weights * jnp.exp(-rates * lag)


def local_kernel(
    width,
    modes,
    count,
    proj_ref,
    prm_ref,
    lam_ref,
    res_ref,
    u0_ref,
    q_ref,
):
    rows = proj_ref.shape[1]
    groups = rows // width
    taps = 3
    rims = 3 * taps
    skip_at = rims + 6
    prm = prm_ref[...]
    query = featurize(proj_ref, prm, 0, taps, rims)
    q_ref[...] = query
    key = featurize(proj_ref, prm, 1, taps, rims).astype(f32)
    value = featurize(proj_ref, prm, 2, taps, rims).astype(f32)
    product = (key * value).astype(bf16)
    stacked = jnp.concatenate(
        [product[:, b * BLOCK : (b + 1) * BLOCK] for b in range(count)], axis=0
    )
    lam = lam_ref[0][0:1, :]
    rates = columns(lam)
    weights = columns(lam_ref[0][1:2, :])
    lanes = lam.shape[1]
    span = (BLOCK - 1 - lax.broadcasted_iota(jnp.int32, (BLOCK, lanes), 0)).astype(f32)
    w_hi, w_lo = split2(jnp.exp(-lam * span))
    used = stacked[: (count - 1) * rows]
    ends = dot(used, w_hi) + dot(used, w_lo)
    own = own_modes(rows, lanes, width, modes)
    decay = jnp.exp(-lam * float(BLOCK))
    state = jnp.where(own, ends[0:rows], 0.0)
    entering = [state]
    for b in range(1, count - 1):
        state = decay * state + jnp.where(own, ends[b * rows : (b + 1) * rows], 0.0)
        entering.append(state)
    z_hi, z_lo = split2(jnp.concatenate(entering, axis=0))
    lead_hi, lead_lo = split2(lead_table(rates, weights, 1, BLOCK))
    far = dot(z_hi, lead_hi) + dot(z_hi, lead_lo) + dot(z_lo, lead_hi)
    member = lax.broadcasted_iota(jnp.int32, (groups, lanes), 0) == (
        lax.broadcasted_iota(jnp.int32, (groups, lanes), 1) // modes
    )
    taps_long = sum(dot(member.astype(bf16), part) for part in split3(lead_table(rates, weights, 0, BLOCK)))

    s_idx = lax.broadcasted_iota(jnp.int32, (BLOCK, BLOCK), 0)
    t_idx = lax.broadcasted_iota(jnp.int32, (BLOCK, BLOCK), 1)
    pieces = [[None] * groups for _ in range(count)]
    for g in range(groups):
        lhs = jnp.concatenate(
            [stacked[b * rows + g * width : b * rows + (g + 1) * width] for b in range(count)],
            axis=0,
        )
        row = taps_long[g : g + 1, :]
        toeplitz = pltpu.roll(jnp.broadcast_to(row, (BLOCK, BLOCK)), 0, 1, stride=1, stride_axis=0)
        toeplitz = jnp.where(t_idx >= s_idx, toeplitz, 0.0)
        t_hi, t_lo = split2(toeplitz)
        near = dot(lhs, t_hi) + dot(lhs, t_lo)
        for b in range(count):
            pieces[b][g] = near[b * width : (b + 1) * width]
    long_term = jnp.concatenate(
        [
            jnp.concatenate(pieces[b], axis=0) + (far[(b - 1) * rows : b * rows] if b else 0.0)
            for b in range(count)
        ],
        axis=1,
    )
    signal = product.astype(f32)
    skip_b = jnp.concatenate([column(prm, skip_at, rows)] * (signal.shape[1] // LANES), axis=1)
    mixed = query.astype(f32) * (long_term + skip_b * signal)
    u0_ref[...] = res_ref[...].astype(f32) + mixed


def finish_kernel(width, modes, u0_ref, q_ref, z_ref, lam_ref, upd_ref, sq_ref):
    rows, length = u0_ref.shape
    lam = lam_ref[0][0:1, :]
    lanes = lam.shape[1]
    spread = exact_dot(z_ref[...], spread_matrix(lanes, modes))
    own = own_modes(rows, lanes, width, modes)
    z_hi, z_lo = split2(jnp.where(own, spread, 0.0))
    lead_hi, lead_lo = split2(lead_table(columns(lam), columns(lam_ref[0][1:2, :]), 1, length))
    far = dot(z_hi, lead_hi) + dot(z_hi, lead_lo) + dot(z_lo, lead_hi)
    updated = u0_ref[...] + q_ref[...].astype(f32) * far
    upd_ref[...] = updated
    sq_ref[0] = jnp.sum(updated * updated, axis=0, keepdims=True)


def local(projections, short_filter, decay_rate, residue, skip, norm_gain, residual):
    channels, length = residual.shape
    groups, modes = decay_rate.shape
    width = channels // groups
    rim_len = short_filter.shape[2] - 1
    count = length // BLOCK
    chunk = 256 if channels % 256 == 0 else channels
    chunk_groups = chunk // width
    lanes = chunk_groups * modes
    steps = channels // chunk

    edge = projections[:, :, length - rim_len :].transpose(0, 2, 1)
    rim = shifted(edge, "ctx", 1)
    prm = jnp.concatenate(
        [
            short_filter.astype(f32).transpose(0, 2, 1).reshape(-1, channels),
            rim.astype(f32).reshape(-1, channels),
            skip[None, :],
        ],
        axis=0,
    )
    prm = jnp.pad(prm, ((0, LANES - prm.shape[0]), (0, 0))).T

    scaled = residue * jnp.sqrt(-jnp.expm1(-2.0 * decay_rate))
    lam = jnp.stack([decay_rate.reshape(steps, lanes), scaled.reshape(steps, lanes)], axis=1)

    proj_spec = pl.BlockSpec((3, chunk, length), lambda i: (0, i, 0))
    prm_spec = pl.BlockSpec((chunk, LANES), lambda i: (i, 0))
    lam_spec = pl.BlockSpec((1, 2, lanes), lambda i: (i, 0, 0))
    row_spec = pl.BlockSpec((chunk, length), lambda i: (i, 0))
    state_spec = pl.BlockSpec((chunk, modes), lambda i: (i, 0))

    end_state = pl.pallas_call(
        functools.partial(state_kernel, width, modes),
        grid=(steps,),
        in_specs=[proj_spec, prm_spec, lam_spec],
        out_specs=state_spec,
        out_shape=jax.ShapeDtypeStruct((channels, modes), f32),
    )(projections, prm, lam)

    size = lax.axis_size("ctx")
    dense = end_state.reshape(channels * modes // 128, 128)
    rate = jnp.repeat(decay_rate, width, axis=0).reshape(dense.shape)
    incoming = incoming_state(dense, rate * length, size).reshape(channels, modes)

    u0, query = pl.pallas_call(
        functools.partial(local_kernel, width, modes, count),
        grid=(steps,),
        in_specs=[proj_spec, prm_spec, lam_spec, row_spec],
        out_specs=[row_spec, row_spec],
        out_shape=[
            jax.ShapeDtypeStruct((channels, length), f32),
            jax.ShapeDtypeStruct((channels, length), bf16),
        ],
    )(projections, prm, lam, residual)

    updated, sq = pl.pallas_call(
        functools.partial(finish_kernel, width, modes),
        grid=(steps,),
        in_specs=[row_spec, row_spec, state_spec, lam_spec],
        out_specs=[row_spec, pl.BlockSpec((1, 1, length), lambda i: (i, 0, 0))],
        out_shape=[
            jax.ShapeDtypeStruct((channels, length), f32),
            jax.ShapeDtypeStruct((steps, 1, length), f32),
        ],
    )(u0, query, incoming, lam)
    squares = lax.psum(jnp.sum(sq, axis=(0, 1)), "tp")
    return (updated * lax.rsqrt(squares / D + epsilon)[None, :] * norm_gain[:, None]).astype(bf16)


def solution(mesh):
    placed = (
        P(None, "tp", "ctx"),
        P(None, "tp", None),
        P("tp", None),
        P("tp", None),
        P("tp"),
        P("tp"),
        P("tp", "ctx"),
    )
    return jax.shard_map(
        local, mesh=mesh, in_specs=placed, out_specs=P("tp", "ctx"), check_vma=False
    )
```

```python
import functools

import jax
import jax.numpy as jnp
from jax import lax
from jax.experimental import pallas as pl
from jax.experimental.pallas import tpu as pltpu
from jax.sharding import PartitionSpec as P

D = 8192
epsilon = 1e-06
BLOCK = 128
LANES = 128
f32 = jnp.float32
bf16 = jnp.bfloat16


def shifted(shard, axis, by):
    size = lax.axis_size(axis)
    pairs = [(i, i + by) for i in range(size) if 0 <= i + by < size]
    return lax.ppermute(shard, axis, pairs)


def incoming_state(ends, span_rate, size):
    place = lax.axis_index("ctx")
    copies = jnp.broadcast_to(ends.astype(bf16)[None], (size,) + ends.shape)
    gathered = lax.all_to_all(copies, "ctx", 0, 0).astype(f32)
    earlier = jnp.arange(size, dtype=jnp.int32)
    gap = jnp.maximum(place - 1 - earlier, 0).astype(f32)
    weight = jnp.where(
        (earlier < place)[:, None, None],
        jnp.exp(-span_rate[None] * gap[:, None, None]),
        0.0,
    )
    return jnp.sum(weight * gathered, axis=0)


def split2(a):
    hi = a.astype(bf16)
    lo = (a - hi.astype(f32)).astype(bf16)
    return hi, lo


def split3(a):
    hi = a.astype(bf16)
    rest = a - hi.astype(f32)
    mid = rest.astype(bf16)
    lo = (rest - mid.astype(f32)).astype(bf16)
    return hi, mid, lo


def dot(a, b):
    return jnp.dot(a, b, preferred_element_type=f32)


def exact_dot(a, select):
    return sum(dot(part, select) for part in split3(a))


def column(prm, k, rows):
    return jnp.broadcast_to(prm[:, k : k + 1], (rows, LANES))


def featurize(proj_ref, prm, p, taps, rims):
    rows, length = proj_ref.shape[1], proj_ref.shape[2]
    t = taps * p
    weights = [column(prm, t + k, rows) for k in range(3)]
    back2 = column(prm, rims + 2 * p, rows)
    back1 = column(prm, rims + 2 * p + 1, rows)
    lane = lax.broadcasted_iota(jnp.int32, (rows, LANES), 1)
    tiles = [proj_ref[p, :, j * LANES : (j + 1) * LANES].astype(f32) for j in range(length // LANES)]
    once = [pltpu.roll(x, 1, 1) for x in tiles]
    twice = [pltpu.roll(x, 2, 1) for x in tiles]
    out = []
    for j, x in enumerate(tiles):
        if j == 0:
            x1 = jnp.where(lane == 0, back1, once[0])
            x2 = jnp.where(lane == 0, back2, jnp.where(lane == 1, back1, twice[0]))
        else:
            x1 = jnp.where(lane == 0, once[j - 1], once[j])
            x2 = jnp.where(lane < 2, twice[j - 1], twice[j])
        summed = weights[0] * x + weights[1] * x1
        summed = summed + weights[2] * x2
        out.append(summed.astype(bf16))
    return jnp.concatenate(out, axis=1)


def own_modes(rows, lanes, width, modes):
    row = lax.broadcasted_iota(jnp.int32, (rows, lanes), 0) // width
    lane = lax.broadcasted_iota(jnp.int32, (rows, lanes), 1) // modes
    return row == lane


def product_stack(proj_ref, prm, taps, rims, count):
    key = featurize(proj_ref, prm, 1, taps, rims).astype(f32)
    value = featurize(proj_ref, prm, 2, taps, rims).astype(f32)
    product = (key * value).astype(bf16)
    stacked = jnp.concatenate(
        [product[:, b * BLOCK : (b + 1) * BLOCK] for b in range(count)], axis=0
    )
    return product, stacked


def masked_ends(stacked, w_hi_ref, w_lo_ref, rows, width, modes, count):
    ends = dot(stacked, w_hi_ref[0]) + dot(stacked, w_lo_ref[0])
    own = own_modes(rows, ends.shape[1], width, modes)
    return [jnp.where(own, ends[b * rows : (b + 1) * rows], 0.0) for b in range(count)], own


def state_kernel(width, modes, proj_ref, prm_ref, lam_ref, out_ref):
    rows, length = proj_ref.shape[1], proj_ref.shape[2]
    prm = prm_ref[...]
    key = featurize(proj_ref, prm, 1, 3, 9).astype(f32)
    value = featurize(proj_ref, prm, 2, 3, 9).astype(f32)
    product = (key * value).astype(bf16)
    lam = lam_ref[0][0:1, :]
    lanes = lam.shape[1]
    span = (length - 1 - lax.broadcasted_iota(jnp.int32, (length, lanes), 0)).astype(f32)
    w_hi, w_lo = split2(jnp.exp(-lam * span))
    ends = dot(product, w_hi) + dot(product, w_lo)
    own = own_modes(rows, lanes, width, modes)
    out_ref[...] = exact_dot(jnp.where(own, ends, 0.0), select_matrix(lanes, modes))[:, :modes]


def select_matrix(lanes, modes):
    mode = lax.broadcasted_iota(jnp.int32, (lanes, LANES), 0) % modes
    lane = lax.broadcasted_iota(jnp.int32, (lanes, LANES), 1)
    return (mode == lane).astype(bf16)


def spread_matrix(lanes, modes):
    lane = lax.broadcasted_iota(jnp.int32, (modes, lanes), 0)
    mode = lax.broadcasted_iota(jnp.int32, (modes, lanes), 1) % modes
    return (mode == lane).astype(bf16)


def columns(row):
    lanes = row.shape[1]
    diagonal = lax.broadcasted_iota(jnp.int32, (lanes, lanes), 0) == lax.broadcasted_iota(
        jnp.int32, (lanes, lanes), 1
    )
    spread = jnp.where(diagonal, jnp.broadcast_to(row, (lanes, lanes)), 0.0)
    return exact_dot(spread, jnp.ones((lanes, LANES), bf16))


def lead_table(rates, weights, first, count):
    wide = count // LANES
    rates = jnp.concatenate([rates] * wide, axis=1) if wide > 1 else rates
    weights = jnp.concatenate([weights] * wide, axis=1) if wide > 1 else weights
    lag = (first + lax.broadcasted_iota(jnp.int32, (rates.shape[0], count), 1)).astype(f32)
    return weights * jnp.exp(-rates * lag)


def local_kernel(
    width,
    modes,
    count,
    proj_ref,
    prm_ref,
    lam_ref,
    res_ref,
    u0_ref,
    q_ref,
):
    rows = proj_ref.shape[1]
    groups = rows // width
    taps = 3
    rims = 3 * taps
    skip_at = rims + 6
    prm = prm_ref[...]
    query = featurize(proj_ref, prm, 0, taps, rims)
    q_ref[...] = query
    key = featurize(proj_ref, prm, 1, taps, rims).astype(f32)
    value = featurize(proj_ref, prm, 2, taps, rims).astype(f32)
    product = (key * value).astype(bf16)
    stacked = jnp.concatenate(
        [product[:, b * BLOCK : (b + 1) * BLOCK] for b in range(count)], axis=0
    )
    lam = lam_ref[0][0:1, :]
    rates = columns(lam)
    weights = columns(lam_ref[0][1:2, :])
    lanes = lam.shape[1]
    span = (BLOCK - 1 - lax.broadcasted_iota(jnp.int32, (BLOCK, lanes), 0)).astype(f32)
    w_hi, w_lo = split2(jnp.exp(-lam * span))
    used = stacked[: (count - 1) * rows]
    ends = dot(used, w_hi) + dot(used, w_lo)
    own = own_modes(rows, lanes, width, modes)
    decay = jnp.exp(-lam * float(BLOCK))
    state = jnp.where(own, ends[0:rows], 0.0)
    entering = [state]
    for b in range(1, count - 1):
        state = decay * state + jnp.where(own, ends[b * rows : (b + 1) * rows], 0.0)
        entering.append(state)
    z_hi, z_lo = split2(jnp.concatenate(entering, axis=0))
    lead_hi, lead_lo = split2(lead_table(rates, weights, 1, BLOCK))
    far = dot(z_hi, lead_hi) + dot(z_hi, lead_lo) + dot(z_lo, lead_hi)
    member = lax.broadcasted_iota(jnp.int32, (groups, lanes), 0) == (
        lax.broadcasted_iota(jnp.int32, (groups, lanes), 1) // modes
    )
    taps_long = sum(dot(member.astype(bf16), part) for part in split3(lead_table(rates, weights, 0, BLOCK)))

    s_idx = lax.broadcasted_iota(jnp.int32, (BLOCK, BLOCK), 0)
    t_idx = lax.broadcasted_iota(jnp.int32, (BLOCK, BLOCK), 1)
    pieces = [[None] * groups for _ in range(count)]
    for g in range(groups):
        lhs = jnp.concatenate(
            [stacked[b * rows + g * width : b * rows + (g + 1) * width] for b in range(count)],
            axis=0,
        )
        row = taps_long[g : g + 1, :]
        toeplitz = pltpu.roll(jnp.broadcast_to(row, (BLOCK, BLOCK)), 0, 1, stride=1, stride_axis=0)
        toeplitz = jnp.where(t_idx >= s_idx, toeplitz, 0.0)
        t_hi, t_lo = split2(toeplitz)
        near = dot(lhs, t_hi) + dot(lhs, t_lo)
        for b in range(count):
            pieces[b][g] = near[b * width : (b + 1) * width]
    long_term = jnp.concatenate(
        [
            jnp.concatenate(pieces[b], axis=0) + (far[(b - 1) * rows : b * rows] if b else 0.0)
            for b in range(count)
        ],
        axis=1,
    )
    signal = product.astype(f32)
    skip_b = jnp.concatenate([column(prm, skip_at, rows)] * (signal.shape[1] // LANES), axis=1)
    mixed = query.astype(f32) * (long_term + skip_b * signal)
    u0_ref[...] = res_ref[...].astype(f32) + mixed


def finish_kernel(width, modes, u0_ref, q_ref, z_ref, lam_ref, upd_ref, sq_ref):
    rows, length = u0_ref.shape
    lam = lam_ref[0][0:1, :]
    lanes = lam.shape[1]
    spread = exact_dot(z_ref[...], spread_matrix(lanes, modes))
    own = own_modes(rows, lanes, width, modes)
    z_hi, z_lo = split2(jnp.where(own, spread, 0.0))
    lead_hi, lead_lo = split2(lead_table(columns(lam), columns(lam_ref[0][1:2, :]), 1, length))
    far = dot(z_hi, lead_hi) + dot(z_hi, lead_lo) + dot(z_lo, lead_hi)
    updated = u0_ref[...] + q_ref[...].astype(f32) * far
    upd_ref[...] = updated
    sq_ref[0] = jnp.sum(updated * updated, axis=0, keepdims=True)


def local(projections, short_filter, decay_rate, residue, skip, norm_gain, residual):
    channels, length = residual.shape
    groups, modes = decay_rate.shape
    width = channels // groups
    rim_len = short_filter.shape[2] - 1
    count = length // BLOCK
    chunk = 256 if channels % 256 == 0 else channels
    chunk_groups = chunk // width
    lanes = chunk_groups * modes
    steps = channels // chunk

    edge = projections[:, :, length - rim_len :].transpose(0, 2, 1)
    rim = shifted(edge, "ctx", 1)
    prm = jnp.concatenate(
        [
            short_filter.astype(f32).transpose(0, 2, 1).reshape(-1, channels),
            rim.astype(f32).reshape(-1, channels),
            skip[None, :],
        ],
        axis=0,
    )
    prm = jnp.pad(prm, ((0, LANES - prm.shape[0]), (0, 0))).T

    scaled = residue * jnp.sqrt(-jnp.expm1(-2.0 * decay_rate))
    lam = jnp.stack([decay_rate.reshape(steps, lanes), scaled.reshape(steps, lanes)], axis=1)

    proj_spec = pl.BlockSpec((3, chunk, length), lambda i: (0, i, 0))
    prm_spec = pl.BlockSpec((chunk, LANES), lambda i: (i, 0))
    lam_spec = pl.BlockSpec((1, 2, lanes), lambda i: (i, 0, 0))
    row_spec = pl.BlockSpec((chunk, length), lambda i: (i, 0))
    state_spec = pl.BlockSpec((chunk, modes), lambda i: (i, 0))

    end_state = pl.pallas_call(
        functools.partial(state_kernel, width, modes),
        grid=(steps,),
        in_specs=[proj_spec, prm_spec, lam_spec],
        out_specs=state_spec,
        out_shape=jax.ShapeDtypeStruct((channels, modes), f32),
    )(projections, prm, lam)

    size = lax.axis_size("ctx")
    dense = end_state.reshape(channels * modes // 128, 128)
    rate = jnp.repeat(decay_rate, width, axis=0).reshape(dense.shape)
    incoming = incoming_state(dense, rate * length, size).reshape(channels, modes)

    u0, query = pl.pallas_call(
        functools.partial(local_kernel, width, modes, count),
        grid=(steps,),
        in_specs=[proj_spec, prm_spec, lam_spec, row_spec],
        out_specs=[row_spec, row_spec],
        out_shape=[
            jax.ShapeDtypeStruct((channels, length), f32),
            jax.ShapeDtypeStruct((channels, length), bf16),
        ],
    )(projections, prm, lam, residual)

    updated, sq = pl.pallas_call(
        functools.partial(finish_kernel, width, modes),
        grid=(steps,),
        in_specs=[row_spec, row_spec, state_spec, lam_spec],
        out_specs=[row_spec, pl.BlockSpec((1, 1, length), lambda i: (i, 0, 0))],
        out_shape=[
            jax.ShapeDtypeStruct((channels, length), f32),
            jax.ShapeDtypeStruct((steps, 1, length), f32),
        ],
    )(u0, query, incoming, lam)
    squares = lax.psum(jnp.sum(sq, axis=(0, 1)), "tp")
    return (updated * lax.rsqrt(squares / D + epsilon)[None, :] * norm_gain[:, None]).astype(bf16)


def solution(mesh):
    placed = (
        P(None, "tp", "ctx"),
        P(None, "tp", None),
        P("tp", None),
        P("tp", None),
        P("tp"),
        P("tp"),
        P("tp", "ctx"),
    )
    return jax.shard_map(
        local, mesh=mesh, in_specs=placed, out_specs=P("tp", "ctx"), check_vma=False
    )
```

```python
import functools

import jax
import jax.numpy as jnp
from jax import lax
from jax.experimental import pallas as pl
from jax.experimental.pallas import tpu as pltpu
from jax.sharding import PartitionSpec as P

D = 8192
epsilon = 1e-06
BLOCK = 128
LANES = 128
f32 = jnp.float32
bf16 = jnp.bfloat16


def shifted(shard, axis, by):
    size = lax.axis_size(axis)
    pairs = [(i, i + by) for i in range(size) if 0 <= i + by < size]
    return lax.ppermute(shard, axis, pairs)


def incoming_state(ends, span_rate, size):
    place = lax.axis_index("ctx")
    copies = jnp.broadcast_to(ends[None], (size,) + ends.shape)
    gathered = lax.all_to_all(copies, "ctx", 0, 0).astype(f32)
    earlier = jnp.arange(size, dtype=jnp.int32)
    gap = jnp.maximum(place - 1 - earlier, 0).astype(f32)
    weight = jnp.where(
        (earlier < place)[:, None, None],
        jnp.exp(-span_rate[None] * gap[:, None, None]),
        0.0,
    )
    return jnp.sum(weight * gathered, axis=0)


def split2(a):
    hi = a.astype(bf16)
    lo = (a - hi.astype(f32)).astype(bf16)
    return hi, lo


def split3(a):
    hi = a.astype(bf16)
    rest = a - hi.astype(f32)
    mid = rest.astype(bf16)
    lo = (rest - mid.astype(f32)).astype(bf16)
    return hi, mid, lo


def dot(a, b):
    return jnp.dot(a, b, preferred_element_type=f32)


def exact_dot(a, select):
    return sum(dot(part, select) for part in split3(a))


def column(prm, k, rows):
    return jnp.broadcast_to(prm[:, k : k + 1], (rows, LANES))


def featurize(proj_ref, prm, p, taps, rims):
    rows, length = proj_ref.shape[1], proj_ref.shape[2]
    t = taps * p
    weights = [column(prm, t + k, rows) for k in range(3)]
    back2 = column(prm, rims + 2 * p, rows)
    back1 = column(prm, rims + 2 * p + 1, rows)
    lane = lax.broadcasted_iota(jnp.int32, (rows, LANES), 1)
    tiles = [proj_ref[p, :, j * LANES : (j + 1) * LANES].astype(f32) for j in range(length // LANES)]
    once = [pltpu.roll(x, 1, 1) for x in tiles]
    twice = [pltpu.roll(x, 2, 1) for x in tiles]
    out = []
    for j, x in enumerate(tiles):
        if j == 0:
            x1 = jnp.where(lane == 0, back1, once[0])
            x2 = jnp.where(lane == 0, back2, jnp.where(lane == 1, back1, twice[0]))
        else:
            x1 = jnp.where(lane == 0, once[j - 1], once[j])
            x2 = jnp.where(lane < 2, twice[j - 1], twice[j])
        summed = weights[0] * x + weights[1] * x1
        summed = summed + weights[2] * x2
        out.append(summed.astype(bf16))
    return jnp.concatenate(out, axis=1)


def own_modes(rows, lanes, width, modes):
    row = lax.broadcasted_iota(jnp.int32, (rows, lanes), 0) // width
    lane = lax.broadcasted_iota(jnp.int32, (rows, lanes), 1) // modes
    return row == lane


def product_stack(proj_ref, prm, taps, rims, count):
    key = featurize(proj_ref, prm, 1, taps, rims).astype(f32)
    value = featurize(proj_ref, prm, 2, taps, rims).astype(f32)
    product = (key * value).astype(bf16)
    stacked = jnp.concatenate(
        [product[:, b * BLOCK : (b + 1) * BLOCK] for b in range(count)], axis=0
    )
    return product, stacked


def masked_ends(stacked, w_hi_ref, w_lo_ref, rows, width, modes, count):
    ends = dot(stacked, w_hi_ref[0]) + dot(stacked, w_lo_ref[0])
    own = own_modes(rows, ends.shape[1], width, modes)
    return [jnp.where(own, ends[b * rows : (b + 1) * rows], 0.0) for b in range(count)], own


def state_kernel(width, modes, proj_ref, prm_ref, lam_ref, out_ref):
    rows, length = proj_ref.shape[1], proj_ref.shape[2]
    prm = prm_ref[...]
    key = featurize(proj_ref, prm, 1, 3, 9).astype(f32)
    value = featurize(proj_ref, prm, 2, 3, 9).astype(f32)
    product = (key * value).astype(bf16)
    lam = lam_ref[0][0:1, :]
    lanes = lam.shape[1]
    span = (length - 1 - lax.broadcasted_iota(jnp.int32, (length, lanes), 0)).astype(f32)
    w_hi, w_lo = split2(jnp.exp(-lam * span))
    ends = dot(product, w_hi) + dot(product, w_lo)
    own = own_modes(rows, lanes, width, modes)
    out_ref[...] = exact_dot(jnp.where(own, ends, 0.0), select_matrix(lanes, modes))[:, :modes].astype(bf16)


def select_matrix(lanes, modes):
    mode = lax.broadcasted_iota(jnp.int32, (lanes, LANES), 0) % modes
    lane = lax.broadcasted_iota(jnp.int32, (lanes, LANES), 1)
    return (mode == lane).astype(bf16)


def spread_matrix(lanes, modes):
    lane = lax.broadcasted_iota(jnp.int32, (modes, lanes), 0)
    mode = lax.broadcasted_iota(jnp.int32, (modes, lanes), 1) % modes
    return (mode == lane).astype(bf16)


def columns(row):
    lanes = row.shape[1]
    diagonal = lax.broadcasted_iota(jnp.int32, (lanes, lanes), 0) == lax.broadcasted_iota(
        jnp.int32, (lanes, lanes), 1
    )
    spread = jnp.where(diagonal, jnp.broadcast_to(row, (lanes, lanes)), 0.0)
    return exact_dot(spread, jnp.ones((lanes, LANES), bf16))


def lead_table(rates, weights, first, count):
    wide = count // LANES
    rates = jnp.concatenate([rates] * wide, axis=1) if wide > 1 else rates
    weights = jnp.concatenate([weights] * wide, axis=1) if wide > 1 else weights
    lag = (first + lax.broadcasted_iota(jnp.int32, (rates.shape[0], count), 1)).astype(f32)
    return weights * jnp.exp(-rates * lag)


def local_kernel(
    width,
    modes,
    count,
    proj_ref,
    prm_ref,
    lam_ref,
    res_ref,
    u0_ref,
    q_ref,
):
    rows = proj_ref.shape[1]
    groups = rows // width
    taps = 3
    rims = 3 * taps
    skip_at = rims + 6
    prm = prm_ref[...]
    query = featurize(proj_ref, prm, 0, taps, rims)
    q_ref[...] = query
    key = featurize(proj_ref, prm, 1, taps, rims).astype(f32)
    value = featurize(proj_ref, prm, 2, taps, rims).astype(f32)
    product = (key * value).astype(bf16)
    stacked = jnp.concatenate(
        [product[:, b * BLOCK : (b + 1) * BLOCK] for b in range(count)], axis=0
    )
    lam = lam_ref[0][0:1, :]
    rates = columns(lam)
    weights = columns(lam_ref[0][1:2, :])
    lanes = lam.shape[1]
    span = (BLOCK - 1 - lax.broadcasted_iota(jnp.int32, (BLOCK, lanes), 0)).astype(f32)
    w_hi, w_lo = split2(jnp.exp(-lam * span))
    used = stacked[: (count - 1) * rows]
    ends = dot(used, w_hi) + dot(used, w_lo)
    own = own_modes(rows, lanes, width, modes)
    decay = jnp.exp(-lam * float(BLOCK))
    state = jnp.where(own, ends[0:rows], 0.0)
    entering = [state]
    for b in range(1, count - 1):
        state = decay * state + jnp.where(own, ends[b * rows : (b + 1) * rows], 0.0)
        entering.append(state)
    z_hi, z_lo = split2(jnp.concatenate(entering, axis=0))
    lead_hi, lead_lo = split2(lead_table(rates, weights, 1, BLOCK))
    far = dot(z_hi, lead_hi) + dot(z_hi, lead_lo) + dot(z_lo, lead_hi)
    member = lax.broadcasted_iota(jnp.int32, (groups, lanes), 0) == (
        lax.broadcasted_iota(jnp.int32, (groups, lanes), 1) // modes
    )
    taps_long = sum(dot(member.astype(bf16), part) for part in split3(lead_table(rates, weights, 0, BLOCK)))

    s_idx = lax.broadcasted_iota(jnp.int32, (BLOCK, BLOCK), 0)
    t_idx = lax.broadcasted_iota(jnp.int32, (BLOCK, BLOCK), 1)
    pieces = [[None] * groups for _ in range(count)]
    for g in range(groups):
        lhs = jnp.concatenate(
            [stacked[b * rows + g * width : b * rows + (g + 1) * width] for b in range(count)],
            axis=0,
        )
        row = taps_long[g : g + 1, :]
        toeplitz = pltpu.roll(jnp.broadcast_to(row, (BLOCK, BLOCK)), 0, 1, stride=1, stride_axis=0)
        toeplitz = jnp.where(t_idx >= s_idx, toeplitz, 0.0)
        t_hi, t_lo = split2(toeplitz)
        near = dot(lhs, t_hi) + dot(lhs, t_lo)
        for b in range(count):
            pieces[b][g] = near[b * width : (b + 1) * width]
    long_term = jnp.concatenate(
        [
            jnp.concatenate(pieces[b], axis=0) + (far[(b - 1) * rows : b * rows] if b else 0.0)
            for b in range(count)
        ],
        axis=1,
    )
    signal = product.astype(f32)
    skip_b = jnp.concatenate([column(prm, skip_at, rows)] * (signal.shape[1] // LANES), axis=1)
    mixed = query.astype(f32) * (long_term + skip_b * signal)
    u0_ref[...] = res_ref[...].astype(f32) + mixed


def finish_kernel(width, modes, u0_ref, q_ref, z_ref, lam_ref, upd_ref, sq_ref):
    rows, length = u0_ref.shape
    lam = lam_ref[0][0:1, :]
    lanes = lam.shape[1]
    spread = exact_dot(z_ref[...], spread_matrix(lanes, modes))
    own = own_modes(rows, lanes, width, modes)
    z_hi = jnp.where(own, spread, 0.0).astype(bf16)
    lead_hi, lead_lo = split2(lead_table(columns(lam), columns(lam_ref[0][1:2, :]), 1, length))
    far = dot(z_hi, lead_hi) + dot(z_hi, lead_lo)
    updated = u0_ref[...] + q_ref[...].astype(f32) * far
    upd_ref[...] = updated
    sq_ref[0] = jnp.sum(updated * updated, axis=0, keepdims=True)


def local(projections, short_filter, decay_rate, residue, skip, norm_gain, residual):
    channels, length = residual.shape
    groups, modes = decay_rate.shape
    width = channels // groups
    rim_len = short_filter.shape[2] - 1
    count = length // BLOCK
    chunk = 256 if channels % 256 == 0 else channels
    chunk_groups = chunk // width
    lanes = chunk_groups * modes
    steps = channels // chunk

    edge = projections[:, :, length - rim_len :].transpose(0, 2, 1)
    rim = shifted(edge, "ctx", 1)
    prm = jnp.concatenate(
        [
            short_filter.astype(f32).transpose(0, 2, 1).reshape(-1, channels),
            rim.astype(f32).reshape(-1, channels),
            skip[None, :],
        ],
        axis=0,
    )
    prm = jnp.pad(prm, ((0, LANES - prm.shape[0]), (0, 0))).T

    scaled = residue * jnp.sqrt(-jnp.expm1(-2.0 * decay_rate))
    lam = jnp.stack([decay_rate.reshape(steps, lanes), scaled.reshape(steps, lanes)], axis=1)

    proj_spec = pl.BlockSpec((3, chunk, length), lambda i: (0, i, 0))
    prm_spec = pl.BlockSpec((chunk, LANES), lambda i: (i, 0))
    lam_spec = pl.BlockSpec((1, 2, lanes), lambda i: (i, 0, 0))
    row_spec = pl.BlockSpec((chunk, length), lambda i: (i, 0))
    state_spec = pl.BlockSpec((chunk, modes), lambda i: (i, 0))

    end_state = pl.pallas_call(
        functools.partial(state_kernel, width, modes),
        grid=(steps,),
        in_specs=[proj_spec, prm_spec, lam_spec],
        out_specs=state_spec,
        out_shape=jax.ShapeDtypeStruct((channels, modes), bf16),
    )(projections, prm, lam)

    size = lax.axis_size("ctx")
    dense = end_state.reshape(channels * modes // 128, 128)
    rate = jnp.repeat(decay_rate, width, axis=0).reshape(dense.shape)
    incoming = incoming_state(dense, rate * length, size).reshape(channels, modes)

    u0, query = pl.pallas_call(
        functools.partial(local_kernel, width, modes, count),
        grid=(steps,),
        in_specs=[proj_spec, prm_spec, lam_spec, row_spec],
        out_specs=[row_spec, row_spec],
        out_shape=[
            jax.ShapeDtypeStruct((channels, length), f32),
            jax.ShapeDtypeStruct((channels, length), bf16),
        ],
    )(projections, prm, lam, residual)

    updated, sq = pl.pallas_call(
        functools.partial(finish_kernel, width, modes),
        grid=(steps,),
        in_specs=[row_spec, row_spec, state_spec, lam_spec],
        out_specs=[row_spec, pl.BlockSpec((1, 1, length), lambda i: (i, 0, 0))],
        out_shape=[
            jax.ShapeDtypeStruct((channels, length), f32),
            jax.ShapeDtypeStruct((steps, 1, length), f32),
        ],
    )(u0, query, incoming, lam)
    squares = lax.psum(jnp.sum(sq, axis=(0, 1)), "tp")
    return (updated * lax.rsqrt(squares / D + epsilon)[None, :] * norm_gain[:, None]).astype(bf16)


def solution(mesh):
    placed = (
        P(None, "tp", "ctx"),
        P(None, "tp", None),
        P("tp", None),
        P("tp", None),
        P("tp"),
        P("tp"),
        P("tp", "ctx"),
    )
    return jax.shard_map(
        local, mesh=mesh, in_specs=placed, out_specs=P("tp", "ctx"), check_vma=False
    )
```

```python
import functools

import jax
import jax.numpy as jnp
from jax import lax
from jax.experimental import pallas as pl
from jax.experimental.pallas import tpu as pltpu
from jax.sharding import PartitionSpec as P

D = 8192
epsilon = 1e-06
BLOCK = 128
LANES = 128
f32 = jnp.float32
bf16 = jnp.bfloat16


def shifted(shard, axis, by):
    size = lax.axis_size(axis)
    pairs = [(i, i + by) for i in range(size) if 0 <= i + by < size]
    return lax.ppermute(shard, axis, pairs)


def incoming_state(ends, span_rate, size):
    place = lax.axis_index("ctx")
    copies = jnp.broadcast_to(ends[None], (size,) + ends.shape)
    gathered = lax.all_to_all(copies, "ctx", 0, 0).astype(f32)
    earlier = jnp.arange(size, dtype=jnp.int32)
    gap = jnp.maximum(place - 1 - earlier, 0).astype(f32)
    weight = jnp.where(
        (earlier < place)[:, None, None],
        jnp.exp(-span_rate[None] * gap[:, None, None]),
        0.0,
    )
    return jnp.sum(weight * gathered, axis=0)


def split2(a):
    hi = a.astype(bf16)
    lo = (a - hi.astype(f32)).astype(bf16)
    return hi, lo


def split3(a):
    hi = a.astype(bf16)
    rest = a - hi.astype(f32)
    mid = rest.astype(bf16)
    lo = (rest - mid.astype(f32)).astype(bf16)
    return hi, mid, lo


def dot(a, b):
    return jnp.dot(a, b, preferred_element_type=f32)


def exact_dot(a, select):
    return sum(dot(part, select) for part in split3(a))


def column(prm, k, rows):
    return jnp.broadcast_to(prm[:, k : k + 1], (rows, LANES))


def featurize(proj_ref, prm, p, taps, rims):
    rows, length = proj_ref.shape[1], proj_ref.shape[2]
    t = taps * p
    weights = [column(prm, t + k, rows) for k in range(3)]
    back2 = column(prm, rims + 2 * p, rows)
    back1 = column(prm, rims + 2 * p + 1, rows)
    lane = lax.broadcasted_iota(jnp.int32, (rows, LANES), 1)
    tiles = [proj_ref[p, :, j * LANES : (j + 1) * LANES].astype(f32) for j in range(length // LANES)]
    once = [pltpu.roll(x, 1, 1) for x in tiles]
    twice = [pltpu.roll(x, 2, 1) for x in tiles]
    out = []
    for j, x in enumerate(tiles):
        if j == 0:
            x1 = jnp.where(lane == 0, back1, once[0])
            x2 = jnp.where(lane == 0, back2, jnp.where(lane == 1, back1, twice[0]))
        else:
            x1 = jnp.where(lane == 0, once[j - 1], once[j])
            x2 = jnp.where(lane < 2, twice[j - 1], twice[j])
        summed = weights[0] * x + weights[1] * x1
        summed = summed + weights[2] * x2
        out.append(summed.astype(bf16))
    return jnp.concatenate(out, axis=1)


def own_modes(rows, lanes, width, modes):
    row = lax.broadcasted_iota(jnp.int32, (rows, lanes), 0) // width
    lane = lax.broadcasted_iota(jnp.int32, (rows, lanes), 1) // modes
    return row == lane


def product_stack(proj_ref, prm, taps, rims, count):
    key = featurize(proj_ref, prm, 1, taps, rims).astype(f32)
    value = featurize(proj_ref, prm, 2, taps, rims).astype(f32)
    product = (key * value).astype(bf16)
    stacked = jnp.concatenate(
        [product[:, b * BLOCK : (b + 1) * BLOCK] for b in range(count)], axis=0
    )
    return product, stacked


def masked_ends(stacked, w_hi_ref, w_lo_ref, rows, width, modes, count):
    ends = dot(stacked, w_hi_ref[0]) + dot(stacked, w_lo_ref[0])
    own = own_modes(rows, ends.shape[1], width, modes)
    return [jnp.where(own, ends[b * rows : (b + 1) * rows], 0.0) for b in range(count)], own


def state_kernel(width, modes, proj_ref, prm_ref, lam_ref, out_ref, x_ref):
    rows, length = proj_ref.shape[1], proj_ref.shape[2]
    prm = prm_ref[...]
    key = featurize(proj_ref, prm, 1, 3, 9).astype(f32)
    value = featurize(proj_ref, prm, 2, 3, 9).astype(f32)
    product = (key * value).astype(bf16)
    x_ref[...] = product
    lam = lam_ref[0][0:1, :]
    lanes = lam.shape[1]
    span = (length - 1 - lax.broadcasted_iota(jnp.int32, (length, lanes), 0)).astype(f32)
    w_hi, w_lo = split2(jnp.exp(-lam * span))
    ends = dot(product, w_hi) + dot(product, w_lo)
    own = own_modes(rows, lanes, width, modes)
    out_ref[...] = exact_dot(jnp.where(own, ends, 0.0), select_matrix(lanes, modes))[:, :modes].astype(bf16)


def select_matrix(lanes, modes):
    mode = lax.broadcasted_iota(jnp.int32, (lanes, LANES), 0) % modes
    lane = lax.broadcasted_iota(jnp.int32, (lanes, LANES), 1)
    return (mode == lane).astype(bf16)


def spread_matrix(lanes, modes):
    lane = lax.broadcasted_iota(jnp.int32, (modes, lanes), 0)
    mode = lax.broadcasted_iota(jnp.int32, (modes, lanes), 1) % modes
    return (mode == lane).astype(bf16)


def columns(row):
    lanes = row.shape[1]
    diagonal = lax.broadcasted_iota(jnp.int32, (lanes, lanes), 0) == lax.broadcasted_iota(
        jnp.int32, (lanes, lanes), 1
    )
    spread = jnp.where(diagonal, jnp.broadcast_to(row, (lanes, lanes)), 0.0)
    return exact_dot(spread, jnp.ones((lanes, LANES), bf16))


def lead_table(rates, weights, first, count):
    wide = count // LANES
    rates = jnp.concatenate([rates] * wide, axis=1) if wide > 1 else rates
    weights = jnp.concatenate([weights] * wide, axis=1) if wide > 1 else weights
    lag = (first + lax.broadcasted_iota(jnp.int32, (rates.shape[0], count), 1)).astype(f32)
    return weights * jnp.exp(-rates * lag)


def local_kernel(
    width,
    modes,
    count,
    proj_ref,
    x_ref,
    prm_ref,
    lam_ref,
    res_ref,
    u0_ref,
    q_ref,
):
    rows = proj_ref.shape[1]
    groups = rows // width
    taps = 3
    rims = 3 * taps
    skip_at = rims + 6
    prm = prm_ref[...]
    query = featurize(proj_ref, prm, 0, taps, rims)
    q_ref[...] = query
    product = x_ref[...]
    stacked = jnp.concatenate(
        [product[:, b * BLOCK : (b + 1) * BLOCK] for b in range(count)], axis=0
    )
    lam = lam_ref[0][0:1, :]
    rates = columns(lam)
    weights = columns(lam_ref[0][1:2, :])
    lanes = lam.shape[1]
    span = (BLOCK - 1 - lax.broadcasted_iota(jnp.int32, (BLOCK, lanes), 0)).astype(f32)
    w_hi, w_lo = split2(jnp.exp(-lam * span))
    used = stacked[: (count - 1) * rows]
    ends = dot(used, w_hi) + dot(used, w_lo)
    own = own_modes(rows, lanes, width, modes)
    decay = jnp.exp(-lam * float(BLOCK))
    state = jnp.where(own, ends[0:rows], 0.0)
    entering = [state]
    for b in range(1, count - 1):
        state = decay * state + jnp.where(own, ends[b * rows : (b + 1) * rows], 0.0)
        entering.append(state)
    z_hi, z_lo = split2(jnp.concatenate(entering, axis=0))
    lead_hi, lead_lo = split2(lead_table(rates, weights, 1, BLOCK))
    far = dot(z_hi, lead_hi) + dot(z_hi, lead_lo) + dot(z_lo, lead_hi)
    member = lax.broadcasted_iota(jnp.int32, (groups, lanes), 0) == (
        lax.broadcasted_iota(jnp.int32, (groups, lanes), 1) // modes
    )
    taps_long = sum(dot(member.astype(bf16), part) for part in split3(lead_table(rates, weights, 0, BLOCK)))

    s_idx = lax.broadcasted_iota(jnp.int32, (BLOCK, BLOCK), 0)
    t_idx = lax.broadcasted_iota(jnp.int32, (BLOCK, BLOCK), 1)
    pieces = [[None] * groups for _ in range(count)]
    for g in range(groups):
        lhs = jnp.concatenate(
            [stacked[b * rows + g * width : b * rows + (g + 1) * width] for b in range(count)],
            axis=0,
        )
        row = taps_long[g : g + 1, :]
        toeplitz = pltpu.roll(jnp.broadcast_to(row, (BLOCK, BLOCK)), 0, 1, stride=1, stride_axis=0)
        toeplitz = jnp.where(t_idx >= s_idx, toeplitz, 0.0)
        t_hi, t_lo = split2(toeplitz)
        near = dot(lhs, t_hi) + dot(lhs, t_lo)
        for b in range(count):
            pieces[b][g] = near[b * width : (b + 1) * width]
    long_term = jnp.concatenate(
        [
            jnp.concatenate(pieces[b], axis=0) + (far[(b - 1) * rows : b * rows] if b else 0.0)
            for b in range(count)
        ],
        axis=1,
    )
    signal = product.astype(f32)
    skip_b = jnp.concatenate([column(prm, skip_at, rows)] * (signal.shape[1] // LANES), axis=1)
    mixed = query.astype(f32) * (long_term + skip_b * signal)
    u0_ref[...] = res_ref[...].astype(f32) + mixed


def finish_kernel(width, modes, u0_ref, q_ref, z_ref, lam_ref, upd_ref, sq_ref):
    rows, length = u0_ref.shape
    lam = lam_ref[0][0:1, :]
    lanes = lam.shape[1]
    spread = exact_dot(z_ref[...], spread_matrix(lanes, modes))
    own = own_modes(rows, lanes, width, modes)
    z_hi = jnp.where(own, spread, 0.0).astype(bf16)
    lead_hi, lead_lo = split2(lead_table(columns(lam), columns(lam_ref[0][1:2, :]), 1, length))
    far = dot(z_hi, lead_hi) + dot(z_hi, lead_lo)
    updated = u0_ref[...] + q_ref[...].astype(f32) * far
    upd_ref[...] = updated
    sq_ref[0] = jnp.sum(updated * updated, axis=0, keepdims=True)


def local(projections, short_filter, decay_rate, residue, skip, norm_gain, residual):
    channels, length = residual.shape
    groups, modes = decay_rate.shape
    width = channels // groups
    rim_len = short_filter.shape[2] - 1
    count = length // BLOCK
    chunk = 256 if channels % 256 == 0 else channels
    chunk_groups = chunk // width
    lanes = chunk_groups * modes
    steps = channels // chunk

    edge = projections[:, :, length - rim_len :].transpose(0, 2, 1)
    rim = shifted(edge, "ctx", 1)
    prm = jnp.concatenate(
        [
            short_filter.astype(f32).transpose(0, 2, 1).reshape(-1, channels),
            rim.astype(f32).reshape(-1, channels),
            skip[None, :],
        ],
        axis=0,
    )
    prm = jnp.pad(prm, ((0, LANES - prm.shape[0]), (0, 0))).T

    scaled = residue * jnp.sqrt(-jnp.expm1(-2.0 * decay_rate))
    lam = jnp.stack([decay_rate.reshape(steps, lanes), scaled.reshape(steps, lanes)], axis=1)

    proj_spec = pl.BlockSpec((3, chunk, length), lambda i: (0, i, 0))
    query_spec = pl.BlockSpec((1, chunk, length), lambda i: (0, i, 0))
    prm_spec = pl.BlockSpec((chunk, LANES), lambda i: (i, 0))
    lam_spec = pl.BlockSpec((1, 2, lanes), lambda i: (i, 0, 0))
    row_spec = pl.BlockSpec((chunk, length), lambda i: (i, 0))
    state_spec = pl.BlockSpec((chunk, modes), lambda i: (i, 0))

    end_state, product = pl.pallas_call(
        functools.partial(state_kernel, width, modes),
        grid=(steps,),
        in_specs=[proj_spec, prm_spec, lam_spec],
        out_specs=[state_spec, row_spec],
        out_shape=[
            jax.ShapeDtypeStruct((channels, modes), bf16),
            jax.ShapeDtypeStruct((channels, length), bf16),
        ],
    )(projections, prm, lam)

    size = lax.axis_size("ctx")
    dense = end_state.reshape(channels * modes // 128, 128)
    rate = jnp.repeat(decay_rate, width, axis=0).reshape(dense.shape)
    incoming = incoming_state(dense, rate * length, size).reshape(channels, modes)

    u0, query = pl.pallas_call(
        functools.partial(local_kernel, width, modes, count),
        grid=(steps,),
        in_specs=[query_spec, row_spec, prm_spec, lam_spec, row_spec],
        out_specs=[row_spec, row_spec],
        out_shape=[
            jax.ShapeDtypeStruct((channels, length), f32),
            jax.ShapeDtypeStruct((channels, length), bf16),
        ],
    )(projections, product, prm, lam, residual)

    updated, sq = pl.pallas_call(
        functools.partial(finish_kernel, width, modes),
        grid=(steps,),
        in_specs=[row_spec, row_spec, state_spec, lam_spec],
        out_specs=[row_spec, pl.BlockSpec((1, 1, length), lambda i: (i, 0, 0))],
        out_shape=[
            jax.ShapeDtypeStruct((channels, length), f32),
            jax.ShapeDtypeStruct((steps, 1, length), f32),
        ],
    )(u0, query, incoming, lam)
    squares = lax.psum(jnp.sum(sq, axis=(0, 1)), "tp")
    return (updated * lax.rsqrt(squares / D + epsilon)[None, :] * norm_gain[:, None]).astype(bf16)


def solution(mesh):
    placed = (
        P(None, "tp", "ctx"),
        P(None, "tp", None),
        P("tp", None),
        P("tp", None),
        P("tp"),
        P("tp"),
        P("tp", "ctx"),
    )
    return jax.shard_map(
        local, mesh=mesh, in_specs=placed, out_specs=P("tp", "ctx"), check_vma=False
    )
```

```python
import functools

import jax
import jax.numpy as jnp
from jax import lax
from jax.experimental import pallas as pl
from jax.experimental.pallas import tpu as pltpu
from jax.sharding import PartitionSpec as P

D = 8192
epsilon = 1e-06
BLOCK = 128
LANES = 128
f32 = jnp.float32
bf16 = jnp.bfloat16


def shifted(shard, axis, by):
    size = lax.axis_size(axis)
    pairs = [(i, i + by) for i in range(size) if 0 <= i + by < size]
    return lax.ppermute(shard, axis, pairs)


def incoming_state(ends, span_rate, size):
    place = lax.axis_index("ctx")
    copies = jnp.broadcast_to(ends[None], (size,) + ends.shape)
    gathered = lax.all_to_all(copies, "ctx", 0, 0).astype(f32)
    earlier = jnp.arange(size, dtype=jnp.int32)
    gap = jnp.maximum(place - 1 - earlier, 0).astype(f32)
    weight = jnp.where(
        (earlier < place)[:, None, None],
        jnp.exp(-span_rate[None] * gap[:, None, None]),
        0.0,
    )
    return jnp.sum(weight * gathered, axis=0)


def split2(a):
    hi = a.astype(bf16)
    lo = (a - hi.astype(f32)).astype(bf16)
    return hi, lo


def split3(a):
    hi = a.astype(bf16)
    rest = a - hi.astype(f32)
    mid = rest.astype(bf16)
    lo = (rest - mid.astype(f32)).astype(bf16)
    return hi, mid, lo


def dot(a, b):
    return jnp.dot(a, b, preferred_element_type=f32)


def exact_dot(a, select):
    return sum(dot(part, select) for part in split3(a))


def column(prm, k, rows):
    return jnp.broadcast_to(prm[:, k : k + 1], (rows, LANES))


def featurize(proj_ref, prm, p, taps, rims):
    rows, length = proj_ref.shape[1], proj_ref.shape[2]
    t = taps * p
    weights = [column(prm, t + k, rows) for k in range(3)]
    back2 = column(prm, rims + 2 * p, rows)
    back1 = column(prm, rims + 2 * p + 1, rows)
    lane = lax.broadcasted_iota(jnp.int32, (rows, LANES), 1)
    tiles = [proj_ref[p, :, j * LANES : (j + 1) * LANES].astype(f32) for j in range(length // LANES)]
    once = [pltpu.roll(x, 1, 1) for x in tiles]
    twice = [pltpu.roll(x, 2, 1) for x in tiles]
    out = []
    for j, x in enumerate(tiles):
        if j == 0:
            x1 = jnp.where(lane == 0, back1, once[0])
            x2 = jnp.where(lane == 0, back2, jnp.where(lane == 1, back1, twice[0]))
        else:
            x1 = jnp.where(lane == 0, once[j - 1], once[j])
            x2 = jnp.where(lane < 2, twice[j - 1], twice[j])
        summed = weights[0] * x + weights[1] * x1
        summed = summed + weights[2] * x2
        out.append(summed.astype(bf16))
    return jnp.concatenate(out, axis=1)


def own_modes(rows, lanes, width, modes):
    row = lax.broadcasted_iota(jnp.int32, (rows, lanes), 0) // width
    lane = lax.broadcasted_iota(jnp.int32, (rows, lanes), 1) // modes
    return row == lane


def product_stack(proj_ref, prm, taps, rims, count):
    key = featurize(proj_ref, prm, 1, taps, rims).astype(f32)
    value = featurize(proj_ref, prm, 2, taps, rims).astype(f32)
    product = (key * value).astype(bf16)
    stacked = jnp.concatenate(
        [product[:, b * BLOCK : (b + 1) * BLOCK] for b in range(count)], axis=0
    )
    return product, stacked


def masked_ends(stacked, w_hi_ref, w_lo_ref, rows, width, modes, count):
    ends = dot(stacked, w_hi_ref[0]) + dot(stacked, w_lo_ref[0])
    own = own_modes(rows, ends.shape[1], width, modes)
    return [jnp.where(own, ends[b * rows : (b + 1) * rows], 0.0) for b in range(count)], own


def state_kernel(width, modes, proj_ref, prm_ref, lam_ref, out_ref, x_ref):
    rows, length = proj_ref.shape[1], proj_ref.shape[2]
    prm = prm_ref[...]
    key = featurize(proj_ref, prm, 1, 3, 9).astype(f32)
    value = featurize(proj_ref, prm, 2, 3, 9).astype(f32)
    product = (key * value).astype(bf16)
    x_ref[...] = product
    lam = lam_ref[0][0:1, :]
    lanes = lam.shape[1]
    span = (BLOCK - 1 - lax.broadcasted_iota(jnp.int32, (BLOCK, lanes), 0)).astype(f32)
    within = jnp.exp(-lam * span)
    blocks = length // BLOCK
    table = jnp.concatenate(
        [within * jnp.exp(-lam * float(BLOCK * (blocks - 1 - b))) for b in range(blocks)], axis=0
    )
    w_hi, w_lo = split2(table)
    ends = dot(product, w_hi) + dot(product, w_lo)
    own = own_modes(rows, lanes, width, modes)
    picked = jnp.where(own, ends, 0.0).astype(bf16)
    out_ref[...] = dot(picked, select_matrix(lanes, modes))[:, :modes].astype(bf16)


def select_matrix(lanes, modes):
    mode = lax.broadcasted_iota(jnp.int32, (lanes, LANES), 0) % modes
    lane = lax.broadcasted_iota(jnp.int32, (lanes, LANES), 1)
    return (mode == lane).astype(bf16)


def spread_matrix(lanes, modes):
    lane = lax.broadcasted_iota(jnp.int32, (modes, lanes), 0)
    mode = lax.broadcasted_iota(jnp.int32, (modes, lanes), 1) % modes
    return (mode == lane).astype(bf16)


def columns(row):
    lanes = row.shape[1]
    diagonal = lax.broadcasted_iota(jnp.int32, (lanes, lanes), 0) == lax.broadcasted_iota(
        jnp.int32, (lanes, lanes), 1
    )
    spread = jnp.where(diagonal, jnp.broadcast_to(row, (lanes, lanes)), 0.0)
    return exact_dot(spread, jnp.ones((lanes, LANES), bf16))


def lead_table(rates, weights, first, count):
    wide = count // LANES
    rates = jnp.concatenate([rates] * wide, axis=1) if wide > 1 else rates
    weights = jnp.concatenate([weights] * wide, axis=1) if wide > 1 else weights
    lag = (first + lax.broadcasted_iota(jnp.int32, (rates.shape[0], count), 1)).astype(f32)
    return weights * jnp.exp(-rates * lag)


def local_kernel(
    width,
    modes,
    count,
    proj_ref,
    x_ref,
    prm_ref,
    lam_ref,
    res_ref,
    u0_ref,
    q_ref,
):
    rows = proj_ref.shape[1]
    groups = rows // width
    taps = 3
    rims = 3 * taps
    skip_at = rims + 6
    prm = prm_ref[...]
    query = featurize(proj_ref, prm, 0, taps, rims)
    q_ref[...] = query
    product = x_ref[...]
    stacked = jnp.concatenate(
        [product[:, b * BLOCK : (b + 1) * BLOCK] for b in range(count)], axis=0
    )
    lam = lam_ref[0][0:1, :]
    rates = columns(lam)
    weights = columns(lam_ref[0][1:2, :])
    lanes = lam.shape[1]
    span = (BLOCK - 1 - lax.broadcasted_iota(jnp.int32, (BLOCK, lanes), 0)).astype(f32)
    w_hi, w_lo = split2(jnp.exp(-lam * span))
    used = stacked[: (count - 1) * rows]
    ends = dot(used, w_hi) + dot(used, w_lo)
    own = own_modes(rows, lanes, width, modes)
    decay = jnp.exp(-lam * float(BLOCK))
    state = jnp.where(own, ends[0:rows], 0.0)
    entering = [state]
    for b in range(1, count - 1):
        state = decay * state + jnp.where(own, ends[b * rows : (b + 1) * rows], 0.0)
        entering.append(state)
    z_hi, z_lo = split2(jnp.concatenate(entering, axis=0))
    lead_hi, lead_lo = split2(lead_table(rates, weights, 1, BLOCK))
    far = dot(z_hi, lead_hi) + dot(z_hi, lead_lo) + dot(z_lo, lead_hi)
    member = lax.broadcasted_iota(jnp.int32, (groups, lanes), 0) == (
        lax.broadcasted_iota(jnp.int32, (groups, lanes), 1) // modes
    )
    taps_long = sum(dot(member.astype(bf16), part) for part in split3(lead_table(rates, weights, 0, BLOCK)))

    s_idx = lax.broadcasted_iota(jnp.int32, (BLOCK, BLOCK), 0)
    t_idx = lax.broadcasted_iota(jnp.int32, (BLOCK, BLOCK), 1)
    pieces = [[None] * groups for _ in range(count)]
    for g in range(groups):
        lhs = jnp.concatenate(
            [stacked[b * rows + g * width : b * rows + (g + 1) * width] for b in range(count)],
            axis=0,
        )
        row = taps_long[g : g + 1, :]
        toeplitz = pltpu.roll(jnp.broadcast_to(row, (BLOCK, BLOCK)), 0, 1, stride=1, stride_axis=0)
        toeplitz = jnp.where(t_idx >= s_idx, toeplitz, 0.0)
        t_hi, t_lo = split2(toeplitz)
        near = dot(lhs, t_hi) + dot(lhs, t_lo)
        for b in range(count):
            pieces[b][g] = near[b * width : (b + 1) * width]
    long_term = jnp.concatenate(
        [
            jnp.concatenate(pieces[b], axis=0) + (far[(b - 1) * rows : b * rows] if b else 0.0)
            for b in range(count)
        ],
        axis=1,
    )
    signal = product.astype(f32)
    skip_b = jnp.concatenate([column(prm, skip_at, rows)] * (signal.shape[1] // LANES), axis=1)
    mixed = query.astype(f32) * (long_term + skip_b * signal)
    u0_ref[...] = res_ref[...].astype(f32) + mixed


def finish_kernel(width, modes, u0_ref, q_ref, z_ref, lam_ref, upd_ref, sq_ref):
    rows, length = u0_ref.shape
    lam = lam_ref[0][0:1, :]
    lanes = lam.shape[1]
    spread = exact_dot(z_ref[...], spread_matrix(lanes, modes))
    own = own_modes(rows, lanes, width, modes)
    z_hi = jnp.where(own, spread, 0.0).astype(bf16)
    lead_hi, lead_lo = split2(lead_table(columns(lam), columns(lam_ref[0][1:2, :]), 1, length))
    far = dot(z_hi, lead_hi) + dot(z_hi, lead_lo)
    updated = u0_ref[...] + q_ref[...].astype(f32) * far
    upd_ref[...] = updated
    sq_ref[0] = jnp.sum(updated * updated, axis=0, keepdims=True)


def local(projections, short_filter, decay_rate, residue, skip, norm_gain, residual):
    channels, length = residual.shape
    groups, modes = decay_rate.shape
    width = channels // groups
    rim_len = short_filter.shape[2] - 1
    count = length // BLOCK
    chunk = 256 if channels % 256 == 0 else channels
    chunk_groups = chunk // width
    lanes = chunk_groups * modes
    steps = channels // chunk

    edge = projections[:, :, length - rim_len :].transpose(0, 2, 1)
    rim = shifted(edge, "ctx", 1)
    prm = jnp.concatenate(
        [
            short_filter.astype(f32).transpose(0, 2, 1).reshape(-1, channels),
            rim.astype(f32).reshape(-1, channels),
            skip[None, :],
        ],
        axis=0,
    )
    prm = jnp.pad(prm, ((0, LANES - prm.shape[0]), (0, 0))).T

    scaled = residue * jnp.sqrt(-jnp.expm1(-2.0 * decay_rate))
    lam = jnp.stack([decay_rate.reshape(steps, lanes), scaled.reshape(steps, lanes)], axis=1)

    proj_spec = pl.BlockSpec((3, chunk, length), lambda i: (0, i, 0))
    query_spec = pl.BlockSpec((1, chunk, length), lambda i: (0, i, 0))
    prm_spec = pl.BlockSpec((chunk, LANES), lambda i: (i, 0))
    lam_spec = pl.BlockSpec((1, 2, lanes), lambda i: (i, 0, 0))
    row_spec = pl.BlockSpec((chunk, length), lambda i: (i, 0))
    state_spec = pl.BlockSpec((chunk, modes), lambda i: (i, 0))

    end_state, product = pl.pallas_call(
        functools.partial(state_kernel, width, modes),
        grid=(steps,),
        in_specs=[proj_spec, prm_spec, lam_spec],
        out_specs=[state_spec, row_spec],
        out_shape=[
            jax.ShapeDtypeStruct((channels, modes), bf16),
            jax.ShapeDtypeStruct((channels, length), bf16),
        ],
    )(projections, prm, lam)

    size = lax.axis_size("ctx")
    dense = end_state.reshape(channels * modes // 128, 128)
    rate = jnp.repeat(decay_rate, width, axis=0).reshape(dense.shape)
    incoming = incoming_state(dense, rate * length, size).reshape(channels, modes)

    u0, query = pl.pallas_call(
        functools.partial(local_kernel, width, modes, count),
        grid=(steps,),
        in_specs=[query_spec, row_spec, prm_spec, lam_spec, row_spec],
        out_specs=[row_spec, row_spec],
        out_shape=[
            jax.ShapeDtypeStruct((channels, length), f32),
            jax.ShapeDtypeStruct((channels, length), bf16),
        ],
    )(projections, product, prm, lam, residual)

    updated, sq = pl.pallas_call(
        functools.partial(finish_kernel, width, modes),
        grid=(steps,),
        in_specs=[row_spec, row_spec, state_spec, lam_spec],
        out_specs=[row_spec, pl.BlockSpec((1, 1, length), lambda i: (i, 0, 0))],
        out_shape=[
            jax.ShapeDtypeStruct((channels, length), f32),
            jax.ShapeDtypeStruct((steps, 1, length), f32),
        ],
    )(u0, query, incoming, lam)
    squares = lax.psum(jnp.sum(sq, axis=(0, 1)), "tp")
    return (updated * lax.rsqrt(squares / D + epsilon)[None, :] * norm_gain[:, None]).astype(bf16)


def solution(mesh):
    placed = (
        P(None, "tp", "ctx"),
        P(None, "tp", None),
        P("tp", None),
        P("tp", None),
        P("tp"),
        P("tp"),
        P("tp", "ctx"),
    )
    return jax.shard_map(
        local, mesh=mesh, in_specs=placed, out_specs=P("tp", "ctx"), check_vma=False
    )
```

```python
import functools

import jax
import jax.numpy as jnp
from jax import lax
from jax.experimental import pallas as pl
from jax.experimental.pallas import tpu as pltpu
from jax.sharding import PartitionSpec as P

D = 8192
epsilon = 1e-06
BLOCK = 128
LANES = 128
f32 = jnp.float32
bf16 = jnp.bfloat16


def shifted(shard, axis, by):
    size = lax.axis_size(axis)
    pairs = [(i, i + by) for i in range(size) if 0 <= i + by < size]
    return lax.ppermute(shard, axis, pairs)


def incoming_state(ends, span_rate, size):
    place = lax.axis_index("ctx")
    copies = jnp.broadcast_to(ends[None], (size,) + ends.shape)
    gathered = lax.all_to_all(copies, "ctx", 0, 0).astype(f32)
    earlier = jnp.arange(size, dtype=jnp.int32)
    gap = jnp.maximum(place - 1 - earlier, 0).astype(f32)
    weight = jnp.where(
        (earlier < place)[:, None, None],
        jnp.exp(-span_rate[None] * gap[:, None, None]),
        0.0,
    )
    return jnp.sum(weight * gathered, axis=0)


def split2(a):
    hi = a.astype(bf16)
    lo = (a - hi.astype(f32)).astype(bf16)
    return hi, lo


def split3(a):
    hi = a.astype(bf16)
    rest = a - hi.astype(f32)
    mid = rest.astype(bf16)
    lo = (rest - mid.astype(f32)).astype(bf16)
    return hi, mid, lo


def dot(a, b):
    return jnp.dot(a, b, preferred_element_type=f32)


def exact_dot(a, select):
    return sum(dot(part, select) for part in split3(a))


def column(prm, k, rows):
    return jnp.broadcast_to(prm[:, k : k + 1], (rows, LANES))


def featurize(proj_ref, prm, p, taps, rims):
    rows, length = proj_ref.shape[1], proj_ref.shape[2]
    t = taps * p
    weights = [column(prm, t + k, rows) for k in range(3)]
    back2 = column(prm, rims + 2 * p, rows)
    back1 = column(prm, rims + 2 * p + 1, rows)
    lane = lax.broadcasted_iota(jnp.int32, (rows, LANES), 1)
    tiles = [proj_ref[p, :, j * LANES : (j + 1) * LANES].astype(f32) for j in range(length // LANES)]
    once = [pltpu.roll(x, 1, 1) for x in tiles]
    twice = [pltpu.roll(x, 2, 1) for x in tiles]
    out = []
    for j, x in enumerate(tiles):
        if j == 0:
            x1 = jnp.where(lane == 0, back1, once[0])
            x2 = jnp.where(lane == 0, back2, jnp.where(lane == 1, back1, twice[0]))
        else:
            x1 = jnp.where(lane == 0, once[j - 1], once[j])
            x2 = jnp.where(lane < 2, twice[j - 1], twice[j])
        summed = weights[0] * x + weights[1] * x1
        summed = summed + weights[2] * x2
        out.append(summed.astype(bf16))
    return jnp.concatenate(out, axis=1)


def own_modes(rows, lanes, width, modes):
    row = lax.broadcasted_iota(jnp.int32, (rows, lanes), 0) // width
    lane = lax.broadcasted_iota(jnp.int32, (rows, lanes), 1) // modes
    return row == lane


def product_stack(proj_ref, prm, taps, rims, count):
    key = featurize(proj_ref, prm, 1, taps, rims).astype(f32)
    value = featurize(proj_ref, prm, 2, taps, rims).astype(f32)
    product = (key * value).astype(bf16)
    stacked = jnp.concatenate(
        [product[:, b * BLOCK : (b + 1) * BLOCK] for b in range(count)], axis=0
    )
    return product, stacked


def masked_ends(stacked, w_hi_ref, w_lo_ref, rows, width, modes, count):
    ends = dot(stacked, w_hi_ref[0]) + dot(stacked, w_lo_ref[0])
    own = own_modes(rows, ends.shape[1], width, modes)
    return [jnp.where(own, ends[b * rows : (b + 1) * rows], 0.0) for b in range(count)], own


def state_kernel(width, modes, proj_ref, prm_ref, lam_ref, out_ref, x_ref):
    rows, length = proj_ref.shape[1], proj_ref.shape[2]
    prm = prm_ref[...]
    key = featurize(proj_ref, prm, 1, 3, 9).astype(f32)
    value = featurize(proj_ref, prm, 2, 3, 9).astype(f32)
    product = (key * value).astype(bf16)
    x_ref[...] = product
    lam = lam_ref[0][0:1, :]
    lanes = lam.shape[1]
    span = (BLOCK - 1 - lax.broadcasted_iota(jnp.int32, (BLOCK, lanes), 0)).astype(f32)
    within = jnp.exp(-lam * span)
    blocks = length // BLOCK
    table = jnp.concatenate(
        [within * jnp.exp(-lam * float(BLOCK * (blocks - 1 - b))) for b in range(blocks)], axis=0
    )
    w_hi, w_lo = split2(table)
    ends = dot(product, w_hi) + dot(product, w_lo)
    own = own_modes(rows, lanes, width, modes)
    picked = jnp.where(own, ends, 0.0).astype(bf16)
    out_ref[...] = dot(picked, select_matrix(lanes, modes))[:, :modes].astype(bf16)


def select_matrix(lanes, modes):
    mode = lax.broadcasted_iota(jnp.int32, (lanes, LANES), 0) % modes
    lane = lax.broadcasted_iota(jnp.int32, (lanes, LANES), 1)
    return (mode == lane).astype(bf16)


def spread_matrix(lanes, modes):
    lane = lax.broadcasted_iota(jnp.int32, (modes, lanes), 0)
    mode = lax.broadcasted_iota(jnp.int32, (modes, lanes), 1) % modes
    return (mode == lane).astype(bf16)


def columns(row):
    lanes = row.shape[1]
    diagonal = lax.broadcasted_iota(jnp.int32, (lanes, lanes), 0) == lax.broadcasted_iota(
        jnp.int32, (lanes, lanes), 1
    )
    spread = jnp.where(diagonal, jnp.broadcast_to(row, (lanes, lanes)), 0.0)
    return exact_dot(spread, jnp.ones((lanes, LANES), bf16))


def lead_table(rates, weights, first, count):
    wide = count // LANES
    rates = jnp.concatenate([rates] * wide, axis=1) if wide > 1 else rates
    weights = jnp.concatenate([weights] * wide, axis=1) if wide > 1 else weights
    lag = (first + lax.broadcasted_iota(jnp.int32, (rates.shape[0], count), 1)).astype(f32)
    return weights * jnp.exp(-rates * lag)


def local_kernel(
    width,
    modes,
    count,
    proj_ref,
    x_ref,
    prm_ref,
    lam_ref,
    res_ref,
    u0_ref,
    q_ref,
):
    rows = proj_ref.shape[1]
    groups = rows // width
    taps = 3
    rims = 3 * taps
    skip_at = rims + 6
    prm = prm_ref[...]
    query = featurize(proj_ref, prm, 0, taps, rims)
    q_ref[...] = query
    product = x_ref[...]
    stacked = jnp.concatenate(
        [product[:, b * BLOCK : (b + 1) * BLOCK] for b in range(count)], axis=0
    )
    lam = lam_ref[0][0:1, :]
    rates = columns(lam)
    weights = columns(lam_ref[0][1:2, :])
    lanes = lam.shape[1]
    span = (BLOCK - 1 - lax.broadcasted_iota(jnp.int32, (BLOCK, lanes), 0)).astype(f32)
    w_hi, w_lo = split2(jnp.exp(-lam * span))
    used = stacked[: (count - 1) * rows]
    ends = dot(used, w_hi) + dot(used, w_lo)
    own = own_modes(rows, lanes, width, modes)
    decay = jnp.exp(-lam * float(BLOCK))
    state = jnp.where(own, ends[0:rows], 0.0)
    entering = [state]
    for b in range(1, count - 1):
        state = decay * state + jnp.where(own, ends[b * rows : (b + 1) * rows], 0.0)
        entering.append(state)
    z_hi, z_lo = split2(jnp.concatenate(entering, axis=0))
    lead_hi, lead_lo = split2(lead_table(rates, weights, 1, BLOCK))
    far = dot(z_hi, lead_hi) + dot(z_hi, lead_lo) + dot(z_lo, lead_hi)
    member = lax.broadcasted_iota(jnp.int32, (groups, lanes), 0) == (
        lax.broadcasted_iota(jnp.int32, (groups, lanes), 1) // modes
    )
    taps_long = sum(dot(member.astype(bf16), part) for part in split3(lead_table(rates, weights, 0, BLOCK)))

    s_idx = lax.broadcasted_iota(jnp.int32, (BLOCK, BLOCK), 0)
    t_idx = lax.broadcasted_iota(jnp.int32, (BLOCK, BLOCK), 1)
    pieces = [[None] * groups for _ in range(count)]
    for g in range(groups):
        lhs = jnp.concatenate(
            [stacked[b * rows + g * width : b * rows + (g + 1) * width] for b in range(count)],
            axis=0,
        )
        row = taps_long[g : g + 1, :]
        toeplitz = pltpu.roll(jnp.broadcast_to(row, (BLOCK, BLOCK)), 0, 1, stride=1, stride_axis=0)
        toeplitz = jnp.where(t_idx >= s_idx, toeplitz, 0.0)
        t_hi, t_lo = split2(toeplitz)
        near = dot(lhs, t_hi) + dot(lhs, t_lo)
        for b in range(count):
            pieces[b][g] = near[b * width : (b + 1) * width]
    long_term = jnp.concatenate(
        [
            jnp.concatenate(pieces[b], axis=0) + (far[(b - 1) * rows : b * rows] if b else 0.0)
            for b in range(count)
        ],
        axis=1,
    )
    signal = product.astype(f32)
    skip_b = jnp.concatenate([column(prm, skip_at, rows)] * (signal.shape[1] // LANES), axis=1)
    mixed = query.astype(f32) * (long_term + skip_b * signal)
    u0_ref[...] = res_ref[...].astype(f32) + mixed


def finish_kernel(width, modes, u0_ref, q_ref, z_ref, lam_ref, upd_ref, sq_ref):
    rows, length = u0_ref.shape
    lam = lam_ref[0][0:1, :]
    lanes = lam.shape[1]
    spread = exact_dot(z_ref[...], spread_matrix(lanes, modes))
    own = own_modes(rows, lanes, width, modes)
    z_hi = jnp.where(own, spread, 0.0).astype(bf16)
    lead_hi, lead_lo = split2(lead_table(columns(lam), columns(lam_ref[0][1:2, :]), 1, length))
    far = dot(z_hi, lead_hi) + dot(z_hi, lead_lo)
    updated = u0_ref[...] + q_ref[...].astype(f32) * far
    upd_ref[...] = updated
    part = jnp.sum(updated * updated, axis=0, keepdims=True)

    @pl.when(pl.program_id(0) == 0)
    def _():
        sq_ref[...] = part

    @pl.when(pl.program_id(0) > 0)
    def _():
        sq_ref[...] += part


def local(projections, short_filter, decay_rate, residue, skip, norm_gain, residual):
    channels, length = residual.shape
    groups, modes = decay_rate.shape
    width = channels // groups
    rim_len = short_filter.shape[2] - 1
    count = length // BLOCK
    chunk = 256 if channels % 256 == 0 else channels
    chunk_groups = chunk // width
    lanes = chunk_groups * modes
    steps = channels // chunk

    edge = projections[:, :, length - rim_len :].transpose(0, 2, 1)
    rim = shifted(edge, "ctx", 1)
    prm = jnp.concatenate(
        [
            short_filter.astype(f32).transpose(0, 2, 1).reshape(-1, channels),
            rim.astype(f32).reshape(-1, channels),
            skip[None, :],
        ],
        axis=0,
    )
    prm = jnp.pad(prm, ((0, LANES - prm.shape[0]), (0, 0))).T

    scaled = residue * jnp.sqrt(-jnp.expm1(-2.0 * decay_rate))
    lam = jnp.stack([decay_rate.reshape(steps, lanes), scaled.reshape(steps, lanes)], axis=1)

    proj_spec = pl.BlockSpec((3, chunk, length), lambda i: (0, i, 0))
    query_spec = pl.BlockSpec((1, chunk, length), lambda i: (0, i, 0))
    prm_spec = pl.BlockSpec((chunk, LANES), lambda i: (i, 0))
    lam_spec = pl.BlockSpec((1, 2, lanes), lambda i: (i, 0, 0))
    row_spec = pl.BlockSpec((chunk, length), lambda i: (i, 0))
    state_spec = pl.BlockSpec((chunk, modes), lambda i: (i, 0))

    end_state, product = pl.pallas_call(
        functools.partial(state_kernel, width, modes),
        grid=(steps,),
        in_specs=[proj_spec, prm_spec, lam_spec],
        out_specs=[state_spec, row_spec],
        out_shape=[
            jax.ShapeDtypeStruct((channels, modes), bf16),
            jax.ShapeDtypeStruct((channels, length), bf16),
        ],
    )(projections, prm, lam)

    size = lax.axis_size("ctx")
    dense = end_state.reshape(channels * modes // 128, 128)
    rate = jnp.repeat(decay_rate, width, axis=0).reshape(dense.shape)
    incoming = incoming_state(dense, rate * length, size).reshape(channels, modes)

    u0, query = pl.pallas_call(
        functools.partial(local_kernel, width, modes, count),
        grid=(steps,),
        in_specs=[query_spec, row_spec, prm_spec, lam_spec, row_spec],
        out_specs=[row_spec, row_spec],
        out_shape=[
            jax.ShapeDtypeStruct((channels, length), f32),
            jax.ShapeDtypeStruct((channels, length), bf16),
        ],
    )(projections, product, prm, lam, residual)

    updated, sq = pl.pallas_call(
        functools.partial(finish_kernel, width, modes),
        grid=(steps,),
        in_specs=[row_spec, row_spec, state_spec, lam_spec],
        out_specs=[row_spec, pl.BlockSpec((1, length), lambda i: (0, 0))],
        out_shape=[
            jax.ShapeDtypeStruct((channels, length), f32),
            jax.ShapeDtypeStruct((1, length), f32),
        ],
    )(u0, query, incoming, lam)
    squares = lax.psum(sq[0], "tp")
    return (updated * lax.rsqrt(squares / D + epsilon)[None, :] * norm_gain[:, None]).astype(bf16)


def solution(mesh):
    placed = (
        P(None, "tp", "ctx"),
        P(None, "tp", None),
        P("tp", None),
        P("tp", None),
        P("tp"),
        P("tp"),
        P("tp", "ctx"),
    )
    return jax.shard_map(
        local, mesh=mesh, in_specs=placed, out_specs=P("tp", "ctx"), check_vma=False
    )
```

```python
import functools

import jax
import jax.numpy as jnp
from jax import lax
from jax.experimental import pallas as pl
from jax.experimental.pallas import tpu as pltpu
from jax.sharding import PartitionSpec as P

D = 8192
epsilon = 1e-06
BLOCK = 128
LANES = 128
f32 = jnp.float32
bf16 = jnp.bfloat16


def shifted(shard, axis, by):
    size = lax.axis_size(axis)
    pairs = [(i, i + by) for i in range(size) if 0 <= i + by < size]
    return lax.ppermute(shard, axis, pairs)


def incoming_state(ends, span_rate, size):
    place = lax.axis_index("ctx")
    copies = jnp.broadcast_to(ends[None], (size,) + ends.shape)
    gathered = lax.all_to_all(copies, "ctx", 0, 0).astype(f32)
    earlier = jnp.arange(size, dtype=jnp.int32)
    gap = jnp.maximum(place - 1 - earlier, 0).astype(f32)
    weight = jnp.where(
        (earlier < place)[:, None, None],
        jnp.exp(-span_rate[None] * gap[:, None, None]),
        0.0,
    )
    return jnp.sum(weight * gathered, axis=0)


def split2(a):
    hi = a.astype(bf16)
    lo = (a - hi.astype(f32)).astype(bf16)
    return hi, lo


def split3(a):
    hi = a.astype(bf16)
    rest = a - hi.astype(f32)
    mid = rest.astype(bf16)
    lo = (rest - mid.astype(f32)).astype(bf16)
    return hi, mid, lo


def dot(a, b):
    return jnp.dot(a, b, preferred_element_type=f32)


def exact_dot(a, select):
    return sum(dot(part, select) for part in split3(a))


def column(prm, k, rows):
    return jnp.broadcast_to(prm[:, k : k + 1], (rows, LANES))


def featurize(proj_ref, prm, p, taps, rims):
    rows, length = proj_ref.shape[1], proj_ref.shape[2]
    t = taps * p
    weights = [column(prm, t + k, rows) for k in range(3)]
    back2 = column(prm, rims + 2 * p, rows)
    back1 = column(prm, rims + 2 * p + 1, rows)
    lane = lax.broadcasted_iota(jnp.int32, (rows, LANES), 1)
    tiles = [proj_ref[p, :, j * LANES : (j + 1) * LANES].astype(f32) for j in range(length // LANES)]
    once = [pltpu.roll(x, 1, 1) for x in tiles]
    twice = [pltpu.roll(x, 2, 1) for x in tiles]
    out = []
    for j, x in enumerate(tiles):
        if j == 0:
            x1 = jnp.where(lane == 0, back1, once[0])
            x2 = jnp.where(lane == 0, back2, jnp.where(lane == 1, back1, twice[0]))
        else:
            x1 = jnp.where(lane == 0, once[j - 1], once[j])
            x2 = jnp.where(lane < 2, twice[j - 1], twice[j])
        summed = weights[0] * x + weights[1] * x1
        summed = summed + weights[2] * x2
        out.append(summed.astype(bf16))
    return jnp.concatenate(out, axis=1)


def own_modes(rows, lanes, width, modes):
    row = lax.broadcasted_iota(jnp.int32, (rows, lanes), 0) // width
    lane = lax.broadcasted_iota(jnp.int32, (rows, lanes), 1) // modes
    return row == lane


def product_stack(proj_ref, prm, taps, rims, count):
    key = featurize(proj_ref, prm, 1, taps, rims).astype(f32)
    value = featurize(proj_ref, prm, 2, taps, rims).astype(f32)
    product = (key * value).astype(bf16)
    stacked = jnp.concatenate(
        [product[:, b * BLOCK : (b + 1) * BLOCK] for b in range(count)], axis=0
    )
    return product, stacked


def masked_ends(stacked, w_hi_ref, w_lo_ref, rows, width, modes, count):
    ends = dot(stacked, w_hi_ref[0]) + dot(stacked, w_lo_ref[0])
    own = own_modes(rows, ends.shape[1], width, modes)
    return [jnp.where(own, ends[b * rows : (b + 1) * rows], 0.0) for b in range(count)], own


def state_kernel(width, modes, proj_ref, prm_ref, lam_ref, out_ref, x_ref):
    rows, length = proj_ref.shape[1], proj_ref.shape[2]
    prm = prm_ref[...]
    key = featurize(proj_ref, prm, 1, 3, 9).astype(f32)
    value = featurize(proj_ref, prm, 2, 3, 9).astype(f32)
    product = (key * value).astype(bf16)
    x_ref[...] = product
    lam = lam_ref[0][0:1, :]
    lanes = lam.shape[1]
    span = (BLOCK - 1 - lax.broadcasted_iota(jnp.int32, (BLOCK, lanes), 0)).astype(f32)
    within = jnp.exp(-lam * span)
    blocks = length // BLOCK
    table = jnp.concatenate(
        [within * jnp.exp(-lam * float(BLOCK * (blocks - 1 - b))) for b in range(blocks)], axis=0
    )
    w_hi, w_lo = split2(table)
    ends = dot(product, w_hi) + dot(product, w_lo)
    own = own_modes(rows, lanes, width, modes)
    picked = jnp.where(own, ends, 0.0).astype(bf16)
    out_ref[...] = dot(picked, select_matrix(lanes, modes))[:, :modes].astype(bf16)


def select_matrix(lanes, modes):
    mode = lax.broadcasted_iota(jnp.int32, (lanes, LANES), 0) % modes
    lane = lax.broadcasted_iota(jnp.int32, (lanes, LANES), 1)
    return (mode == lane).astype(bf16)


def spread_matrix(lanes, modes):
    lane = lax.broadcasted_iota(jnp.int32, (modes, lanes), 0)
    mode = lax.broadcasted_iota(jnp.int32, (modes, lanes), 1) % modes
    return (mode == lane).astype(bf16)


def rate_columns(pair):
    lanes = pair.shape[1]
    padded = jnp.concatenate([pair, jnp.zeros((LANES - pair.shape[0], lanes), f32)], axis=0)
    turned = padded.T
    rates = jnp.broadcast_to(turned[:, 0:1], (lanes, LANES))
    weights = jnp.broadcast_to(turned[:, 1:2], (lanes, LANES))
    return rates, weights


def lead_table(rates, weights, first, count):
    wide = count // LANES
    rates = jnp.concatenate([rates] * wide, axis=1) if wide > 1 else rates
    weights = jnp.concatenate([weights] * wide, axis=1) if wide > 1 else weights
    lag = (first + lax.broadcasted_iota(jnp.int32, (rates.shape[0], count), 1)).astype(f32)
    return weights * jnp.exp(-rates * lag)


def local_kernel(
    width,
    modes,
    count,
    proj_ref,
    x_ref,
    prm_ref,
    lam_ref,
    res_ref,
    u0_ref,
    q_ref,
):
    rows = proj_ref.shape[1]
    groups = rows // width
    taps = 3
    rims = 3 * taps
    skip_at = rims + 6
    prm = prm_ref[...]
    query = featurize(proj_ref, prm, 0, taps, rims)
    q_ref[...] = query
    product = x_ref[...]
    stacked = jnp.concatenate(
        [product[:, b * BLOCK : (b + 1) * BLOCK] for b in range(count)], axis=0
    )
    lam = lam_ref[0][0:1, :]
    rates, weights = rate_columns(lam_ref[0])
    lanes = lam.shape[1]
    span = (BLOCK - 1 - lax.broadcasted_iota(jnp.int32, (BLOCK, lanes), 0)).astype(f32)
    w_hi, w_lo = split2(jnp.exp(-lam * span))
    used = stacked[: (count - 1) * rows]
    ends = dot(used, w_hi) + dot(used, w_lo)
    own = own_modes(rows, lanes, width, modes)
    decay = jnp.exp(-lam * float(BLOCK))
    state = jnp.where(own, ends[0:rows], 0.0)
    entering = [state]
    for b in range(1, count - 1):
        state = decay * state + jnp.where(own, ends[b * rows : (b + 1) * rows], 0.0)
        entering.append(state)
    z_hi, z_lo = split2(jnp.concatenate(entering, axis=0))
    lead_hi, lead_lo = split2(lead_table(rates, weights, 1, BLOCK))
    far = dot(z_hi, lead_hi) + dot(z_hi, lead_lo) + dot(z_lo, lead_hi)
    member = lax.broadcasted_iota(jnp.int32, (groups, lanes), 0) == (
        lax.broadcasted_iota(jnp.int32, (groups, lanes), 1) // modes
    )
    taps_long = sum(dot(member.astype(bf16), part) for part in split3(lead_table(rates, weights, 0, BLOCK)))

    s_idx = lax.broadcasted_iota(jnp.int32, (BLOCK, BLOCK), 0)
    t_idx = lax.broadcasted_iota(jnp.int32, (BLOCK, BLOCK), 1)
    pieces = [[None] * groups for _ in range(count)]
    for g in range(groups):
        lhs = jnp.concatenate(
            [stacked[b * rows + g * width : b * rows + (g + 1) * width] for b in range(count)],
            axis=0,
        )
        row = taps_long[g : g + 1, :]
        toeplitz = pltpu.roll(jnp.broadcast_to(row, (BLOCK, BLOCK)), 0, 1, stride=1, stride_axis=0)
        toeplitz = jnp.where(t_idx >= s_idx, toeplitz, 0.0)
        t_hi, t_lo = split2(toeplitz)
        near = dot(lhs, t_hi) + dot(lhs, t_lo)
        for b in range(count):
            pieces[b][g] = near[b * width : (b + 1) * width]
    long_term = jnp.concatenate(
        [
            jnp.concatenate(pieces[b], axis=0) + (far[(b - 1) * rows : b * rows] if b else 0.0)
            for b in range(count)
        ],
        axis=1,
    )
    signal = product.astype(f32)
    skip_b = jnp.concatenate([column(prm, skip_at, rows)] * (signal.shape[1] // LANES), axis=1)
    mixed = query.astype(f32) * (long_term + skip_b * signal)
    u0_ref[...] = res_ref[...].astype(f32) + mixed


def finish_kernel(width, modes, u0_ref, q_ref, z_ref, lam_ref, upd_ref, sq_ref):
    rows, length = u0_ref.shape
    lam = lam_ref[0][0:1, :]
    lanes = lam.shape[1]
    spread = exact_dot(z_ref[...], spread_matrix(lanes, modes))
    own = own_modes(rows, lanes, width, modes)
    z_hi = jnp.where(own, spread, 0.0).astype(bf16)
    lead_hi, lead_lo = split2(lead_table(*rate_columns(lam_ref[0]), 1, length))
    far = dot(z_hi, lead_hi) + dot(z_hi, lead_lo)
    updated = u0_ref[...] + q_ref[...].astype(f32) * far
    upd_ref[...] = updated
    part = jnp.sum(updated * updated, axis=0, keepdims=True)

    @pl.when(pl.program_id(0) == 0)
    def _():
        sq_ref[...] = part

    @pl.when(pl.program_id(0) > 0)
    def _():
        sq_ref[...] += part


def local(projections, short_filter, decay_rate, residue, skip, norm_gain, residual):
    channels, length = residual.shape
    groups, modes = decay_rate.shape
    width = channels // groups
    rim_len = short_filter.shape[2] - 1
    count = length // BLOCK
    chunk = 256 if channels % 256 == 0 else channels
    chunk_groups = chunk // width
    lanes = chunk_groups * modes
    steps = channels // chunk

    edge = projections[:, :, length - rim_len :].transpose(0, 2, 1)
    rim = shifted(edge, "ctx", 1)
    prm = jnp.concatenate(
        [
            short_filter.astype(f32).transpose(0, 2, 1).reshape(-1, channels),
            rim.astype(f32).reshape(-1, channels),
            skip[None, :],
        ],
        axis=0,
    )
    prm = jnp.pad(prm, ((0, LANES - prm.shape[0]), (0, 0))).T

    scaled = residue * jnp.sqrt(-jnp.expm1(-2.0 * decay_rate))
    lam = jnp.stack([decay_rate.reshape(steps, lanes), scaled.reshape(steps, lanes)], axis=1)

    proj_spec = pl.BlockSpec((3, chunk, length), lambda i: (0, i, 0))
    query_spec = pl.BlockSpec((1, chunk, length), lambda i: (0, i, 0))
    prm_spec = pl.BlockSpec((chunk, LANES), lambda i: (i, 0))
    lam_spec = pl.BlockSpec((1, 2, lanes), lambda i: (i, 0, 0))
    row_spec = pl.BlockSpec((chunk, length), lambda i: (i, 0))
    state_spec = pl.BlockSpec((chunk, modes), lambda i: (i, 0))

    end_state, product = pl.pallas_call(
        functools.partial(state_kernel, width, modes),
        grid=(steps,),
        in_specs=[proj_spec, prm_spec, lam_spec],
        out_specs=[state_spec, row_spec],
        out_shape=[
            jax.ShapeDtypeStruct((channels, modes), bf16),
            jax.ShapeDtypeStruct((channels, length), bf16),
        ],
    )(projections, prm, lam)

    size = lax.axis_size("ctx")
    dense = end_state.reshape(channels * modes // 128, 128)
    rate = jnp.repeat(decay_rate, width, axis=0).reshape(dense.shape)
    incoming = incoming_state(dense, rate * length, size).reshape(channels, modes)

    u0, query = pl.pallas_call(
        functools.partial(local_kernel, width, modes, count),
        grid=(steps,),
        in_specs=[query_spec, row_spec, prm_spec, lam_spec, row_spec],
        out_specs=[row_spec, row_spec],
        out_shape=[
            jax.ShapeDtypeStruct((channels, length), f32),
            jax.ShapeDtypeStruct((channels, length), bf16),
        ],
    )(projections, product, prm, lam, residual)

    updated, sq = pl.pallas_call(
        functools.partial(finish_kernel, width, modes),
        grid=(steps,),
        in_specs=[row_spec, row_spec, state_spec, lam_spec],
        out_specs=[row_spec, pl.BlockSpec((1, length), lambda i: (0, 0))],
        out_shape=[
            jax.ShapeDtypeStruct((channels, length), f32),
            jax.ShapeDtypeStruct((1, length), f32),
        ],
    )(u0, query, incoming, lam)
    squares = lax.psum(sq[0], "tp")
    return (updated * lax.rsqrt(squares / D + epsilon)[None, :] * norm_gain[:, None]).astype(bf16)


def solution(mesh):
    placed = (
        P(None, "tp", "ctx"),
        P(None, "tp", None),
        P("tp", None),
        P("tp", None),
        P("tp"),
        P("tp"),
        P("tp", "ctx"),
    )
    return jax.shard_map(
        local, mesh=mesh, in_specs=placed, out_specs=P("tp", "ctx"), check_vma=False
    )
```

```python
import functools

import jax
import jax.numpy as jnp
from jax import lax
from jax.experimental import pallas as pl
from jax.experimental.pallas import tpu as pltpu
from jax.sharding import PartitionSpec as P

D = 8192
epsilon = 1e-06
BLOCK = 128
LANES = 128
f32 = jnp.float32
bf16 = jnp.bfloat16


def shifted(shard, axis, by):
    size = lax.axis_size(axis)
    pairs = [(i, i + by) for i in range(size) if 0 <= i + by < size]
    return lax.ppermute(shard, axis, pairs)


def incoming_state(ends, span_rate, size):
    place = lax.axis_index("ctx")
    copies = jnp.broadcast_to(ends[None], (size,) + ends.shape)
    gathered = lax.all_to_all(copies, "ctx", 0, 0).astype(f32)
    earlier = jnp.arange(size, dtype=jnp.int32)
    gap = jnp.maximum(place - 1 - earlier, 0).astype(f32)
    weight = jnp.where(
        (earlier < place)[:, None, None],
        jnp.exp(-span_rate[None] * gap[:, None, None]),
        0.0,
    )
    return jnp.sum(weight * gathered, axis=0)


def split2(a):
    hi = a.astype(bf16)
    lo = (a - hi.astype(f32)).astype(bf16)
    return hi, lo


def split3(a):
    hi = a.astype(bf16)
    rest = a - hi.astype(f32)
    mid = rest.astype(bf16)
    lo = (rest - mid.astype(f32)).astype(bf16)
    return hi, mid, lo


def dot(a, b):
    return jnp.dot(a, b, preferred_element_type=f32)


def exact_dot(a, select):
    return sum(dot(part, select) for part in split3(a))


def column(prm, k, rows):
    return jnp.broadcast_to(prm[:, k : k + 1], (rows, LANES))


def featurize(proj_ref, prm, p, taps, rims, slot=None):
    slot = p if slot is None else slot
    rows, length = proj_ref.shape[1], proj_ref.shape[2]
    t = taps * p
    weights = [column(prm, t + k, rows) for k in range(3)]
    back2 = column(prm, rims + 2 * p, rows)
    back1 = column(prm, rims + 2 * p + 1, rows)
    lane = lax.broadcasted_iota(jnp.int32, (rows, LANES), 1)
    tiles = [proj_ref[slot, :, j * LANES : (j + 1) * LANES].astype(f32) for j in range(length // LANES)]
    once = [pltpu.roll(x, 1, 1) for x in tiles]
    twice = [pltpu.roll(x, 2, 1) for x in tiles]
    out = []
    for j, x in enumerate(tiles):
        if j == 0:
            x1 = jnp.where(lane == 0, back1, once[0])
            x2 = jnp.where(lane == 0, back2, jnp.where(lane == 1, back1, twice[0]))
        else:
            x1 = jnp.where(lane == 0, once[j - 1], once[j])
            x2 = jnp.where(lane < 2, twice[j - 1], twice[j])
        summed = weights[0] * x + weights[1] * x1
        summed = summed + weights[2] * x2
        out.append(summed.astype(bf16))
    return jnp.concatenate(out, axis=1)


def own_modes(rows, lanes, width, modes):
    row = lax.broadcasted_iota(jnp.int32, (rows, lanes), 0) // width
    lane = lax.broadcasted_iota(jnp.int32, (rows, lanes), 1) // modes
    return row == lane


def product_stack(proj_ref, prm, taps, rims, count):
    key = featurize(proj_ref, prm, 1, taps, rims).astype(f32)
    value = featurize(proj_ref, prm, 2, taps, rims).astype(f32)
    product = (key * value).astype(bf16)
    stacked = jnp.concatenate(
        [product[:, b * BLOCK : (b + 1) * BLOCK] for b in range(count)], axis=0
    )
    return product, stacked


def masked_ends(stacked, w_hi_ref, w_lo_ref, rows, width, modes, count):
    ends = dot(stacked, w_hi_ref[0]) + dot(stacked, w_lo_ref[0])
    own = own_modes(rows, ends.shape[1], width, modes)
    return [jnp.where(own, ends[b * rows : (b + 1) * rows], 0.0) for b in range(count)], own


def state_kernel(width, modes, key_ref, value_ref, prm_ref, lam_ref, out_ref, x_ref):
    rows, length = key_ref.shape[1], key_ref.shape[2]
    prm = prm_ref[...]
    key = featurize(key_ref, prm, 1, 3, 9, 0).astype(f32)
    value = featurize(value_ref, prm, 2, 3, 9, 0).astype(f32)
    product = (key * value).astype(bf16)
    x_ref[...] = product
    lam = lam_ref[0][0:1, :]
    lanes = lam.shape[1]
    span = (BLOCK - 1 - lax.broadcasted_iota(jnp.int32, (BLOCK, lanes), 0)).astype(f32)
    within = jnp.exp(-lam * span)
    blocks = length // BLOCK
    table = jnp.concatenate(
        [within * jnp.exp(-lam * float(BLOCK * (blocks - 1 - b))) for b in range(blocks)], axis=0
    )
    w_hi, w_lo = split2(table)
    ends = dot(product, w_hi) + dot(product, w_lo)
    own = own_modes(rows, lanes, width, modes)
    picked = jnp.where(own, ends, 0.0).astype(bf16)
    out_ref[...] = dot(picked, select_matrix(lanes, modes))[:, :modes].astype(bf16)


def select_matrix(lanes, modes):
    mode = lax.broadcasted_iota(jnp.int32, (lanes, LANES), 0) % modes
    lane = lax.broadcasted_iota(jnp.int32, (lanes, LANES), 1)
    return (mode == lane).astype(bf16)


def spread_matrix(lanes, modes):
    lane = lax.broadcasted_iota(jnp.int32, (modes, lanes), 0)
    mode = lax.broadcasted_iota(jnp.int32, (modes, lanes), 1) % modes
    return (mode == lane).astype(bf16)


def columns(row):
    lanes = row.shape[1]
    diagonal = lax.broadcasted_iota(jnp.int32, (lanes, lanes), 0) == lax.broadcasted_iota(
        jnp.int32, (lanes, lanes), 1
    )
    spread = jnp.where(diagonal, jnp.broadcast_to(row, (lanes, lanes)), 0.0)
    return exact_dot(spread, jnp.ones((lanes, LANES), bf16))


def lead_table(rates, weights, first, count):
    wide = count // LANES
    rates = jnp.concatenate([rates] * wide, axis=1) if wide > 1 else rates
    weights = jnp.concatenate([weights] * wide, axis=1) if wide > 1 else weights
    lag = (first + lax.broadcasted_iota(jnp.int32, (rates.shape[0], count), 1)).astype(f32)
    return weights * jnp.exp(-rates * lag)


def local_kernel(
    width,
    modes,
    count,
    proj_ref,
    x_ref,
    prm_ref,
    lam_ref,
    res_ref,
    u0_ref,
    q_ref,
):
    rows = proj_ref.shape[1]
    groups = rows // width
    taps = 3
    rims = 3 * taps
    skip_at = rims + 6
    prm = prm_ref[...]
    query = featurize(proj_ref, prm, 0, taps, rims)
    q_ref[...] = query
    product = x_ref[...]
    stacked = jnp.concatenate(
        [product[:, b * BLOCK : (b + 1) * BLOCK] for b in range(count)], axis=0
    )
    lam = lam_ref[0][0:1, :]
    rates = columns(lam)
    weights = columns(lam_ref[0][1:2, :])
    lanes = lam.shape[1]
    span = (BLOCK - 1 - lax.broadcasted_iota(jnp.int32, (BLOCK, lanes), 0)).astype(f32)
    w_hi, w_lo = split2(jnp.exp(-lam * span))
    used = stacked[: (count - 1) * rows]
    ends = dot(used, w_hi) + dot(used, w_lo)
    own = own_modes(rows, lanes, width, modes)
    decay = jnp.exp(-lam * float(BLOCK))
    state = jnp.where(own, ends[0:rows], 0.0)
    entering = [state]
    for b in range(1, count - 1):
        state = decay * state + jnp.where(own, ends[b * rows : (b + 1) * rows], 0.0)
        entering.append(state)
    z_hi, z_lo = split2(jnp.concatenate(entering, axis=0))
    lead_hi, lead_lo = split2(lead_table(rates, weights, 1, BLOCK))
    far = dot(z_hi, lead_hi) + dot(z_hi, lead_lo) + dot(z_lo, lead_hi)
    member = lax.broadcasted_iota(jnp.int32, (groups, lanes), 0) == (
        lax.broadcasted_iota(jnp.int32, (groups, lanes), 1) // modes
    )
    taps_long = sum(dot(member.astype(bf16), part) for part in split3(lead_table(rates, weights, 0, BLOCK)))

    s_idx = lax.broadcasted_iota(jnp.int32, (BLOCK, BLOCK), 0)
    t_idx = lax.broadcasted_iota(jnp.int32, (BLOCK, BLOCK), 1)
    pieces = [[None] * groups for _ in range(count)]
    for g in range(groups):
        lhs = jnp.concatenate(
            [stacked[b * rows + g * width : b * rows + (g + 1) * width] for b in range(count)],
            axis=0,
        )
        row = taps_long[g : g + 1, :]
        toeplitz = pltpu.roll(jnp.broadcast_to(row, (BLOCK, BLOCK)), 0, 1, stride=1, stride_axis=0)
        toeplitz = jnp.where(t_idx >= s_idx, toeplitz, 0.0)
        t_hi, t_lo = split2(toeplitz)
        near = dot(lhs, t_hi) + dot(lhs, t_lo)
        for b in range(count):
            pieces[b][g] = near[b * width : (b + 1) * width]
    long_term = jnp.concatenate(
        [
            jnp.concatenate(pieces[b], axis=0) + (far[(b - 1) * rows : b * rows] if b else 0.0)
            for b in range(count)
        ],
        axis=1,
    )
    signal = product.astype(f32)
    skip_b = jnp.concatenate([column(prm, skip_at, rows)] * (signal.shape[1] // LANES), axis=1)
    mixed = query.astype(f32) * (long_term + skip_b * signal)
    u0_ref[...] = res_ref[...].astype(f32) + mixed


def finish_kernel(width, modes, u0_ref, q_ref, z_ref, lam_ref, upd_ref, sq_ref):
    rows, length = u0_ref.shape
    lam = lam_ref[0][0:1, :]
    lanes = lam.shape[1]
    spread = exact_dot(z_ref[...], spread_matrix(lanes, modes))
    own = own_modes(rows, lanes, width, modes)
    z_hi = jnp.where(own, spread, 0.0).astype(bf16)
    lead_hi, lead_lo = split2(lead_table(columns(lam), columns(lam_ref[0][1:2, :]), 1, length))
    far = dot(z_hi, lead_hi) + dot(z_hi, lead_lo)
    updated = u0_ref[...] + q_ref[...].astype(f32) * far
    upd_ref[...] = updated
    part = jnp.sum(updated * updated, axis=0, keepdims=True)

    @pl.when(pl.program_id(0) == 0)
    def _():
        sq_ref[...] = part

    @pl.when(pl.program_id(0) > 0)
    def _():
        sq_ref[...] += part


def local(projections, short_filter, decay_rate, residue, skip, norm_gain, residual):
    channels, length = residual.shape
    groups, modes = decay_rate.shape
    width = channels // groups
    rim_len = short_filter.shape[2] - 1
    count = length // BLOCK
    chunk = 256 if channels % 256 == 0 else channels
    chunk_groups = chunk // width
    lanes = chunk_groups * modes
    steps = channels // chunk

    edge = projections[:, :, length - rim_len :].transpose(0, 2, 1)
    rim = shifted(edge, "ctx", 1)
    prm = jnp.concatenate(
        [
            short_filter.astype(f32).transpose(0, 2, 1).reshape(-1, channels),
            rim.astype(f32).reshape(-1, channels),
            skip[None, :],
        ],
        axis=0,
    )
    prm = jnp.pad(prm, ((0, LANES - prm.shape[0]), (0, 0))).T

    scaled = residue * jnp.sqrt(-jnp.expm1(-2.0 * decay_rate))
    lam = jnp.stack([decay_rate.reshape(steps, lanes), scaled.reshape(steps, lanes)], axis=1)

    proj_spec = pl.BlockSpec((3, chunk, length), lambda i: (0, i, 0))
    query_spec = pl.BlockSpec((1, chunk, length), lambda i: (0, i, 0))
    prm_spec = pl.BlockSpec((chunk, LANES), lambda i: (i, 0))
    lam_spec = pl.BlockSpec((1, 2, lanes), lambda i: (i, 0, 0))
    row_spec = pl.BlockSpec((chunk, length), lambda i: (i, 0))
    state_spec = pl.BlockSpec((chunk, modes), lambda i: (i, 0))

    end_state, product = pl.pallas_call(
        functools.partial(state_kernel, width, modes),
        grid=(steps,),
        in_specs=[
            pl.BlockSpec((1, chunk, length), lambda i: (1, i, 0)),
            pl.BlockSpec((1, chunk, length), lambda i: (2, i, 0)),
            prm_spec,
            lam_spec,
        ],
        out_specs=[state_spec, row_spec],
        out_shape=[
            jax.ShapeDtypeStruct((channels, modes), bf16),
            jax.ShapeDtypeStruct((channels, length), bf16),
        ],
    )(projections, projections, prm, lam)

    size = lax.axis_size("ctx")
    dense = end_state.reshape(channels * modes // 128, 128)
    rate = jnp.repeat(decay_rate, width, axis=0).reshape(dense.shape)
    incoming = incoming_state(dense, rate * length, size).reshape(channels, modes)

    u0, query = pl.pallas_call(
        functools.partial(local_kernel, width, modes, count),
        grid=(steps,),
        in_specs=[query_spec, row_spec, prm_spec, lam_spec, row_spec],
        out_specs=[row_spec, row_spec],
        out_shape=[
            jax.ShapeDtypeStruct((channels, length), f32),
            jax.ShapeDtypeStruct((channels, length), bf16),
        ],
    )(projections, product, prm, lam, residual)

    updated, sq = pl.pallas_call(
        functools.partial(finish_kernel, width, modes),
        grid=(steps,),
        in_specs=[row_spec, row_spec, state_spec, lam_spec],
        out_specs=[row_spec, pl.BlockSpec((1, length), lambda i: (0, 0))],
        out_shape=[
            jax.ShapeDtypeStruct((channels, length), f32),
            jax.ShapeDtypeStruct((1, length), f32),
        ],
    )(u0, query, incoming, lam)
    squares = lax.psum(sq[0], "tp")
    return (updated * lax.rsqrt(squares / D + epsilon)[None, :] * norm_gain[:, None]).astype(bf16)


def solution(mesh):
    placed = (
        P(None, "tp", "ctx"),
        P(None, "tp", None),
        P("tp", None),
        P("tp", None),
        P("tp"),
        P("tp"),
        P("tp", "ctx"),
    )
    return jax.shard_map(
        local, mesh=mesh, in_specs=placed, out_specs=P("tp", "ctx"), check_vma=False
    )
```

```python
import functools

import jax
import jax.numpy as jnp
from jax import lax
from jax.experimental import pallas as pl
from jax.experimental.pallas import tpu as pltpu
from jax.sharding import PartitionSpec as P

D = 8192
epsilon = 1e-06
BLOCK = 128
LANES = 128
f32 = jnp.float32
bf16 = jnp.bfloat16


def shifted(shard, axis, by):
    size = lax.axis_size(axis)
    pairs = [(i, i + by) for i in range(size) if 0 <= i + by < size]
    return lax.ppermute(shard, axis, pairs)


def incoming_state(ends, span_rate, size):
    place = lax.axis_index("ctx")
    copies = jnp.broadcast_to(ends[None], (size,) + ends.shape)
    gathered = lax.all_to_all(copies, "ctx", 0, 0).astype(f32)
    earlier = jnp.arange(size, dtype=jnp.int32)
    gap = jnp.maximum(place - 1 - earlier, 0).astype(f32)
    weight = jnp.where(
        (earlier < place)[:, None, None],
        jnp.exp(-span_rate[None] * gap[:, None, None]),
        0.0,
    )
    return jnp.sum(weight * gathered, axis=0)


def split2(a):
    hi = a.astype(bf16)
    lo = (a - hi.astype(f32)).astype(bf16)
    return hi, lo


def split3(a):
    hi = a.astype(bf16)
    rest = a - hi.astype(f32)
    mid = rest.astype(bf16)
    lo = (rest - mid.astype(f32)).astype(bf16)
    return hi, mid, lo


def dot(a, b):
    return jnp.dot(a, b, preferred_element_type=f32)


def dot_nt(a, b):
    return lax.dot_general(a, b, (((1,), (1,)), ((), ())), preferred_element_type=f32)


def lead_rows(pair, first, count):
    lanes = pair.shape[1]
    lag = (first + lax.broadcasted_iota(jnp.int32, (count, lanes), 0)).astype(f32)
    return pair[1:2, :] * jnp.exp(-pair[0:1, :] * lag)


def exact_dot(a, select):
    return sum(dot(part, select) for part in split3(a))


def column(prm, k, rows):
    return jnp.broadcast_to(prm[:, k : k + 1], (rows, LANES))


def featurize(proj_ref, prm, p, taps, rims, slot=None):
    slot = p if slot is None else slot
    rows, length = proj_ref.shape[1], proj_ref.shape[2]
    t = taps * p
    weights = [column(prm, t + k, rows) for k in range(3)]
    back2 = column(prm, rims + 2 * p, rows)
    back1 = column(prm, rims + 2 * p + 1, rows)
    lane = lax.broadcasted_iota(jnp.int32, (rows, LANES), 1)
    tiles = [proj_ref[slot, :, j * LANES : (j + 1) * LANES].astype(f32) for j in range(length // LANES)]
    once = [pltpu.roll(x, 1, 1) for x in tiles]
    twice = [pltpu.roll(x, 2, 1) for x in tiles]
    out = []
    for j, x in enumerate(tiles):
        if j == 0:
            x1 = jnp.where(lane == 0, back1, once[0])
            x2 = jnp.where(lane == 0, back2, jnp.where(lane == 1, back1, twice[0]))
        else:
            x1 = jnp.where(lane == 0, once[j - 1], once[j])
            x2 = jnp.where(lane < 2, twice[j - 1], twice[j])
        summed = weights[0] * x + weights[1] * x1
        summed = summed + weights[2] * x2
        out.append(summed.astype(bf16))
    return jnp.concatenate(out, axis=1)


def own_modes(rows, lanes, width, modes):
    row = lax.broadcasted_iota(jnp.int32, (rows, lanes), 0) // width
    lane = lax.broadcasted_iota(jnp.int32, (rows, lanes), 1) // modes
    return row == lane


def product_stack(proj_ref, prm, taps, rims, count):
    key = featurize(proj_ref, prm, 1, taps, rims).astype(f32)
    value = featurize(proj_ref, prm, 2, taps, rims).astype(f32)
    product = (key * value).astype(bf16)
    stacked = jnp.concatenate(
        [product[:, b * BLOCK : (b + 1) * BLOCK] for b in range(count)], axis=0
    )
    return product, stacked


def masked_ends(stacked, w_hi_ref, w_lo_ref, rows, width, modes, count):
    ends = dot(stacked, w_hi_ref[0]) + dot(stacked, w_lo_ref[0])
    own = own_modes(rows, ends.shape[1], width, modes)
    return [jnp.where(own, ends[b * rows : (b + 1) * rows], 0.0) for b in range(count)], own


def state_kernel(width, modes, key_ref, value_ref, prm_ref, lam_ref, out_ref, x_ref):
    rows, length = key_ref.shape[1], key_ref.shape[2]
    prm = prm_ref[...]
    key = featurize(key_ref, prm, 1, 3, 9, 0).astype(f32)
    value = featurize(value_ref, prm, 2, 3, 9, 0).astype(f32)
    product = (key * value).astype(bf16)
    x_ref[...] = product
    lam = lam_ref[0][0:1, :]
    lanes = lam.shape[1]
    span = (BLOCK - 1 - lax.broadcasted_iota(jnp.int32, (BLOCK, lanes), 0)).astype(f32)
    within = jnp.exp(-lam * span)
    blocks = length // BLOCK
    table = jnp.concatenate(
        [within * jnp.exp(-lam * float(BLOCK * (blocks - 1 - b))) for b in range(blocks)], axis=0
    )
    w_hi, w_lo = split2(table)
    ends = dot(product, w_hi) + dot(product, w_lo)
    own = own_modes(rows, lanes, width, modes)
    picked = jnp.where(own, ends, 0.0).astype(bf16)
    out_ref[...] = dot(picked, select_matrix(lanes, modes))[:, :modes].astype(bf16)


def select_matrix(lanes, modes):
    mode = lax.broadcasted_iota(jnp.int32, (lanes, LANES), 0) % modes
    lane = lax.broadcasted_iota(jnp.int32, (lanes, LANES), 1)
    return (mode == lane).astype(bf16)


def spread_matrix(lanes, modes):
    lane = lax.broadcasted_iota(jnp.int32, (modes, lanes), 0)
    mode = lax.broadcasted_iota(jnp.int32, (modes, lanes), 1) % modes
    return (mode == lane).astype(bf16)


def columns(row):
    lanes = row.shape[1]
    diagonal = lax.broadcasted_iota(jnp.int32, (lanes, lanes), 0) == lax.broadcasted_iota(
        jnp.int32, (lanes, lanes), 1
    )
    spread = jnp.where(diagonal, jnp.broadcast_to(row, (lanes, lanes)), 0.0)
    return exact_dot(spread, jnp.ones((lanes, LANES), bf16))


def lead_table(rates, weights, first, count):
    wide = count // LANES
    rates = jnp.concatenate([rates] * wide, axis=1) if wide > 1 else rates
    weights = jnp.concatenate([weights] * wide, axis=1) if wide > 1 else weights
    lag = (first + lax.broadcasted_iota(jnp.int32, (rates.shape[0], count), 1)).astype(f32)
    return weights * jnp.exp(-rates * lag)


def local_kernel(
    width,
    modes,
    count,
    proj_ref,
    x_ref,
    prm_ref,
    lam_ref,
    res_ref,
    u0_ref,
    q_ref,
):
    rows = proj_ref.shape[1]
    groups = rows // width
    taps = 3
    rims = 3 * taps
    skip_at = rims + 6
    prm = prm_ref[...]
    query = featurize(proj_ref, prm, 0, taps, rims)
    q_ref[...] = query
    product = x_ref[...]
    stacked = jnp.concatenate(
        [product[:, b * BLOCK : (b + 1) * BLOCK] for b in range(count)], axis=0
    )
    lam = lam_ref[0][0:1, :]
    pair = lam_ref[0]
    lanes = lam.shape[1]
    span = (BLOCK - 1 - lax.broadcasted_iota(jnp.int32, (BLOCK, lanes), 0)).astype(f32)
    w_hi, w_lo = split2(jnp.exp(-lam * span))
    used = stacked[: (count - 1) * rows]
    ends = dot(used, w_hi) + dot(used, w_lo)
    own = own_modes(rows, lanes, width, modes)
    decay = jnp.exp(-lam * float(BLOCK))
    state = jnp.where(own, ends[0:rows], 0.0)
    entering = [state]
    for b in range(1, count - 1):
        state = decay * state + jnp.where(own, ends[b * rows : (b + 1) * rows], 0.0)
        entering.append(state)
    z_hi, z_lo = split2(jnp.concatenate(entering, axis=0))
    lead_hi, lead_lo = split2(lead_rows(pair, 1, BLOCK))
    far = dot_nt(z_hi, lead_hi) + dot_nt(z_hi, lead_lo) + dot_nt(z_lo, lead_hi)
    member = lax.broadcasted_iota(jnp.int32, (groups, lanes), 0) == (
        lax.broadcasted_iota(jnp.int32, (groups, lanes), 1) // modes
    )
    taps_long = sum(dot_nt(member.astype(bf16), part) for part in split3(lead_rows(pair, 0, BLOCK)))

    s_idx = lax.broadcasted_iota(jnp.int32, (BLOCK, BLOCK), 0)
    t_idx = lax.broadcasted_iota(jnp.int32, (BLOCK, BLOCK), 1)
    pieces = [[None] * groups for _ in range(count)]
    for g in range(groups):
        lhs = jnp.concatenate(
            [stacked[b * rows + g * width : b * rows + (g + 1) * width] for b in range(count)],
            axis=0,
        )
        row = taps_long[g : g + 1, :]
        toeplitz = pltpu.roll(jnp.broadcast_to(row, (BLOCK, BLOCK)), 0, 1, stride=1, stride_axis=0)
        toeplitz = jnp.where(t_idx >= s_idx, toeplitz, 0.0)
        t_hi, t_lo = split2(toeplitz)
        near = dot(lhs, t_hi) + dot(lhs, t_lo)
        for b in range(count):
            pieces[b][g] = near[b * width : (b + 1) * width]
    long_term = jnp.concatenate(
        [
            jnp.concatenate(pieces[b], axis=0) + (far[(b - 1) * rows : b * rows] if b else 0.0)
            for b in range(count)
        ],
        axis=1,
    )
    signal = product.astype(f32)
    skip_b = jnp.concatenate([column(prm, skip_at, rows)] * (signal.shape[1] // LANES), axis=1)
    mixed = query.astype(f32) * (long_term + skip_b * signal)
    u0_ref[...] = res_ref[...].astype(f32) + mixed


def finish_kernel(width, modes, u0_ref, q_ref, z_ref, lam_ref, upd_ref, sq_ref):
    rows, length = u0_ref.shape
    lam = lam_ref[0][0:1, :]
    lanes = lam.shape[1]
    spread = exact_dot(z_ref[...], spread_matrix(lanes, modes))
    own = own_modes(rows, lanes, width, modes)
    z_hi = jnp.where(own, spread, 0.0).astype(bf16)
    lead_hi, lead_lo = split2(lead_rows(lam_ref[0], 1, length))
    far = dot_nt(z_hi, lead_hi) + dot_nt(z_hi, lead_lo)
    updated = u0_ref[...] + q_ref[...].astype(f32) * far
    upd_ref[...] = updated
    part = jnp.sum(updated * updated, axis=0, keepdims=True)

    @pl.when(pl.program_id(0) == 0)
    def _():
        sq_ref[...] = part

    @pl.when(pl.program_id(0) > 0)
    def _():
        sq_ref[...] += part


def local(projections, short_filter, decay_rate, residue, skip, norm_gain, residual):
    channels, length = residual.shape
    groups, modes = decay_rate.shape
    width = channels // groups
    rim_len = short_filter.shape[2] - 1
    count = length // BLOCK
    chunk = 256 if channels % 256 == 0 else channels
    chunk_groups = chunk // width
    lanes = chunk_groups * modes
    steps = channels // chunk

    edge = projections[:, :, length - rim_len :].transpose(0, 2, 1)
    rim = shifted(edge, "ctx", 1)
    prm = jnp.concatenate(
        [
            short_filter.astype(f32).transpose(0, 2, 1).reshape(-1, channels),
            rim.astype(f32).reshape(-1, channels),
            skip[None, :],
        ],
        axis=0,
    )
    prm = jnp.pad(prm, ((0, LANES - prm.shape[0]), (0, 0))).T

    scaled = residue * jnp.sqrt(-jnp.expm1(-2.0 * decay_rate))
    lam = jnp.stack([decay_rate.reshape(steps, lanes), scaled.reshape(steps, lanes)], axis=1)

    proj_spec = pl.BlockSpec((3, chunk, length), lambda i: (0, i, 0))
    query_spec = pl.BlockSpec((1, chunk, length), lambda i: (0, i, 0))
    prm_spec = pl.BlockSpec((chunk, LANES), lambda i: (i, 0))
    lam_spec = pl.BlockSpec((1, 2, lanes), lambda i: (i, 0, 0))
    row_spec = pl.BlockSpec((chunk, length), lambda i: (i, 0))
    state_spec = pl.BlockSpec((chunk, modes), lambda i: (i, 0))

    end_state, product = pl.pallas_call(
        functools.partial(state_kernel, width, modes),
        grid=(steps,),
        in_specs=[
            pl.BlockSpec((1, chunk, length), lambda i: (1, i, 0)),
            pl.BlockSpec((1, chunk, length), lambda i: (2, i, 0)),
            prm_spec,
            lam_spec,
        ],
        out_specs=[state_spec, row_spec],
        out_shape=[
            jax.ShapeDtypeStruct((channels, modes), bf16),
            jax.ShapeDtypeStruct((channels, length), bf16),
        ],
    )(projections, projections, prm, lam)

    size = lax.axis_size("ctx")
    dense = end_state.reshape(channels * modes // 128, 128)
    rate = jnp.repeat(decay_rate, width, axis=0).reshape(dense.shape)
    incoming = incoming_state(dense, rate * length, size).reshape(channels, modes)

    u0, query = pl.pallas_call(
        functools.partial(local_kernel, width, modes, count),
        grid=(steps,),
        in_specs=[query_spec, row_spec, prm_spec, lam_spec, row_spec],
        out_specs=[row_spec, row_spec],
        out_shape=[
            jax.ShapeDtypeStruct((channels, length), f32),
            jax.ShapeDtypeStruct((channels, length), bf16),
        ],
    )(projections, product, prm, lam, residual)

    updated, sq = pl.pallas_call(
        functools.partial(finish_kernel, width, modes),
        grid=(steps,),
        in_specs=[row_spec, row_spec, state_spec, lam_spec],
        out_specs=[row_spec, pl.BlockSpec((1, length), lambda i: (0, 0))],
        out_shape=[
            jax.ShapeDtypeStruct((channels, length), f32),
            jax.ShapeDtypeStruct((1, length), f32),
        ],
    )(u0, query, incoming, lam)
    squares = lax.psum(sq[0], "tp")
    return (updated * lax.rsqrt(squares / D + epsilon)[None, :] * norm_gain[:, None]).astype(bf16)


def solution(mesh):
    placed = (
        P(None, "tp", "ctx"),
        P(None, "tp", None),
        P("tp", None),
        P("tp", None),
        P("tp"),
        P("tp"),
        P("tp", "ctx"),
    )
    return jax.shard_map(
        local, mesh=mesh, in_specs=placed, out_specs=P("tp", "ctx"), check_vma=False
    )
```

```python
import functools

import jax
import jax.numpy as jnp
from jax import lax
from jax.experimental import pallas as pl
from jax.experimental.pallas import tpu as pltpu
from jax.sharding import PartitionSpec as P

D = 8192
epsilon = 1e-06
BLOCK = 128
LANES = 128
f32 = jnp.float32
bf16 = jnp.bfloat16


def shifted(shard, axis, by):
    size = lax.axis_size(axis)
    pairs = [(i, i + by) for i in range(size) if 0 <= i + by < size]
    return lax.ppermute(shard, axis, pairs)


def incoming_state(ends, span_rate, size):
    place = lax.axis_index("ctx")
    copies = jnp.broadcast_to(ends[None], (size,) + ends.shape)
    gathered = lax.all_to_all(copies, "ctx", 0, 0).astype(f32)
    earlier = jnp.arange(size, dtype=jnp.int32)
    gap = jnp.maximum(place - 1 - earlier, 0).astype(f32)
    weight = jnp.where(
        (earlier < place)[:, None, None],
        jnp.exp(-span_rate[None] * gap[:, None, None]),
        0.0,
    )
    return jnp.sum(weight * gathered, axis=0)


def split2(a):
    hi = a.astype(bf16)
    lo = (a - hi.astype(f32)).astype(bf16)
    return hi, lo


def split3(a):
    hi = a.astype(bf16)
    rest = a - hi.astype(f32)
    mid = rest.astype(bf16)
    lo = (rest - mid.astype(f32)).astype(bf16)
    return hi, mid, lo


def dot(a, b):
    return jnp.dot(a, b, preferred_element_type=f32)


def dot_nt(a, b):
    return lax.dot_general(a, b, (((1,), (1,)), ((), ())), preferred_element_type=f32)


def lead_rows(pair, first, count):
    lanes = pair.shape[1]
    lag = (first + lax.broadcasted_iota(jnp.int32, (count, lanes), 0)).astype(f32)
    return pair[1:2, :] * jnp.exp(-pair[0:1, :] * lag)


def exact_dot(a, select):
    return sum(dot(part, select) for part in split3(a))


def column(prm, k, rows):
    return jnp.broadcast_to(prm[:, k : k + 1], (rows, LANES))


def featurize(proj_ref, prm, p, taps, rims, slot=None):
    slot = p if slot is None else slot
    rows, length = proj_ref.shape[1], proj_ref.shape[2]
    t = taps * p
    weights = [column(prm, t + k, rows) for k in range(3)]
    back2 = column(prm, rims + 2 * p, rows)
    back1 = column(prm, rims + 2 * p + 1, rows)
    lane = lax.broadcasted_iota(jnp.int32, (rows, LANES), 1)
    tiles = [proj_ref[slot, :, j * LANES : (j + 1) * LANES].astype(f32) for j in range(length // LANES)]
    once = [pltpu.roll(x, 1, 1) for x in tiles]
    twice = [pltpu.roll(x, 2, 1) for x in tiles]
    out = []
    for j, x in enumerate(tiles):
        if j == 0:
            x1 = jnp.where(lane == 0, back1, once[0])
            x2 = jnp.where(lane == 0, back2, jnp.where(lane == 1, back1, twice[0]))
        else:
            x1 = jnp.where(lane == 0, once[j - 1], once[j])
            x2 = jnp.where(lane < 2, twice[j - 1], twice[j])
        summed = weights[0] * x + weights[1] * x1
        summed = summed + weights[2] * x2
        out.append(summed.astype(bf16))
    return jnp.concatenate(out, axis=1)


def own_modes(rows, lanes, width, modes):
    row = lax.broadcasted_iota(jnp.int32, (rows, lanes), 0) // width
    lane = lax.broadcasted_iota(jnp.int32, (rows, lanes), 1) // modes
    return row == lane


def product_stack(proj_ref, prm, taps, rims, count):
    key = featurize(proj_ref, prm, 1, taps, rims).astype(f32)
    value = featurize(proj_ref, prm, 2, taps, rims).astype(f32)
    product = (key * value).astype(bf16)
    stacked = jnp.concatenate(
        [product[:, b * BLOCK : (b + 1) * BLOCK] for b in range(count)], axis=0
    )
    return product, stacked


def masked_ends(stacked, w_hi_ref, w_lo_ref, rows, width, modes, count):
    ends = dot(stacked, w_hi_ref[0]) + dot(stacked, w_lo_ref[0])
    own = own_modes(rows, ends.shape[1], width, modes)
    return [jnp.where(own, ends[b * rows : (b + 1) * rows], 0.0) for b in range(count)], own


def state_kernel(width, modes, key_ref, value_ref, prm_ref, lam_ref, out_ref, x_ref):
    rows, length = key_ref.shape[1], key_ref.shape[2]
    prm = prm_ref[...]
    key = featurize(key_ref, prm, 1, 3, 9, 0).astype(f32)
    value = featurize(value_ref, prm, 2, 3, 9, 0).astype(f32)
    product = (key * value).astype(bf16)
    x_ref[...] = product
    lam = lam_ref[0][0:1, :]
    lanes = lam.shape[1]
    span = (BLOCK - 1 - lax.broadcasted_iota(jnp.int32, (BLOCK, lanes), 0)).astype(f32)
    within = jnp.exp(-lam * span)
    blocks = length // BLOCK
    table = jnp.concatenate(
        [within * jnp.exp(-lam * float(BLOCK * (blocks - 1 - b))) for b in range(blocks)], axis=0
    )
    w_hi, w_lo = split2(table)
    ends = dot(product, w_hi) + dot(product, w_lo)
    own = own_modes(rows, lanes, width, modes)
    picked = jnp.where(own, ends, 0.0).astype(bf16)
    out_ref[...] = dot(picked, select_matrix(lanes, modes))[:, :modes].astype(bf16)


def select_matrix(lanes, modes):
    mode = lax.broadcasted_iota(jnp.int32, (lanes, LANES), 0) % modes
    lane = lax.broadcasted_iota(jnp.int32, (lanes, LANES), 1)
    return (mode == lane).astype(bf16)


def spread_matrix(lanes, modes):
    lane = lax.broadcasted_iota(jnp.int32, (modes, lanes), 0)
    mode = lax.broadcasted_iota(jnp.int32, (modes, lanes), 1) % modes
    return (mode == lane).astype(bf16)


def columns(row):
    lanes = row.shape[1]
    diagonal = lax.broadcasted_iota(jnp.int32, (lanes, lanes), 0) == lax.broadcasted_iota(
        jnp.int32, (lanes, lanes), 1
    )
    spread = jnp.where(diagonal, jnp.broadcast_to(row, (lanes, lanes)), 0.0)
    return exact_dot(spread, jnp.ones((lanes, LANES), bf16))


def lead_table(rates, weights, first, count):
    wide = count // LANES
    rates = jnp.concatenate([rates] * wide, axis=1) if wide > 1 else rates
    weights = jnp.concatenate([weights] * wide, axis=1) if wide > 1 else weights
    lag = (first + lax.broadcasted_iota(jnp.int32, (rates.shape[0], count), 1)).astype(f32)
    return weights * jnp.exp(-rates * lag)


def local_kernel(
    width,
    modes,
    count,
    proj_ref,
    x_ref,
    prm_ref,
    lam_ref,
    res_ref,
    u0_ref,
    q_ref,
):
    rows = proj_ref.shape[1]
    groups = rows // width
    taps = 3
    rims = 3 * taps
    skip_at = rims + 6
    prm = prm_ref[...]
    query = featurize(proj_ref, prm, 0, taps, rims)
    q_ref[...] = query
    product = x_ref[...]
    stacked = jnp.concatenate(
        [product[:, b * BLOCK : (b + 1) * BLOCK] for b in range(count)], axis=0
    )
    lam = lam_ref[0][0:1, :]
    pair = lam_ref[0]
    lanes = lam.shape[1]
    span = (BLOCK - 1 - lax.broadcasted_iota(jnp.int32, (BLOCK, lanes), 0)).astype(f32)
    w_hi, w_lo = split2(jnp.exp(-lam * span))
    used = stacked[: (count - 1) * rows]
    ends = dot(used, w_hi) + dot(used, w_lo)
    own = own_modes(rows, lanes, width, modes)
    decay = jnp.exp(-lam * float(BLOCK))
    state = jnp.where(own, ends[0:rows], 0.0)
    entering = [state]
    for b in range(1, count - 1):
        state = decay * state + jnp.where(own, ends[b * rows : (b + 1) * rows], 0.0)
        entering.append(state)
    z_hi, z_lo = split2(jnp.concatenate(entering, axis=0))
    lead_hi, lead_lo = split2(lead_rows(pair, 1, BLOCK))
    far = dot_nt(z_hi, lead_hi) + dot_nt(z_hi, lead_lo) + dot_nt(z_lo, lead_hi)
    member = lax.broadcasted_iota(jnp.int32, (groups, lanes), 0) == (
        lax.broadcasted_iota(jnp.int32, (groups, lanes), 1) // modes
    )
    taps_long = sum(dot_nt(member.astype(bf16), part) for part in split3(lead_rows(pair, 0, BLOCK)))

    s_idx = lax.broadcasted_iota(jnp.int32, (BLOCK, BLOCK), 0)
    t_idx = lax.broadcasted_iota(jnp.int32, (BLOCK, BLOCK), 1)
    pieces = [[None] * groups for _ in range(count)]
    for g in range(groups):
        lhs = jnp.concatenate(
            [stacked[b * rows + g * width : b * rows + (g + 1) * width] for b in range(count)],
            axis=0,
        )
        row = taps_long[g : g + 1, :]
        toeplitz = pltpu.roll(jnp.broadcast_to(row, (BLOCK, BLOCK)), 0, 1, stride=1, stride_axis=0)
        toeplitz = jnp.where(t_idx >= s_idx, toeplitz, 0.0)
        t_hi, t_lo = split2(toeplitz)
        near = dot(lhs, t_hi) + dot(lhs, t_lo)
        for b in range(count):
            pieces[b][g] = near[b * width : (b + 1) * width]
    long_term = jnp.concatenate(
        [
            jnp.concatenate(pieces[b], axis=0) + (far[(b - 1) * rows : b * rows] if b else 0.0)
            for b in range(count)
        ],
        axis=1,
    )
    signal = product.astype(f32)
    skip_b = jnp.concatenate([column(prm, skip_at, rows)] * (signal.shape[1] // LANES), axis=1)
    mixed = query.astype(f32) * (long_term + skip_b * signal)
    u0_ref[...] = res_ref[...].astype(f32) + mixed


def finish_kernel(width, modes, u0_ref, q_ref, z_ref, lam_ref, upd_ref, sq_ref):
    rows, length = u0_ref.shape
    lam = lam_ref[0][0:1, :]
    lanes = lam.shape[1]
    spread = dot(z_ref[...].astype(bf16), spread_matrix(lanes, modes))
    own = own_modes(rows, lanes, width, modes)
    z_hi = jnp.where(own, spread, 0.0).astype(bf16)
    lead_hi, lead_lo = split2(lead_rows(lam_ref[0], 1, length))
    far = dot_nt(z_hi, lead_hi) + dot_nt(z_hi, lead_lo)
    updated = u0_ref[...] + q_ref[...].astype(f32) * far
    upd_ref[...] = updated
    part = jnp.sum(updated * updated, axis=0, keepdims=True)

    @pl.when(pl.program_id(0) == 0)
    def _():
        sq_ref[...] = part

    @pl.when(pl.program_id(0) > 0)
    def _():
        sq_ref[...] += part


def local(projections, short_filter, decay_rate, residue, skip, norm_gain, residual):
    channels, length = residual.shape
    groups, modes = decay_rate.shape
    width = channels // groups
    rim_len = short_filter.shape[2] - 1
    count = length // BLOCK
    chunk = 256 if channels % 256 == 0 else channels
    chunk_groups = chunk // width
    lanes = chunk_groups * modes
    steps = channels // chunk

    edge = projections[:, :, length - rim_len :].transpose(0, 2, 1)
    rim = shifted(edge, "ctx", 1)
    prm = jnp.concatenate(
        [
            short_filter.astype(f32).transpose(0, 2, 1).reshape(-1, channels),
            rim.astype(f32).reshape(-1, channels),
            skip[None, :],
        ],
        axis=0,
    )
    prm = jnp.pad(prm, ((0, LANES - prm.shape[0]), (0, 0))).T

    scaled = residue * jnp.sqrt(-jnp.expm1(-2.0 * decay_rate))
    lam = jnp.stack([decay_rate.reshape(steps, lanes), scaled.reshape(steps, lanes)], axis=1)

    proj_spec = pl.BlockSpec((3, chunk, length), lambda i: (0, i, 0))
    query_spec = pl.BlockSpec((1, chunk, length), lambda i: (0, i, 0))
    prm_spec = pl.BlockSpec((chunk, LANES), lambda i: (i, 0))
    lam_spec = pl.BlockSpec((1, 2, lanes), lambda i: (i, 0, 0))
    row_spec = pl.BlockSpec((chunk, length), lambda i: (i, 0))
    state_spec = pl.BlockSpec((chunk, modes), lambda i: (i, 0))

    end_state, product = pl.pallas_call(
        functools.partial(state_kernel, width, modes),
        grid=(steps,),
        in_specs=[
            pl.BlockSpec((1, chunk, length), lambda i: (1, i, 0)),
            pl.BlockSpec((1, chunk, length), lambda i: (2, i, 0)),
            prm_spec,
            lam_spec,
        ],
        out_specs=[state_spec, row_spec],
        out_shape=[
            jax.ShapeDtypeStruct((channels, modes), bf16),
            jax.ShapeDtypeStruct((channels, length), bf16),
        ],
    )(projections, projections, prm, lam)

    size = lax.axis_size("ctx")
    dense = end_state.reshape(channels * modes // 128, 128)
    rate = jnp.repeat(decay_rate, width, axis=0).reshape(dense.shape)
    incoming = incoming_state(dense, rate * length, size).reshape(channels, modes)

    u0, query = pl.pallas_call(
        functools.partial(local_kernel, width, modes, count),
        grid=(steps,),
        in_specs=[query_spec, row_spec, prm_spec, lam_spec, row_spec],
        out_specs=[row_spec, row_spec],
        out_shape=[
            jax.ShapeDtypeStruct((channels, length), f32),
            jax.ShapeDtypeStruct((channels, length), bf16),
        ],
    )(projections, product, prm, lam, residual)

    updated, sq = pl.pallas_call(
        functools.partial(finish_kernel, width, modes),
        grid=(steps,),
        in_specs=[row_spec, row_spec, state_spec, lam_spec],
        out_specs=[row_spec, pl.BlockSpec((1, length), lambda i: (0, 0))],
        out_shape=[
            jax.ShapeDtypeStruct((channels, length), f32),
            jax.ShapeDtypeStruct((1, length), f32),
        ],
    )(u0, query, incoming, lam)
    squares = lax.psum(sq[0], "tp")
    return (updated * lax.rsqrt(squares / D + epsilon)[None, :] * norm_gain[:, None]).astype(bf16)


def solution(mesh):
    placed = (
        P(None, "tp", "ctx"),
        P(None, "tp", None),
        P("tp", None),
        P("tp", None),
        P("tp"),
        P("tp"),
        P("tp", "ctx"),
    )
    return jax.shard_map(
        local, mesh=mesh, in_specs=placed, out_specs=P("tp", "ctx"), check_vma=False
    )
```

```python
import functools

import jax
import jax.numpy as jnp
from jax import lax
from jax.experimental import pallas as pl
from jax.experimental.pallas import tpu as pltpu
from jax.sharding import PartitionSpec as P

D = 8192
epsilon = 1e-06
BLOCK = 128
LANES = 128
f32 = jnp.float32
bf16 = jnp.bfloat16


def shifted(shard, axis, by):
    size = lax.axis_size(axis)
    pairs = [(i, i + by) for i in range(size) if 0 <= i + by < size]
    return lax.ppermute(shard, axis, pairs)


def incoming_state(ends, span_rate, size):
    place = lax.axis_index("ctx")
    copies = jnp.broadcast_to(ends[None], (size,) + ends.shape)
    gathered = lax.all_to_all(copies, "ctx", 0, 0).astype(f32)
    earlier = jnp.arange(size, dtype=jnp.int32)
    gap = jnp.maximum(place - 1 - earlier, 0).astype(f32)
    weight = jnp.where(
        (earlier < place)[:, None, None],
        jnp.exp(-span_rate[None] * gap[:, None, None]),
        0.0,
    )
    return jnp.sum(weight * gathered, axis=0)


def split2(a):
    hi = a.astype(bf16)
    lo = (a - hi.astype(f32)).astype(bf16)
    return hi, lo


def split3(a):
    hi = a.astype(bf16)
    rest = a - hi.astype(f32)
    mid = rest.astype(bf16)
    lo = (rest - mid.astype(f32)).astype(bf16)
    return hi, mid, lo


def dot(a, b):
    return jnp.dot(a, b, preferred_element_type=f32)


def dot_nt(a, b):
    return lax.dot_general(a, b, (((1,), (1,)), ((), ())), preferred_element_type=f32)


def lead_rows(pair, first, count):
    lanes = pair.shape[1]
    lag = (first + lax.broadcasted_iota(jnp.int32, (count, lanes), 0)).astype(f32)
    return pair[1:2, :] * jnp.exp(-pair[0:1, :] * lag)


def exact_dot(a, select):
    return sum(dot(part, select) for part in split3(a))


def column(prm, k, rows):
    return jnp.broadcast_to(prm[:, k : k + 1], (rows, LANES))


def featurize(proj_ref, prm, p, taps, rims, slot=None):
    slot = p if slot is None else slot
    rows, length = proj_ref.shape[1], proj_ref.shape[2]
    t = taps * p
    weights = [column(prm, t + k, rows) for k in range(3)]
    back2 = column(prm, rims + 2 * p, rows)
    back1 = column(prm, rims + 2 * p + 1, rows)
    lane = lax.broadcasted_iota(jnp.int32, (rows, LANES), 1)
    tiles = [proj_ref[slot, :, j * LANES : (j + 1) * LANES].astype(f32) for j in range(length // LANES)]
    once = [pltpu.roll(x, 1, 1) for x in tiles]
    twice = [pltpu.roll(x, 2, 1) for x in tiles]
    out = []
    for j, x in enumerate(tiles):
        if j == 0:
            x1 = jnp.where(lane == 0, back1, once[0])
            x2 = jnp.where(lane == 0, back2, jnp.where(lane == 1, back1, twice[0]))
        else:
            x1 = jnp.where(lane == 0, once[j - 1], once[j])
            x2 = jnp.where(lane < 2, twice[j - 1], twice[j])
        summed = weights[0] * x + weights[1] * x1
        summed = summed + weights[2] * x2
        out.append(summed.astype(bf16))
    return jnp.concatenate(out, axis=1)


def own_modes(rows, lanes, width, modes):
    row = lax.broadcasted_iota(jnp.int32, (rows, lanes), 0) // width
    lane = lax.broadcasted_iota(jnp.int32, (rows, lanes), 1) // modes
    return row == lane


def product_stack(proj_ref, prm, taps, rims, count):
    key = featurize(proj_ref, prm, 1, taps, rims).astype(f32)
    value = featurize(proj_ref, prm, 2, taps, rims).astype(f32)
    product = (key * value).astype(bf16)
    stacked = jnp.concatenate(
        [product[:, b * BLOCK : (b + 1) * BLOCK] for b in range(count)], axis=0
    )
    return product, stacked


def masked_ends(stacked, w_hi_ref, w_lo_ref, rows, width, modes, count):
    ends = dot(stacked, w_hi_ref[0]) + dot(stacked, w_lo_ref[0])
    own = own_modes(rows, ends.shape[1], width, modes)
    return [jnp.where(own, ends[b * rows : (b + 1) * rows], 0.0) for b in range(count)], own


def state_kernel(width, modes, key_ref, value_ref, prm_ref, lam_ref, out_ref, x_ref):
    rows, length = key_ref.shape[1], key_ref.shape[2]
    prm = prm_ref[...]
    key = featurize(key_ref, prm, 1, 3, 9, 0).astype(f32)
    value = featurize(value_ref, prm, 2, 3, 9, 0).astype(f32)
    product = (key * value).astype(bf16)
    x_ref[...] = product
    lam = lam_ref[0][0:1, :]
    lanes = lam.shape[1]
    span = (BLOCK - 1 - lax.broadcasted_iota(jnp.int32, (BLOCK, lanes), 0)).astype(f32)
    within = jnp.exp(-lam * span)
    blocks = length // BLOCK
    table = jnp.concatenate(
        [within * jnp.exp(-lam * float(BLOCK * (blocks - 1 - b))) for b in range(blocks)], axis=0
    )
    w_hi, w_lo = split2(table)
    ends = dot(product, w_hi) + dot(product, w_lo)
    own = own_modes(rows, lanes, width, modes)
    picked = jnp.where(own, ends, 0.0).astype(bf16)
    out_ref[...] = dot(picked, select_matrix(lanes, modes))[:, :modes].astype(bf16)


def select_matrix(lanes, modes):
    mode = lax.broadcasted_iota(jnp.int32, (lanes, LANES), 0) % modes
    lane = lax.broadcasted_iota(jnp.int32, (lanes, LANES), 1)
    return (mode == lane).astype(bf16)


def spread_matrix(lanes, modes):
    lane = lax.broadcasted_iota(jnp.int32, (modes, lanes), 0)
    mode = lax.broadcasted_iota(jnp.int32, (modes, lanes), 1) % modes
    return (mode == lane).astype(bf16)


def columns(row):
    lanes = row.shape[1]
    diagonal = lax.broadcasted_iota(jnp.int32, (lanes, lanes), 0) == lax.broadcasted_iota(
        jnp.int32, (lanes, lanes), 1
    )
    spread = jnp.where(diagonal, jnp.broadcast_to(row, (lanes, lanes)), 0.0)
    return exact_dot(spread, jnp.ones((lanes, LANES), bf16))


def lead_table(rates, weights, first, count):
    wide = count // LANES
    rates = jnp.concatenate([rates] * wide, axis=1) if wide > 1 else rates
    weights = jnp.concatenate([weights] * wide, axis=1) if wide > 1 else weights
    lag = (first + lax.broadcasted_iota(jnp.int32, (rates.shape[0], count), 1)).astype(f32)
    return weights * jnp.exp(-rates * lag)


def local_kernel(
    width,
    modes,
    count,
    proj_ref,
    x_ref,
    prm_ref,
    lam_ref,
    res_ref,
    u0_ref,
    q_ref,
):
    rows = proj_ref.shape[1]
    groups = rows // width
    taps = 3
    rims = 3 * taps
    skip_at = rims + 6
    prm = prm_ref[...]
    query = featurize(proj_ref, prm, 0, taps, rims)
    q_ref[...] = query
    product = x_ref[...]
    stacked = jnp.concatenate(
        [product[:, b * BLOCK : (b + 1) * BLOCK] for b in range(count)], axis=0
    )
    lam = lam_ref[0][0:1, :]
    pair = lam_ref[0]
    lanes = lam.shape[1]
    span = (BLOCK - 1 - lax.broadcasted_iota(jnp.int32, (BLOCK, lanes), 0)).astype(f32)
    w_hi, w_lo = split2(jnp.exp(-lam * span))
    used = stacked[: (count - 1) * rows]
    ends = dot(used, w_hi) + dot(used, w_lo)
    own = own_modes(rows, lanes, width, modes)
    decay = jnp.exp(-lam * float(BLOCK))
    state = jnp.where(own, ends[0:rows], 0.0)
    entering = [state]
    for b in range(1, count - 1):
        state = decay * state + jnp.where(own, ends[b * rows : (b + 1) * rows], 0.0)
        entering.append(state)
    z_hi, z_lo = split2(jnp.concatenate(entering, axis=0))
    lead_hi, lead_lo = split2(lead_rows(pair, 1, BLOCK))
    far = dot_nt(z_hi, lead_hi) + dot_nt(z_hi, lead_lo) + dot_nt(z_lo, lead_hi)
    member = lax.broadcasted_iota(jnp.int32, (groups, lanes), 0) == (
        lax.broadcasted_iota(jnp.int32, (groups, lanes), 1) // modes
    )
    taps_long = sum(dot_nt(member.astype(bf16), part) for part in split3(lead_rows(pair, 0, BLOCK)))

    s_idx = lax.broadcasted_iota(jnp.int32, (BLOCK, BLOCK), 0)
    t_idx = lax.broadcasted_iota(jnp.int32, (BLOCK, BLOCK), 1)
    taps_parts = [part.astype(f32) for part in split2(taps_long)]
    pieces = [[None] * groups for _ in range(count)]
    for g in range(groups):
        lhs = jnp.concatenate(
            [stacked[b * rows + g * width : b * rows + (g + 1) * width] for b in range(count)],
            axis=0,
        )
        t_hi, t_lo = [
            jnp.where(
                t_idx >= s_idx,
                pltpu.roll(jnp.broadcast_to(part[g : g + 1, :], (BLOCK, BLOCK)), 0, 1, stride=1, stride_axis=0),
                0.0,
            ).astype(bf16)
            for part in taps_parts
        ]
        near = dot(lhs, t_hi) + dot(lhs, t_lo)
        for b in range(count):
            pieces[b][g] = near[b * width : (b + 1) * width]
    long_term = jnp.concatenate(
        [
            jnp.concatenate(pieces[b], axis=0) + (far[(b - 1) * rows : b * rows] if b else 0.0)
            for b in range(count)
        ],
        axis=1,
    )
    signal = product.astype(f32)
    skip_b = jnp.concatenate([column(prm, skip_at, rows)] * (signal.shape[1] // LANES), axis=1)
    mixed = query.astype(f32) * (long_term + skip_b * signal)
    u0_ref[...] = res_ref[...].astype(f32) + mixed


def finish_kernel(width, modes, u0_ref, q_ref, z_ref, lam_ref, upd_ref, sq_ref):
    rows, length = u0_ref.shape
    lam = lam_ref[0][0:1, :]
    lanes = lam.shape[1]
    spread = dot(z_ref[...].astype(bf16), spread_matrix(lanes, modes))
    own = own_modes(rows, lanes, width, modes)
    z_hi = jnp.where(own, spread, 0.0).astype(bf16)
    lead_hi, lead_lo = split2(lead_rows(lam_ref[0], 1, length))
    far = dot_nt(z_hi, lead_hi) + dot_nt(z_hi, lead_lo)
    updated = u0_ref[...] + q_ref[...].astype(f32) * far
    upd_ref[...] = updated
    part = jnp.sum(updated * updated, axis=0, keepdims=True)

    @pl.when(pl.program_id(0) == 0)
    def _():
        sq_ref[...] = part

    @pl.when(pl.program_id(0) > 0)
    def _():
        sq_ref[...] += part


def local(projections, short_filter, decay_rate, residue, skip, norm_gain, residual):
    channels, length = residual.shape
    groups, modes = decay_rate.shape
    width = channels // groups
    rim_len = short_filter.shape[2] - 1
    count = length // BLOCK
    chunk = 256 if channels % 256 == 0 else channels
    chunk_groups = chunk // width
    lanes = chunk_groups * modes
    steps = channels // chunk

    edge = projections[:, :, length - rim_len :].transpose(0, 2, 1)
    rim = shifted(edge, "ctx", 1)
    prm = jnp.concatenate(
        [
            short_filter.astype(f32).transpose(0, 2, 1).reshape(-1, channels),
            rim.astype(f32).reshape(-1, channels),
            skip[None, :],
        ],
        axis=0,
    )
    prm = jnp.pad(prm, ((0, LANES - prm.shape[0]), (0, 0))).T

    scaled = residue * jnp.sqrt(-jnp.expm1(-2.0 * decay_rate))
    lam = jnp.stack([decay_rate.reshape(steps, lanes), scaled.reshape(steps, lanes)], axis=1)

    proj_spec = pl.BlockSpec((3, chunk, length), lambda i: (0, i, 0))
    query_spec = pl.BlockSpec((1, chunk, length), lambda i: (0, i, 0))
    prm_spec = pl.BlockSpec((chunk, LANES), lambda i: (i, 0))
    lam_spec = pl.BlockSpec((1, 2, lanes), lambda i: (i, 0, 0))
    row_spec = pl.BlockSpec((chunk, length), lambda i: (i, 0))
    state_spec = pl.BlockSpec((chunk, modes), lambda i: (i, 0))

    end_state, product = pl.pallas_call(
        functools.partial(state_kernel, width, modes),
        grid=(steps,),
        in_specs=[
            pl.BlockSpec((1, chunk, length), lambda i: (1, i, 0)),
            pl.BlockSpec((1, chunk, length), lambda i: (2, i, 0)),
            prm_spec,
            lam_spec,
        ],
        out_specs=[state_spec, row_spec],
        out_shape=[
            jax.ShapeDtypeStruct((channels, modes), bf16),
            jax.ShapeDtypeStruct((channels, length), bf16),
        ],
    )(projections, projections, prm, lam)

    size = lax.axis_size("ctx")
    dense = end_state.reshape(channels * modes // 128, 128)
    rate = jnp.repeat(decay_rate, width, axis=0).reshape(dense.shape)
    incoming = incoming_state(dense, rate * length, size).reshape(channels, modes)

    u0, query = pl.pallas_call(
        functools.partial(local_kernel, width, modes, count),
        grid=(steps,),
        in_specs=[query_spec, row_spec, prm_spec, lam_spec, row_spec],
        out_specs=[row_spec, row_spec],
        out_shape=[
            jax.ShapeDtypeStruct((channels, length), f32),
            jax.ShapeDtypeStruct((channels, length), bf16),
        ],
    )(projections, product, prm, lam, residual)

    updated, sq = pl.pallas_call(
        functools.partial(finish_kernel, width, modes),
        grid=(steps,),
        in_specs=[row_spec, row_spec, state_spec, lam_spec],
        out_specs=[row_spec, pl.BlockSpec((1, length), lambda i: (0, 0))],
        out_shape=[
            jax.ShapeDtypeStruct((channels, length), f32),
            jax.ShapeDtypeStruct((1, length), f32),
        ],
    )(u0, query, incoming, lam)
    squares = lax.psum(sq[0], "tp")
    return (updated * lax.rsqrt(squares / D + epsilon)[None, :] * norm_gain[:, None]).astype(bf16)


def solution(mesh):
    placed = (
        P(None, "tp", "ctx"),
        P(None, "tp", None),
        P("tp", None),
        P("tp", None),
        P("tp"),
        P("tp"),
        P("tp", "ctx"),
    )
    return jax.shard_map(
        local, mesh=mesh, in_specs=placed, out_specs=P("tp", "ctx"), check_vma=False
    )
```

```python
import functools

import jax
import jax.numpy as jnp
from jax import lax
from jax.experimental import pallas as pl
from jax.experimental.pallas import tpu as pltpu
from jax.sharding import PartitionSpec as P

D = 8192
epsilon = 1e-06
BLOCK = 128
LANES = 128
f32 = jnp.float32
bf16 = jnp.bfloat16


def shifted(shard, axis, by):
    size = lax.axis_size(axis)
    pairs = [(i, i + by) for i in range(size) if 0 <= i + by < size]
    return lax.ppermute(shard, axis, pairs)


def incoming_state(ends, span_rate, size):
    place = lax.axis_index("ctx")
    copies = jnp.broadcast_to(ends[None], (size,) + ends.shape)
    gathered = lax.all_to_all(copies, "ctx", 0, 0).astype(f32)
    earlier = jnp.arange(size, dtype=jnp.int32)
    gap = jnp.maximum(place - 1 - earlier, 0).astype(f32)
    weight = jnp.where(
        (earlier < place)[:, None, None],
        jnp.exp(-span_rate[None] * gap[:, None, None]),
        0.0,
    )
    return jnp.sum(weight * gathered, axis=0)


def split2(a):
    hi = a.astype(bf16)
    lo = (a - hi.astype(f32)).astype(bf16)
    return hi, lo


def split3(a):
    hi = a.astype(bf16)
    rest = a - hi.astype(f32)
    mid = rest.astype(bf16)
    lo = (rest - mid.astype(f32)).astype(bf16)
    return hi, mid, lo


def dot(a, b):
    return jnp.dot(a, b, preferred_element_type=f32)


def dot_nt(a, b):
    return lax.dot_general(a, b, (((1,), (1,)), ((), ())), preferred_element_type=f32)


def lead_rows(pair, first, count):
    lanes = pair.shape[1]
    lag = (first + lax.broadcasted_iota(jnp.int32, (count, lanes), 0)).astype(f32)
    return pair[1:2, :] * jnp.exp(-pair[0:1, :] * lag)


def exact_dot(a, select):
    return sum(dot(part, select) for part in split3(a))


def column(prm, k, rows):
    return jnp.broadcast_to(prm[:, k : k + 1], (rows, LANES))


def featurize(proj_ref, prm, p, taps, rims, slot=None):
    slot = p if slot is None else slot
    rows, length = proj_ref.shape[1], proj_ref.shape[2]
    t = taps * p
    weights = [column(prm, t + k, rows) for k in range(3)]
    back2 = column(prm, rims + 2 * p, rows)
    back1 = column(prm, rims + 2 * p + 1, rows)
    lane = lax.broadcasted_iota(jnp.int32, (rows, LANES), 1)
    tiles = [proj_ref[slot, :, j * LANES : (j + 1) * LANES].astype(f32) for j in range(length // LANES)]
    once = [pltpu.roll(x, 1, 1) for x in tiles]
    twice = [pltpu.roll(x, 2, 1) for x in tiles]
    out = []
    for j, x in enumerate(tiles):
        if j == 0:
            x1 = jnp.where(lane == 0, back1, once[0])
            x2 = jnp.where(lane == 0, back2, jnp.where(lane == 1, back1, twice[0]))
        else:
            x1 = jnp.where(lane == 0, once[j - 1], once[j])
            x2 = jnp.where(lane < 2, twice[j - 1], twice[j])
        summed = weights[0] * x + weights[1] * x1
        summed = summed + weights[2] * x2
        out.append(summed.astype(bf16))
    return jnp.concatenate(out, axis=1)


def own_modes(rows, lanes, width, modes):
    row = lax.broadcasted_iota(jnp.int32, (rows, lanes), 0) // width
    lane = lax.broadcasted_iota(jnp.int32, (rows, lanes), 1) // modes
    return row == lane


def product_stack(proj_ref, prm, taps, rims, count):
    key = featurize(proj_ref, prm, 1, taps, rims).astype(f32)
    value = featurize(proj_ref, prm, 2, taps, rims).astype(f32)
    product = (key * value).astype(bf16)
    stacked = jnp.concatenate(
        [product[:, b * BLOCK : (b + 1) * BLOCK] for b in range(count)], axis=0
    )
    return product, stacked


def masked_ends(stacked, w_hi_ref, w_lo_ref, rows, width, modes, count):
    ends = dot(stacked, w_hi_ref[0]) + dot(stacked, w_lo_ref[0])
    own = own_modes(rows, ends.shape[1], width, modes)
    return [jnp.where(own, ends[b * rows : (b + 1) * rows], 0.0) for b in range(count)], own


def state_kernel(width, modes, key_ref, value_ref, prm_ref, lam_ref, out_ref, x_ref):
    rows, length = key_ref.shape[1], key_ref.shape[2]
    prm = prm_ref[...]
    key = featurize(key_ref, prm, 1, 3, 9, 0).astype(f32)
    value = featurize(value_ref, prm, 2, 3, 9, 0).astype(f32)
    product = (key * value).astype(bf16)
    x_ref[...] = product
    lam = lam_ref[0][0:1, :]
    lanes = lam.shape[1]
    span = (BLOCK - 1 - lax.broadcasted_iota(jnp.int32, (BLOCK, lanes), 0)).astype(f32)
    within = jnp.exp(-lam * span)
    blocks = length // BLOCK
    table = jnp.concatenate(
        [within * jnp.exp(-lam * float(BLOCK * (blocks - 1 - b))) for b in range(blocks)], axis=0
    )
    w_hi, w_lo = split2(table)
    ends = dot(product, w_hi) + dot(product, w_lo)
    own = own_modes(rows, lanes, width, modes)
    picked = jnp.where(own, ends, 0.0).astype(bf16)
    out_ref[...] = dot(picked, select_matrix(lanes, modes))[:, :modes].astype(bf16)


def select_matrix(lanes, modes):
    mode = lax.broadcasted_iota(jnp.int32, (lanes, LANES), 0) % modes
    lane = lax.broadcasted_iota(jnp.int32, (lanes, LANES), 1)
    return (mode == lane).astype(bf16)


def spread_matrix(lanes, modes):
    lane = lax.broadcasted_iota(jnp.int32, (modes, lanes), 0)
    mode = lax.broadcasted_iota(jnp.int32, (modes, lanes), 1) % modes
    return (mode == lane).astype(bf16)


def columns(row):
    lanes = row.shape[1]
    diagonal = lax.broadcasted_iota(jnp.int32, (lanes, lanes), 0) == lax.broadcasted_iota(
        jnp.int32, (lanes, lanes), 1
    )
    spread = jnp.where(diagonal, jnp.broadcast_to(row, (lanes, lanes)), 0.0)
    return exact_dot(spread, jnp.ones((lanes, LANES), bf16))


def lead_table(rates, weights, first, count):
    wide = count // LANES
    rates = jnp.concatenate([rates] * wide, axis=1) if wide > 1 else rates
    weights = jnp.concatenate([weights] * wide, axis=1) if wide > 1 else weights
    lag = (first + lax.broadcasted_iota(jnp.int32, (rates.shape[0], count), 1)).astype(f32)
    return weights * jnp.exp(-rates * lag)


def local_kernel(
    width,
    modes,
    count,
    proj_ref,
    x_ref,
    prm_ref,
    lam_ref,
    res_ref,
    u0_ref,
    q_ref,
):
    rows = proj_ref.shape[1]
    groups = rows // width
    taps = 3
    rims = 3 * taps
    skip_at = rims + 6
    prm = prm_ref[...]
    query = featurize(proj_ref, prm, 0, taps, rims)
    q_ref[...] = query
    product = x_ref[...]
    stacked = jnp.concatenate(
        [product[:, b * BLOCK : (b + 1) * BLOCK] for b in range(count)], axis=0
    )
    lam = lam_ref[0][0:1, :]
    pair = lam_ref[0]
    lanes = lam.shape[1]
    span = (BLOCK - 1 - lax.broadcasted_iota(jnp.int32, (BLOCK, lanes), 0)).astype(f32)
    w_hi, w_lo = split2(jnp.exp(-lam * span))
    used = stacked[: (count - 1) * rows]
    ends = dot(used, w_hi) + dot(used, w_lo)
    own = own_modes(rows, lanes, width, modes)
    decay = jnp.exp(-lam * float(BLOCK))
    state = jnp.where(own, ends[0:rows], 0.0)
    entering = [state]
    for b in range(1, count - 1):
        state = decay * state + jnp.where(own, ends[b * rows : (b + 1) * rows], 0.0)
        entering.append(state)
    z_hi, z_lo = split2(jnp.concatenate(entering, axis=0))
    lead_hi, lead_lo = split2(lead_rows(pair, 1, BLOCK))
    far = dot_nt(z_hi, lead_hi) + dot_nt(z_hi, lead_lo) + dot_nt(z_lo, lead_hi)
    member = lax.broadcasted_iota(jnp.int32, (groups, lanes), 0) == (
        lax.broadcasted_iota(jnp.int32, (groups, lanes), 1) // modes
    )
    taps_long = sum(dot_nt(member.astype(bf16), part) for part in split3(lead_rows(pair, 0, BLOCK)))

    s_idx = lax.broadcasted_iota(jnp.int32, (BLOCK, BLOCK), 0)
    t_idx = lax.broadcasted_iota(jnp.int32, (BLOCK, BLOCK), 1)
    taps_parts = [part.astype(f32) for part in split2(taps_long)]
    pieces = [[None] * groups for _ in range(count)]
    for g in range(groups):
        lhs = jnp.concatenate(
            [stacked[b * rows + g * width : b * rows + (g + 1) * width] for b in range(count)],
            axis=0,
        )
        t_hi, t_lo = [
            jnp.where(
                t_idx >= s_idx,
                pltpu.roll(jnp.broadcast_to(part[g : g + 1, :], (BLOCK, BLOCK)), 0, 1, stride=1, stride_axis=0),
                0.0,
            ).astype(bf16)
            for part in taps_parts
        ]
        near = dot(lhs, t_hi) + dot(lhs, t_lo)
        for b in range(count):
            pieces[b][g] = near[b * width : (b + 1) * width]
    long_term = jnp.concatenate(
        [
            jnp.concatenate(pieces[b], axis=0) + (far[(b - 1) * rows : b * rows] if b else 0.0)
            for b in range(count)
        ],
        axis=1,
    )
    signal = product.astype(f32)
    skip_b = jnp.concatenate([column(prm, skip_at, rows)] * (signal.shape[1] // LANES), axis=1)
    mixed = query.astype(f32) * (long_term + skip_b * signal)
    u0_ref[...] = res_ref[...].astype(f32) + mixed


def finish_kernel(width, modes, u0_ref, q_ref, z_ref, lam_ref, upd_ref, sq_ref):
    rows, length = u0_ref.shape
    lam = lam_ref[0][0:1, :]
    lanes = lam.shape[1]
    spread = dot(z_ref[...].astype(bf16), spread_matrix(lanes, modes))
    own = own_modes(rows, lanes, width, modes)
    z_hi = jnp.where(own, spread, 0.0).astype(bf16)
    lead_hi, lead_lo = split2(lead_rows(lam_ref[0], 1, length))
    far = dot_nt(z_hi, lead_hi) + dot_nt(z_hi, lead_lo)
    updated = u0_ref[...] + q_ref[...].astype(f32) * far
    upd_ref[...] = updated
    part = jnp.sum(updated * updated, axis=0, keepdims=True)

    @pl.when(pl.program_id(0) == 0)
    def _():
        sq_ref[...] = part

    @pl.when(pl.program_id(0) > 0)
    def _():
        sq_ref[...] += part


def local(projections, short_filter, decay_rate, residue, skip, norm_gain, residual):
    channels, length = residual.shape
    groups, modes = decay_rate.shape
    width = channels // groups
    rim_len = short_filter.shape[2] - 1
    count = length // BLOCK
    chunk = 256 if channels % 256 == 0 else channels
    chunk_groups = chunk // width
    lanes = chunk_groups * modes
    steps = channels // chunk

    edge = projections[:, :, length - rim_len :].transpose(0, 2, 1)
    rim = shifted(edge, "ctx", 1)
    prm = jnp.concatenate(
        [
            short_filter.astype(f32).transpose(0, 2, 1).reshape(-1, channels),
            rim.astype(f32).reshape(-1, channels),
            skip[None, :],
        ],
        axis=0,
    )
    prm = jnp.pad(prm, ((0, LANES - prm.shape[0]), (0, 0))).T

    scaled = residue * jnp.sqrt(-jnp.expm1(-2.0 * decay_rate))
    lam = jnp.stack([decay_rate.reshape(steps, lanes), scaled.reshape(steps, lanes)], axis=1)

    proj_spec = pl.BlockSpec((3, chunk, length), lambda i: (0, i, 0))
    query_spec = pl.BlockSpec((1, chunk, length), lambda i: (0, i, 0))
    prm_spec = pl.BlockSpec((chunk, LANES), lambda i: (i, 0))
    lam_spec = pl.BlockSpec((1, 2, lanes), lambda i: (i, 0, 0))
    row_spec = pl.BlockSpec((chunk, length), lambda i: (i, 0))
    state_spec = pl.BlockSpec((chunk, modes), lambda i: (i, 0))

    end_state, product = pl.pallas_call(
        functools.partial(state_kernel, width, modes),
        grid=(steps,),
        in_specs=[
            pl.BlockSpec((1, chunk, length), lambda i: (1, i, 0)),
            pl.BlockSpec((1, chunk, length), lambda i: (2, i, 0)),
            prm_spec,
            lam_spec,
        ],
        out_specs=[state_spec, row_spec],
        out_shape=[
            jax.ShapeDtypeStruct((channels, modes), bf16),
            jax.ShapeDtypeStruct((channels, length), bf16),
        ],
    )(projections, projections, prm, lam)

    size = lax.axis_size("ctx")
    dense = end_state.reshape(channels * modes // 128, 128)
    rate = jnp.repeat(decay_rate, width, axis=0).reshape(dense.shape)
    incoming = incoming_state(dense, rate * length, size).astype(bf16).reshape(channels, modes)

    u0, query = pl.pallas_call(
        functools.partial(local_kernel, width, modes, count),
        grid=(steps,),
        in_specs=[query_spec, row_spec, prm_spec, lam_spec, row_spec],
        out_specs=[row_spec, row_spec],
        out_shape=[
            jax.ShapeDtypeStruct((channels, length), f32),
            jax.ShapeDtypeStruct((channels, length), bf16),
        ],
    )(projections, product, prm, lam, residual)

    updated, sq = pl.pallas_call(
        functools.partial(finish_kernel, width, modes),
        grid=(steps,),
        in_specs=[row_spec, row_spec, state_spec, lam_spec],
        out_specs=[row_spec, pl.BlockSpec((1, length), lambda i: (0, 0))],
        out_shape=[
            jax.ShapeDtypeStruct((channels, length), f32),
            jax.ShapeDtypeStruct((1, length), f32),
        ],
    )(u0, query, incoming, lam)
    squares = lax.psum(sq[0], "tp")
    return (updated * lax.rsqrt(squares / D + epsilon)[None, :] * norm_gain[:, None]).astype(bf16)


def solution(mesh):
    placed = (
        P(None, "tp", "ctx"),
        P(None, "tp", None),
        P("tp", None),
        P("tp", None),
        P("tp"),
        P("tp"),
        P("tp", "ctx"),
    )
    return jax.shard_map(
        local, mesh=mesh, in_specs=placed, out_specs=P("tp", "ctx"), check_vma=False
    )
```
